32 devices in a mesh: rep: 4 (over y, core), seq: 4 (over z), fsdp: 2 (over x).
Axes of the slice: x: 2, y: 2, z: 4, core: 2. Of those that a mesh axis runs over, the one named last changes fastest.
Arguments:
- tokens: bfloat16 [4096, 4096], P(('rep', 'seq')), may hold values from -6 to 6
- cotangent: bfloat16 [4096, 4096], P(('rep', 'seq')), may hold values from -3 to 3
- norm_gain: float32 [4096], replicated, may hold values from 0.1 to 1.9
- gate_weight: bfloat16 [4096, 12288], P(None, ('seq', 'fsdp')), may hold values from -0.09375 to 0.09375
- up_weight: bfloat16 [4096, 12288], P(None, ('seq', 'fsdp')), may hold values from -0.09375 to 0.09375
- down_weight: bfloat16 [12288, 4096], P(('seq', 'fsdp')), may hold values from -0.0546875 to 0.0546875
- depths: int32 [4096], P(('rep', 'seq')), may hold values from 0 to 4, as said below
Outputs:
- branch_grad: bfloat16 [4096, 4096], P(('rep', 'seq', 'fsdp'))
- gate_grad: float32 [4096, 12288], P('rep', ('seq', 'fsdp'))
- up_grad: float32 [4096, 12288], P('rep', ('seq', 'fsdp'))
- down_grad: float32 [12288, 4096], P(('seq', 'fsdp'), 'rep')
The draws below stay inside these ranges and needn't reach their ends.
Inputs may be any that keep to these rules, and one draw needn't show every extreme that they name: `depths`: within each aligned block of 256 rows (the tokens of one seq shard) at most 8 and at least 4 tokens have a depth greater than 1, and some block has exactly 8.
All inputs are finite; a program needn't handle non-finite values.
Results may differ from the reference program's by a relative error of at most 0.019.
Values may be sent and summed in bfloat16 or wider, within the bound.
No kernel may reach another device: no remote copies, remote signals or barrier semaphores. Data moves between devices by JAX's collectives and lax.ppermute only.
A program may use at most 192 MiB of HBM per device.

```python
from functools import partial
import jax
import jax.numpy as jnp
from jax import lax

D = 4096
FF = 12288
REC = 1
TOK_DEV = 256
MAXACT = 8
WINDOW = 1024
TOKENS = 4096
N_REP = 4


def draw_depths(key, part):
    shard_count = TOKENS // TOK_DEV
    counts = jax.random.randint(jax.random.fold_in(key, 102), (shard_count,), MAXACT // 2, MAXACT + 1, dtype=jnp.int32)
    busiest = jax.random.randint(jax.random.fold_in(key, 103), (), 0, shard_count, dtype=jnp.int32)
    counts = jnp.where(jnp.arange(shard_count, dtype=jnp.int32) == busiest, MAXACT, counts)
    scores = jax.random.randint(jax.random.fold_in(key, 104), (shard_count, TOK_DEV), 0, 1 << 20, dtype=jnp.int32)
    scores = scores * TOK_DEV + jnp.arange(TOK_DEV, dtype=jnp.int32)[None, :]
    ranking = jnp.argsort(jnp.argsort(scores, axis=1, stable=True), axis=1, stable=True).astype(jnp.int32)
    chosen = ranking < counts[:, None]
    deeper = jax.random.randint(jax.random.fold_in(key, 105), (shard_count, TOK_DEV), REC + 1, 5, dtype=jnp.int32)
    shallow = jax.random.randint(jax.random.fold_in(key, 106), (shard_count, TOK_DEV), 0, REC + 1, dtype=jnp.int32)
    return jnp.where(chosen, deeper, shallow).reshape(TOKENS)


def block_levels(stream_key, dims, shards, low, high):
    level, own = 1.0, jax.random.fold_in(stream_key, 6)
    for dim, parts in shards:
        steps = jnp.exp(jax.random.uniform(jax.random.fold_in(own, dim), (parts,), jnp.float32, low / len(shards), high / len(shards)))
        level = level * jnp.repeat(steps, dims[dim] // parts).reshape([-1 if axis == dim else 1 for axis in range(len(dims))])
    return level


def noise(rng, extent, scale, bound, shards=(), held_as=jnp.bfloat16):
    level = block_levels(rng, extent, shards, -0.22, 0.18) if shards else 1.0
    entries = jax.random.normal(rng, extent, jnp.float32) * scale * level
    return jnp.minimum(jnp.maximum(entries, -bound), bound).astype(held_as)


def setup_inputs(seed: int = 0) -> dict:
    seeds = jax.random.split(jax.random.key(seed), 8)
    tokens = noise(seeds[0], (TOKENS, D), 1.0, 6.0, ((0, 16),))
    cotangent = noise(seeds[1], (TOKENS, D), 0.5, 3.0, ((0, 16),))
    norm_gain = jnp.clip(1.0 + 0.18 * jax.random.normal(seeds[2], (D,), jnp.float32), 0.1, 1.9)
    gate_weight = noise(seeds[3], (D, FF), D ** -0.5, 0.09375, ((1, 8),))
    up_weight = noise(seeds[4], (D, FF), D ** -0.5, 0.09375, ((1, 8),))
    down_weight = noise(seeds[5], (FF, D), FF ** -0.5, 0.0546875, ((0, 8),))
    depths = draw_depths(jax.random.fold_in(seeds[7], 71), 0)
    return dict(tokens=tokens, cotangent=cotangent, norm_gain=norm_gain, gate_weight=gate_weight, up_weight=up_weight, down_weight=down_weight, depths=depths)


EPSILON = 1e-05

def normalize(widened, norm_gain):
    factor = lax.rsqrt(lax.optimization_barrier(jnp.mean(widened * widened, axis=-1, keepdims=True)) + EPSILON)
    return widened * factor * norm_gain

def rounded(term):
    narrow = lax.optimization_barrier(term.astype(jnp.bfloat16))
    return narrow.astype(jnp.float32)

def reference(tokens, cotangent, norm_gain, gate_weight, up_weight, down_weight, depths):
    active = depths > REC
    widened = tokens.astype(jnp.float32)
    normed = normalize(widened, norm_gain).astype(jnp.bfloat16)
    masked = jnp.where(active[:, None], cotangent, jnp.zeros_like(cotangent))
    gate = jnp.dot(normed, gate_weight, preferred_element_type=jnp.float32)
    up = jnp.dot(normed, up_weight, preferred_element_type=jnp.float32)
    sigmoid_gate = jax.nn.sigmoid(gate)
    swished = gate * sigmoid_gate
    hidden = (swished * up).astype(jnp.bfloat16)
    hidden_grad = jnp.dot(masked, down_weight.T, preferred_element_type=jnp.float32)
    gate_rows = (hidden_grad * up * sigmoid_gate * (1.0 + gate * (1.0 - sigmoid_gate))).astype(jnp.bfloat16)
    up_rows = (hidden_grad * swished).astype(jnp.bfloat16)

    def replica_terms(carry, pieces):
        normed_part, masked_part, hidden_part, gate_part, up_part = pieces
        gate_term = jnp.dot(normed_part.T, gate_part, preferred_element_type=jnp.float32)
        up_term = jnp.dot(normed_part.T, up_part, preferred_element_type=jnp.float32)
        down_term = jnp.dot(hidden_part.T, masked_part, preferred_element_type=jnp.float32)
        return ((carry[0] + rounded(gate_term), carry[1] + rounded(up_term), carry[2] + rounded(down_term)), None)
    pieces = (normed.reshape(N_REP, WINDOW, D), masked.reshape(N_REP, WINDOW, D), hidden.reshape(N_REP, WINDOW, FF), gate_rows.reshape(N_REP, WINDOW, FF), up_rows.reshape(N_REP, WINDOW, FF))
    initial = (jnp.zeros((D, FF), jnp.float32), jnp.zeros((D, FF), jnp.float32), jnp.zeros((FF, D), jnp.float32))
    grads, _ = lax.scan(replica_terms, initial, pieces)
    feature_grad = jnp.dot(gate_rows, gate_weight.T, preferred_element_type=jnp.float32)
    feature_grad = feature_grad + jnp.dot(up_rows, up_weight.T, preferred_element_type=jnp.float32)
    _, pullback = jax.vjp(partial(normalize, norm_gain=norm_gain), widened)
    branch_grad = pullback(feature_grad)[0].astype(jnp.bfloat16)
    return (branch_grad, grads[0], grads[1], grads[2])
```

```python
from functools import partial

import jax
import jax.numpy as jnp
from jax import lax
from jax.sharding import PartitionSpec as P

REC = 1
MAXACT = 8


EPSILON = 1e-05


def normalize(widened, norm_gain):
    factor = lax.rsqrt(jnp.mean(widened * widened, axis=-1, keepdims=True) + EPSILON)
    return widened * factor * norm_gain


def contract_first(left, right):
    return lax.dot_general(
        left, right, (((0,), (0,)), ((), ())), preferred_element_type=jnp.float32
    )


def contract_last(left, right):
    return lax.dot_general(
        left, right, (((1,), (1,)), ((), ())), preferred_element_type=jnp.float32
    )


def local(tokens, cotangent, norm_gain, gate_weight, up_weight, down_weight, depths):
    parts = lax.axis_size("fsdp")
    place = lax.axis_index("fsdp")
    replicas = lax.axis_size("rep")
    replica = lax.axis_index("rep")
    features = tokens.shape[1]
    feature_share = features // replicas
    rows_here = tokens.shape[0]
    own_rows = rows_here // parts
    active = depths > REC
    ordinal = jnp.cumsum(active.astype(jnp.int32)) - 1
    selector = (ordinal[None, :] == jnp.arange(MAXACT, dtype=jnp.int32)[:, None]) & active[None, :]
    picker = selector.astype(jnp.bfloat16)
    source = jnp.dot(picker, tokens, preferred_element_type=jnp.float32)
    send_masked = jnp.dot(picker, cotangent, preferred_element_type=jnp.float32).astype(jnp.bfloat16)
    send_normed = normalize(source, norm_gain).astype(jnp.bfloat16)
    all_normed = lax.all_gather(send_normed, ("rep", "seq"), axis=0, tiled=True)
    all_masked = lax.all_gather(send_masked, ("rep", "seq"), axis=0, tiled=True)
    gate = jnp.dot(all_normed, gate_weight, preferred_element_type=jnp.float32)
    up = jnp.dot(all_normed, up_weight, preferred_element_type=jnp.float32)
    sigmoid_gate = jax.nn.sigmoid(gate)
    swished = gate * sigmoid_gate
    hidden = (swished * up).astype(jnp.bfloat16)
    hidden_grad = contract_last(all_masked, down_weight)
    gate_rows = (hidden_grad * up * sigmoid_gate * (1.0 + gate * (1.0 - sigmoid_gate))).astype(
        jnp.bfloat16
    )
    up_rows = (hidden_grad * swished).astype(jnp.bfloat16)
    normed_cols = lax.dynamic_slice_in_dim(all_normed, replica * feature_share, feature_share, 1)
    masked_cols = lax.dynamic_slice_in_dim(all_masked, replica * feature_share, feature_share, 1)
    gate_grad = contract_first(normed_cols, gate_rows)
    up_grad = contract_first(normed_cols, up_rows)
    down_grad = contract_first(hidden, masked_cols)
    window = all_normed.shape[0] // replicas
    window_gate = lax.dynamic_slice_in_dim(gate_rows, replica * window, window, 0)
    window_up = lax.dynamic_slice_in_dim(up_rows, replica * window, window, 0)
    partial_features = contract_last(window_gate, gate_weight) + contract_last(window_up, up_weight)
    slot_count = send_normed.shape[0]
    share = slot_count // parts
    feature_grad = lax.psum_scatter(
        partial_features.astype(jnp.bfloat16),
        ("seq", "fsdp"),
        scatter_dimension=0,
        tiled=True,
    ).astype(jnp.float32)
    mine = lax.dynamic_slice_in_dim(source, place * share, share, 0)
    _, pullback = jax.vjp(partial(normalize, norm_gain=norm_gain), mine)
    slot_grad = pullback(feature_grad)[0].astype(jnp.bfloat16)
    every_slot = lax.all_gather(slot_grad, "fsdp", axis=0, tiled=True)
    own_columns = lax.dynamic_slice_in_dim(picker, place * own_rows, own_rows, 1)
    branch_grad = contract_first(own_columns, every_slot).astype(jnp.bfloat16)
    return (branch_grad, gate_grad, up_grad, down_grad)


def solution(mesh):
    in_specs = (
        P(("rep", "seq"), None),
        P(("rep", "seq"), None),
        P(),
        P(None, ("seq", "fsdp")),
        P(None, ("seq", "fsdp")),
        P(("seq", "fsdp"), None),
        P(("rep", "seq")),
    )
    out_specs = (
        P(("rep", "seq", "fsdp"), None),
        P("rep", ("seq", "fsdp")),
        P("rep", ("seq", "fsdp")),
        P(("seq", "fsdp"), "rep"),
    )
    return jax.shard_map(local, mesh=mesh, in_specs=in_specs, out_specs=out_specs, check_vma=False)
```

```python
from functools import partial

import jax
import jax.numpy as jnp
from jax import lax
from jax.sharding import PartitionSpec as P

REC = 1
MAXACT = 8


EPSILON = 1e-05


def normalize(widened, norm_gain):
    factor = lax.rsqrt(jnp.mean(widened * widened, axis=-1, keepdims=True) + EPSILON)
    return widened * factor * norm_gain


def contract_first(left, right):
    return lax.dot_general(
        left, right, (((0,), (0,)), ((), ())), preferred_element_type=jnp.float32
    )


def contract_last(left, right):
    return lax.dot_general(
        left, right, (((1,), (1,)), ((), ())), preferred_element_type=jnp.float32
    )


def local(tokens, cotangent, norm_gain, gate_weight, up_weight, down_weight, depths):
    parts = lax.axis_size("fsdp")
    place = lax.axis_index("fsdp")
    replicas = lax.axis_size("rep")
    shards = lax.axis_size("seq")
    features = tokens.shape[1]
    feature_share = features // replicas
    rows_here = tokens.shape[0]
    own_rows = rows_here // parts
    active = depths > REC
    ordinal = jnp.cumsum(active.astype(jnp.int32)) - 1
    selector = (ordinal[None, :] == jnp.arange(MAXACT, dtype=jnp.int32)[:, None]) & active[None, :]
    picker = selector.astype(jnp.bfloat16)
    source = jnp.dot(picker, tokens, preferred_element_type=jnp.float32)
    send_masked = jnp.dot(picker, cotangent, preferred_element_type=jnp.float32).astype(jnp.bfloat16)
    send_normed = normalize(source, norm_gain).astype(jnp.bfloat16)
    packed = lax.all_gather(
        jnp.concatenate([send_normed, send_masked], axis=0), "seq", axis=0, tiled=False
    )
    window_normed = packed[:, :MAXACT].reshape(shards * MAXACT, features)
    window_masked = packed[:, MAXACT:].reshape(shards * MAXACT, features)
    window = window_normed.shape[0]
    gate = jnp.dot(window_normed, gate_weight, preferred_element_type=jnp.float32)
    up = jnp.dot(window_normed, up_weight, preferred_element_type=jnp.float32)
    sigmoid_gate = jax.nn.sigmoid(gate)
    swished = gate * sigmoid_gate
    hidden = (swished * up).astype(jnp.bfloat16)
    hidden_grad = contract_last(window_masked, down_weight)
    gate_rows = (hidden_grad * up * sigmoid_gate * (1.0 + gate * (1.0 - sigmoid_gate))).astype(
        jnp.bfloat16
    )
    up_rows = (hidden_grad * swished).astype(jnp.bfloat16)
    partial_features = contract_last(gate_rows, gate_weight) + contract_last(up_rows, up_weight)
    outgoing = jnp.broadcast_to(
        partial_features.astype(jnp.bfloat16).reshape(shards, 1, MAXACT, features),
        (shards, parts, MAXACT, features),
    ).reshape(shards * parts, MAXACT, features)
    incoming = lax.all_to_all(outgoing, ("seq", "fsdp"), 0, 0, tiled=True)
    feature_grad = jnp.sum(incoming.astype(jnp.float32), axis=0)
    factors = lax.all_gather(
        jnp.concatenate([gate_rows, up_rows, hidden], axis=0), "rep", axis=0, tiled=False
    )
    every_gate = factors[:, :window].reshape(replicas * window, -1)
    every_up = factors[:, window : 2 * window].reshape(replicas * window, -1)
    every_hidden = factors[:, 2 * window :].reshape(replicas * window, -1)
    columns = jnp.concatenate([window_normed, window_masked], axis=0)
    columns = columns.reshape(2 * window, replicas, feature_share).transpose(1, 0, 2)
    columns = lax.all_to_all(columns, "rep", 0, 0, tiled=True)
    normed_cols = columns[:, :window].reshape(replicas * window, feature_share)
    masked_cols = columns[:, window:].reshape(replicas * window, feature_share)
    gate_grad = contract_first(normed_cols, every_gate)
    up_grad = contract_first(normed_cols, every_up)
    down_grad = contract_first(every_hidden, masked_cols)
    _, pullback = jax.vjp(partial(normalize, norm_gain=norm_gain), source)
    slot_grad = pullback(feature_grad)[0].astype(jnp.bfloat16)
    own_columns = lax.dynamic_slice_in_dim(picker, place * own_rows, own_rows, 1)
    branch_grad = contract_first(own_columns, slot_grad).astype(jnp.bfloat16)
    return (branch_grad, gate_grad, up_grad, down_grad)


def solution(mesh):
    in_specs = (
        P(("rep", "seq"), None),
        P(("rep", "seq"), None),
        P(),
        P(None, ("seq", "fsdp")),
        P(None, ("seq", "fsdp")),
        P(("seq", "fsdp"), None),
        P(("rep", "seq")),
    )
    out_specs = (
        P(("rep", "seq", "fsdp"), None),
        P("rep", ("seq", "fsdp")),
        P("rep", ("seq", "fsdp")),
        P(("seq", "fsdp"), "rep"),
    )
    return jax.shard_map(local, mesh=mesh, in_specs=in_specs, out_specs=out_specs, check_vma=False)
```

```python
from functools import partial

import jax
import jax.numpy as jnp
from jax import lax
from jax.sharding import PartitionSpec as P

REC = 1
MAXACT = 8


EPSILON = 1e-05


def normalize(widened, norm_gain):
    factor = lax.rsqrt(jnp.mean(widened * widened, axis=-1, keepdims=True) + EPSILON)
    return widened * factor * norm_gain


def contract_first(left, right):
    return lax.dot_general(
        left, right, (((0,), (0,)), ((), ())), preferred_element_type=jnp.float32
    )


def contract_last(left, right):
    return lax.dot_general(
        left, right, (((1,), (1,)), ((), ())), preferred_element_type=jnp.float32
    )


def shifted(value, axes, sizes, steps):
    total = 1
    for size in sizes:
        total *= size
    pairs = []
    for index in range(total):
        coords, rest = [], index
        for size in reversed(sizes):
            coords.append(rest % size)
            rest //= size
        coords = coords[::-1]
        target, scale = 0, 1
        for axis in reversed(range(len(sizes))):
            target += ((coords[axis] + steps[axis]) % sizes[axis]) * scale
            scale *= sizes[axis]
        pairs.append((index, target))
    return lax.ppermute(value, axes, pairs)


def local(tokens, cotangent, norm_gain, gate_weight, up_weight, down_weight, depths):
    parts = lax.axis_size("fsdp")
    place = lax.axis_index("fsdp")
    replicas = lax.axis_size("rep")
    shards = lax.axis_size("seq")
    features = tokens.shape[1]
    feature_share = features // replicas
    rows_here = tokens.shape[0]
    own_rows = rows_here // parts
    active = depths > REC
    ordinal = jnp.cumsum(active.astype(jnp.int32)) - 1
    selector = (ordinal[None, :] == jnp.arange(MAXACT, dtype=jnp.int32)[:, None]) & active[None, :]
    picker = selector.astype(jnp.bfloat16)
    source = jnp.dot(picker, tokens, preferred_element_type=jnp.float32)
    send_masked = jnp.dot(picker, cotangent, preferred_element_type=jnp.float32).astype(jnp.bfloat16)
    send_normed = normalize(source, norm_gain).astype(jnp.bfloat16)
    packed = jnp.concatenate([send_normed, send_masked], axis=0)
    blocks = [packed] + [shifted(packed, "seq", (shards,), (k,)) for k in range(1, shards)]
    window_normed = jnp.concatenate([b[:MAXACT] for b in blocks], axis=0)
    window_masked = jnp.concatenate([b[MAXACT:] for b in blocks], axis=0)
    window = window_normed.shape[0]
    gate = jnp.dot(window_normed, gate_weight, preferred_element_type=jnp.float32)
    up = jnp.dot(window_normed, up_weight, preferred_element_type=jnp.float32)
    sigmoid_gate = jax.nn.sigmoid(gate)
    swished = gate * sigmoid_gate
    hidden = (swished * up).astype(jnp.bfloat16)
    hidden_grad = contract_last(window_masked, down_weight)
    gate_rows = (hidden_grad * up * sigmoid_gate * (1.0 + gate * (1.0 - sigmoid_gate))).astype(
        jnp.bfloat16
    )
    up_rows = (hidden_grad * swished).astype(jnp.bfloat16)
    factors = jnp.concatenate([gate_rows, up_rows, hidden], axis=0)
    columns = jnp.concatenate([window_normed, window_masked], axis=0)
    columns = columns.reshape(2 * window, replicas, feature_share)
    replica = lax.axis_index("rep")
    every_factors = [factors]
    every_columns = [lax.dynamic_index_in_dim(columns, replica, 1, keepdims=False)]
    for j in range(1, replicas):
        every_factors.append(shifted(factors, "rep", (replicas,), (j,)))
        outgoing = lax.dynamic_index_in_dim(columns, (replica + j) % replicas, 1, keepdims=False)
        every_columns.append(shifted(outgoing, "rep", (replicas,), (j,)))
    partial_features = (
        contract_last(gate_rows, gate_weight) + contract_last(up_rows, up_weight)
    ).astype(jnp.bfloat16)
    feature_grad = partial_features[:MAXACT].astype(jnp.float32)
    for k in range(shards):
        piece = partial_features[k * MAXACT : (k + 1) * MAXACT]
        for step in range(parts):
            if k == 0 and step == 0:
                continue
            arrived = shifted(piece, ("seq", "fsdp"), (shards, parts), (-k, step))
            feature_grad = feature_grad + arrived.astype(jnp.float32)
    every_gate = jnp.concatenate([f[:window] for f in every_factors], axis=0)
    every_up = jnp.concatenate([f[window : 2 * window] for f in every_factors], axis=0)
    every_hidden = jnp.concatenate([f[2 * window :] for f in every_factors], axis=0)
    normed_cols = jnp.concatenate([c[:window] for c in every_columns], axis=0)
    masked_cols = jnp.concatenate([c[window:] for c in every_columns], axis=0)
    gate_grad = contract_first(normed_cols, every_gate)
    up_grad = contract_first(normed_cols, every_up)
    down_grad = contract_first(every_hidden, masked_cols)
    _, pullback = jax.vjp(partial(normalize, norm_gain=norm_gain), source)
    slot_grad = pullback(feature_grad)[0].astype(jnp.bfloat16)
    own_columns = lax.dynamic_slice_in_dim(picker, place * own_rows, own_rows, 1)
    branch_grad = contract_first(own_columns, slot_grad).astype(jnp.bfloat16)
    return (branch_grad, gate_grad, up_grad, down_grad)


def solution(mesh):
    in_specs = (
        P(("rep", "seq"), None),
        P(("rep", "seq"), None),
        P(),
        P(None, ("seq", "fsdp")),
        P(None, ("seq", "fsdp")),
        P(("seq", "fsdp"), None),
        P(("rep", "seq")),
    )
    out_specs = (
        P(("rep", "seq", "fsdp"), None),
        P("rep", ("seq", "fsdp")),
        P("rep", ("seq", "fsdp")),
        P(("seq", "fsdp"), "rep"),
    )
    return jax.shard_map(local, mesh=mesh, in_specs=in_specs, out_specs=out_specs, check_vma=False)
```

```python
from functools import partial

import jax
import jax.numpy as jnp
from jax import lax
from jax.sharding import PartitionSpec as P

REC = 1
MAXACT = 8


EPSILON = 1e-05


def normalize(widened, norm_gain):
    factor = lax.rsqrt(jnp.mean(widened * widened, axis=-1, keepdims=True) + EPSILON)
    return widened * factor * norm_gain


def contract_first(left, right):
    return lax.dot_general(
        left, right, (((0,), (0,)), ((), ())), preferred_element_type=jnp.float32
    )


def contract_last(left, right):
    return lax.dot_general(
        left, right, (((1,), (1,)), ((), ())), preferred_element_type=jnp.float32
    )


def shifted(value, axes, sizes, steps):
    total = 1
    for size in sizes:
        total *= size
    pairs = []
    for index in range(total):
        coords, rest = [], index
        for size in reversed(sizes):
            coords.append(rest % size)
            rest //= size
        coords = coords[::-1]
        target, scale = 0, 1
        for axis in reversed(range(len(sizes))):
            target += ((coords[axis] + steps[axis]) % sizes[axis]) * scale
            scale *= sizes[axis]
        pairs.append((index, target))
    return lax.ppermute(value, axes, pairs)


def swapped(value, axis, size, distance):
    return lax.ppermute(value, axis, [(i, i ^ distance) for i in range(size)])


def power_of_two(size):
    return size & (size - 1) == 0


def gather_blocks(value, axis, size):
    if power_of_two(size):
        blocks, distance = [value], 1
        while distance < size:
            arrived = swapped(jnp.stack(blocks), axis, size, distance)
            blocks = blocks + [arrived[k] for k in range(distance)]
            distance *= 2
        return blocks, lambda k: ("xor", k)
    blocks = [value] + [shifted(value, axis, (size,), (k,)) for k in range(1, size)]
    return blocks, lambda k: ("shift", k)


def scatter_sum(pieces, axis, size):
    if power_of_two(size):
        held = {k: piece.astype(jnp.float32) for k, piece in enumerate(pieces)}
        distance = size // 2
        while distance >= 1:
            leaving = sorted(k for k in held if k & distance)
            arrived = swapped(
                jnp.stack([held[k] for k in leaving]).astype(jnp.bfloat16), axis, size, distance
            )
            for position, k in enumerate(leaving):
                held[k ^ distance] = held[k ^ distance] + arrived[position].astype(jnp.float32)
            held = {k: v for k, v in held.items() if not k & distance}
            distance //= 2
        return held[0]
    total = pieces[0].astype(jnp.float32)
    for k in range(1, size):
        total = total + shifted(pieces[k], axis, (size,), (-k,)).astype(jnp.float32)
    return total


def all_sum(value, axis, size):
    if power_of_two(size):
        total, distance = value, 1
        while distance < size:
            total = total + swapped(total.astype(jnp.bfloat16), axis, size, distance).astype(jnp.float32)
            distance *= 2
        return total
    total = value
    for k in range(1, size):
        total = total + shifted(value.astype(jnp.bfloat16), axis, (size,), (k,)).astype(jnp.float32)
    return total


def exchange_blocks(blocks, axis, size):
    index = lax.axis_index(axis)
    if power_of_two(size):
        stacked = jnp.stack(blocks)
        held = {(0, k): lax.dynamic_index_in_dim(stacked, index ^ k, 0, keepdims=False) for k in range(size)}
        distance = 1
        while distance < size:
            leaving = sorted(key for key in held if key[1] & distance)
            arrived = swapped(jnp.stack([held[key] for key in leaving]), axis, size, distance)
            held = {key: v for key, v in held.items() if not key[1] & distance}
            for position, (origin, target) in enumerate(leaving):
                held[(origin ^ distance, target ^ distance)] = arrived[position]
            distance *= 2
        return [held[(k, 0)] for k in range(size)]
    stacked = jnp.stack(blocks)
    out = [lax.dynamic_index_in_dim(stacked, index, 0, keepdims=False)]
    for k in range(1, size):
        outgoing = lax.dynamic_index_in_dim(stacked, (index + k) % size, 0, keepdims=False)
        out.append(shifted(outgoing, axis, (size,), (k,)))
    return out


def local(tokens, cotangent, norm_gain, gate_weight, up_weight, down_weight, depths):
    parts = lax.axis_size("fsdp")
    place = lax.axis_index("fsdp")
    replicas = lax.axis_size("rep")
    shards = lax.axis_size("seq")
    features = tokens.shape[1]
    feature_share = features // replicas
    rows_here = tokens.shape[0]
    own_rows = rows_here // parts
    active = depths > REC
    ordinal = jnp.cumsum(active.astype(jnp.int32)) - 1
    selector = (ordinal[None, :] == jnp.arange(MAXACT, dtype=jnp.int32)[:, None]) & active[None, :]
    picker = selector.astype(jnp.bfloat16)
    source = jnp.dot(picker, tokens, preferred_element_type=jnp.float32)
    send_masked = jnp.dot(picker, cotangent, preferred_element_type=jnp.float32).astype(jnp.bfloat16)
    send_normed = normalize(source, norm_gain).astype(jnp.bfloat16)
    blocks, _ = gather_blocks(jnp.concatenate([send_normed, send_masked], axis=0), "seq", shards)
    window_normed = jnp.concatenate([b[:MAXACT] for b in blocks], axis=0)
    window_masked = jnp.concatenate([b[MAXACT:] for b in blocks], axis=0)
    window = window_normed.shape[0]
    columns = jnp.concatenate([window_normed, window_masked], axis=0)
    columns = columns.reshape(2 * window, replicas, feature_share)
    every_columns = exchange_blocks(
        [columns[:, b] for b in range(replicas)], "rep", replicas
    )
    gate = jnp.dot(window_normed, gate_weight, preferred_element_type=jnp.float32)
    up = jnp.dot(window_normed, up_weight, preferred_element_type=jnp.float32)
    sigmoid_gate = jax.nn.sigmoid(gate)
    swished = gate * sigmoid_gate
    hidden = (swished * up).astype(jnp.bfloat16)
    hidden_grad = contract_last(window_masked, down_weight)
    gate_rows = (hidden_grad * up * sigmoid_gate * (1.0 + gate * (1.0 - sigmoid_gate))).astype(
        jnp.bfloat16
    )
    up_rows = (hidden_grad * swished).astype(jnp.bfloat16)
    every_factors, _ = gather_blocks(
        jnp.concatenate([gate_rows, up_rows, hidden], axis=0), "rep", replicas
    )
    partial_features = contract_last(gate_rows, gate_weight) + contract_last(up_rows, up_weight)
    pieces = [partial_features[k * MAXACT : (k + 1) * MAXACT] for k in range(shards)]
    feature_grad = all_sum(scatter_sum(pieces, "seq", shards), "fsdp", parts)
    every_gate = jnp.concatenate([f[:window] for f in every_factors], axis=0)
    every_up = jnp.concatenate([f[window : 2 * window] for f in every_factors], axis=0)
    every_hidden = jnp.concatenate([f[2 * window :] for f in every_factors], axis=0)
    normed_cols = jnp.concatenate([c[:window] for c in every_columns], axis=0)
    masked_cols = jnp.concatenate([c[window:] for c in every_columns], axis=0)
    gate_grad = contract_first(normed_cols, every_gate)
    up_grad = contract_first(normed_cols, every_up)
    down_grad = contract_first(every_hidden, masked_cols)
    _, pullback = jax.vjp(partial(normalize, norm_gain=norm_gain), source)
    slot_grad = pullback(feature_grad)[0].astype(jnp.bfloat16)
    own_columns = lax.dynamic_slice_in_dim(picker, place * own_rows, own_rows, 1)
    branch_grad = contract_first(own_columns, slot_grad).astype(jnp.bfloat16)
    return (branch_grad, gate_grad, up_grad, down_grad)


def solution(mesh):
    in_specs = (
        P(("rep", "seq"), None),
        P(("rep", "seq"), None),
        P(),
        P(None, ("seq", "fsdp")),
        P(None, ("seq", "fsdp")),
        P(("seq", "fsdp"), None),
        P(("rep", "seq")),
    )
    out_specs = (
        P(("rep", "seq", "fsdp"), None),
        P("rep", ("seq", "fsdp")),
        P("rep", ("seq", "fsdp")),
        P(("seq", "fsdp"), "rep"),
    )
    return jax.shard_map(local, mesh=mesh, in_specs=in_specs, out_specs=out_specs, check_vma=False)
```

```python
from functools import partial

import jax
import jax.numpy as jnp
from jax import lax
from jax.experimental import pallas as pl
from jax.sharding import PartitionSpec as P

REC = 1
MAXACT = 8


EPSILON = 1e-05


def normalize(widened, norm_gain):
    factor = lax.rsqrt(jnp.mean(widened * widened, axis=-1, keepdims=True) + EPSILON)
    return widened * factor * norm_gain


def contract_first(left, right):
    return lax.dot_general(
        left, right, (((0,), (0,)), ((), ())), preferred_element_type=jnp.float32
    )


def contract_last(left, right):
    return lax.dot_general(
        left, right, (((1,), (1,)), ((), ())), preferred_element_type=jnp.float32
    )


def shifted(value, axes, sizes, steps):
    total = 1
    for size in sizes:
        total *= size
    pairs = []
    for index in range(total):
        coords, rest = [], index
        for size in reversed(sizes):
            coords.append(rest % size)
            rest //= size
        coords = coords[::-1]
        target, scale = 0, 1
        for axis in reversed(range(len(sizes))):
            target += ((coords[axis] + steps[axis]) % sizes[axis]) * scale
            scale *= sizes[axis]
        pairs.append((index, target))
    return lax.ppermute(value, axes, pairs)


def swapped(value, axis, size, distance):
    return lax.ppermute(value, axis, [(i, i ^ distance) for i in range(size)])


def power_of_two(size):
    return size & (size - 1) == 0


def gather_blocks(value, axis, size):
    if power_of_two(size):
        blocks, distance = [value], 1
        while distance < size:
            arrived = swapped(jnp.stack(blocks), axis, size, distance)
            blocks = blocks + [arrived[k] for k in range(distance)]
            distance *= 2
        return blocks, lambda k: ("xor", k)
    blocks = [value] + [shifted(value, axis, (size,), (k,)) for k in range(1, size)]
    return blocks, lambda k: ("shift", k)


def scatter_sum(pieces, axis, size):
    if power_of_two(size):
        held = {k: piece.astype(jnp.float32) for k, piece in enumerate(pieces)}
        distance = size // 2
        while distance >= 1:
            leaving = sorted(k for k in held if k & distance)
            arrived = swapped(
                jnp.stack([held[k] for k in leaving]).astype(jnp.bfloat16), axis, size, distance
            )
            for position, k in enumerate(leaving):
                held[k ^ distance] = held[k ^ distance] + arrived[position].astype(jnp.float32)
            held = {k: v for k, v in held.items() if not k & distance}
            distance //= 2
        return held[0]
    total = pieces[0].astype(jnp.float32)
    for k in range(1, size):
        total = total + shifted(pieces[k], axis, (size,), (-k,)).astype(jnp.float32)
    return total


def all_sum(value, axis, size):
    if power_of_two(size):
        total, distance = value, 1
        while distance < size:
            total = total + swapped(total.astype(jnp.bfloat16), axis, size, distance).astype(jnp.float32)
            distance *= 2
        return total
    total = value
    for k in range(1, size):
        total = total + shifted(value.astype(jnp.bfloat16), axis, (size,), (k,)).astype(jnp.float32)
    return total


def exchange_blocks(blocks, axis, size):
    index = lax.axis_index(axis)
    if power_of_two(size):
        stacked = jnp.stack(blocks)
        held = {(0, k): lax.dynamic_index_in_dim(stacked, index ^ k, 0, keepdims=False) for k in range(size)}
        distance = 1
        while distance < size:
            leaving = sorted(key for key in held if key[1] & distance)
            arrived = swapped(jnp.stack([held[key] for key in leaving]), axis, size, distance)
            held = {key: v for key, v in held.items() if not key[1] & distance}
            for position, (origin, target) in enumerate(leaving):
                held[(origin ^ distance, target ^ distance)] = arrived[position]
            distance *= 2
        return [held[(k, 0)] for k in range(size)]
    stacked = jnp.stack(blocks)
    out = [lax.dynamic_index_in_dim(stacked, index, 0, keepdims=False)]
    for k in range(1, size):
        outgoing = lax.dynamic_index_in_dim(stacked, (index + k) % size, 0, keepdims=False)
        out.append(shifted(outgoing, axis, (size,), (k,)))
    return out


def weight_pass_kernel(normed_ref, masked_ref, gate_w_ref, up_w_ref, down_w_ref,
                       gate_rows_ref, up_rows_ref, hidden_ref, features_ref):
    step = pl.program_id(0)
    normed = normed_ref[...]
    gate_w = gate_w_ref[...]
    up_w = up_w_ref[...]
    gate = jnp.dot(normed, gate_w, preferred_element_type=jnp.float32)
    up = jnp.dot(normed, up_w, preferred_element_type=jnp.float32)
    hidden_grad = contract_last(masked_ref[...], down_w_ref[...])
    sigmoid_gate = 1.0 / (1.0 + jnp.exp(-gate))
    swished = gate * sigmoid_gate
    gate_rows = (hidden_grad * up * sigmoid_gate * (1.0 + gate * (1.0 - sigmoid_gate))).astype(
        jnp.bfloat16
    )
    up_rows = (hidden_grad * swished).astype(jnp.bfloat16)
    hidden_ref[...] = (swished * up).astype(jnp.bfloat16)
    gate_rows_ref[...] = gate_rows
    up_rows_ref[...] = up_rows
    partial_features = contract_last(gate_rows, gate_w) + contract_last(up_rows, up_w)

    @pl.when(step == 0)
    def _():
        features_ref[...] = partial_features

    @pl.when(step > 0)
    def _():
        features_ref[...] += partial_features


def weight_pass(window_normed, window_masked, gate_weight, up_weight, down_weight):
    rows, features = window_normed.shape
    units = gate_weight.shape[1]
    chunk = 256 if units % 256 == 0 else units
    factor_shape = jax.ShapeDtypeStruct((rows, units), jnp.bfloat16)
    return pl.pallas_call(
        weight_pass_kernel,
        grid=(units // chunk,),
        in_specs=[
            pl.BlockSpec((rows, features), lambda j: (0, 0)),
            pl.BlockSpec((rows, features), lambda j: (0, 0)),
            pl.BlockSpec((features, chunk), lambda j: (0, j)),
            pl.BlockSpec((features, chunk), lambda j: (0, j)),
            pl.BlockSpec((chunk, features), lambda j: (j, 0)),
        ],
        out_specs=[
            pl.BlockSpec((rows, chunk), lambda j: (0, j)),
            pl.BlockSpec((rows, chunk), lambda j: (0, j)),
            pl.BlockSpec((rows, chunk), lambda j: (0, j)),
            pl.BlockSpec((rows, features), lambda j: (0, 0)),
        ],
        out_shape=[
            factor_shape,
            factor_shape,
            factor_shape,
            jax.ShapeDtypeStruct((rows, features), jnp.float32),
        ],
        cost_estimate=pl.CostEstimate(
            flops=10 * rows * features * units,
            transcendentals=rows * units,
            bytes_accessed=6 * features * units + 4 * rows * features * 2,
        ),
    )(window_normed, window_masked, gate_weight, up_weight, down_weight)


def local(tokens, cotangent, norm_gain, gate_weight, up_weight, down_weight, depths):
    parts = lax.axis_size("fsdp")
    place = lax.axis_index("fsdp")
    replicas = lax.axis_size("rep")
    replica = lax.axis_index("rep")
    shards = lax.axis_size("seq")
    features = tokens.shape[1]
    feature_share = features // replicas
    rows_here = tokens.shape[0]
    own_rows = rows_here // parts
    active = depths > REC
    ordinal = jnp.cumsum(active.astype(jnp.int32)) - 1
    selector = (ordinal[None, :] == jnp.arange(MAXACT, dtype=jnp.int32)[:, None]) & active[None, :]
    picker = selector.astype(jnp.bfloat16)
    source = jnp.dot(picker, tokens, preferred_element_type=jnp.float32)
    send_masked = jnp.dot(picker, cotangent, preferred_element_type=jnp.float32).astype(jnp.bfloat16)
    send_normed = normalize(source, norm_gain).astype(jnp.bfloat16)
    packed = jnp.concatenate([send_normed, send_masked], axis=0)
    blocks = [packed] + [shifted(packed, "seq", (shards,), (k,)) for k in range(1, shards)]
    window_normed = jnp.concatenate([b[:MAXACT] for b in blocks], axis=0)
    window_masked = jnp.concatenate([b[MAXACT:] for b in blocks], axis=0)
    window = window_normed.shape[0]
    columns = jnp.concatenate([window_normed, window_masked], axis=0)
    columns = columns.reshape(2 * window, replicas, feature_share)
    every_columns = [lax.dynamic_index_in_dim(columns, replica, 1, keepdims=False)]
    for j in range(1, replicas):
        outgoing = lax.dynamic_index_in_dim(columns, (replica + j) % replicas, 1, keepdims=False)
        every_columns.append(shifted(outgoing, "rep", (replicas,), (j,)))
    gate_rows, up_rows, hidden, partial_features = weight_pass(
        window_normed, window_masked, gate_weight, up_weight, down_weight
    )
    factors = jnp.concatenate([gate_rows, up_rows, hidden], axis=0)
    every_factors = [factors] + [shifted(factors, "rep", (replicas,), (j,)) for j in range(1, replicas)]
    partial_features = partial_features.astype(jnp.bfloat16)
    feature_grad = partial_features[:MAXACT].astype(jnp.float32)
    for k in range(1, shards):
        piece = partial_features[k * MAXACT : (k + 1) * MAXACT]
        feature_grad = feature_grad + shifted(piece, "seq", (shards,), (-k,)).astype(jnp.float32)
    seq_sum = feature_grad.astype(jnp.bfloat16)
    for step in range(1, parts):
        feature_grad = feature_grad + shifted(seq_sum, "fsdp", (parts,), (step,)).astype(jnp.float32)
    every_gate = jnp.concatenate([f[:window] for f in every_factors], axis=0)
    every_up = jnp.concatenate([f[window : 2 * window] for f in every_factors], axis=0)
    every_hidden = jnp.concatenate([f[2 * window :] for f in every_factors], axis=0)
    normed_cols = jnp.concatenate([c[:window] for c in every_columns], axis=0)
    masked_cols = jnp.concatenate([c[window:] for c in every_columns], axis=0)
    gate_grad = contract_first(normed_cols, every_gate)
    up_grad = contract_first(normed_cols, every_up)
    down_grad = contract_first(every_hidden, masked_cols)
    _, pullback = jax.vjp(partial(normalize, norm_gain=norm_gain), source)
    slot_grad = pullback(feature_grad)[0].astype(jnp.bfloat16)
    own_columns = lax.dynamic_slice_in_dim(picker, place * own_rows, own_rows, 1)
    branch_grad = contract_first(own_columns, slot_grad).astype(jnp.bfloat16)
    return (branch_grad, gate_grad, up_grad, down_grad)


def solution(mesh):
    in_specs = (
        P(("rep", "seq"), None),
        P(("rep", "seq"), None),
        P(),
        P(None, ("seq", "fsdp")),
        P(None, ("seq", "fsdp")),
        P(("seq", "fsdp"), None),
        P(("rep", "seq")),
    )
    out_specs = (
        P(("rep", "seq", "fsdp"), None),
        P("rep", ("seq", "fsdp")),
        P("rep", ("seq", "fsdp")),
        P(("seq", "fsdp"), "rep"),
    )
    return jax.shard_map(local, mesh=mesh, in_specs=in_specs, out_specs=out_specs, check_vma=False)
```

```python
from functools import partial

import jax
import jax.numpy as jnp
from jax import lax
from jax.experimental import pallas as pl
from jax.experimental.pallas import tpu as pltpu
from jax.sharding import PartitionSpec as P

REC = 1
MAXACT = 8


EPSILON = 1e-05


def normalize(widened, norm_gain):
    factor = lax.rsqrt(jnp.mean(widened * widened, axis=-1, keepdims=True) + EPSILON)
    return widened * factor * norm_gain


def contract_first(left, right):
    return lax.dot_general(
        left, right, (((0,), (0,)), ((), ())), preferred_element_type=jnp.float32
    )


def contract_last(left, right):
    return lax.dot_general(
        left, right, (((1,), (1,)), ((), ())), preferred_element_type=jnp.float32
    )


def shifted(value, axes, sizes, steps):
    total = 1
    for size in sizes:
        total *= size
    pairs = []
    for index in range(total):
        coords, rest = [], index
        for size in reversed(sizes):
            coords.append(rest % size)
            rest //= size
        coords = coords[::-1]
        target, scale = 0, 1
        for axis in reversed(range(len(sizes))):
            target += ((coords[axis] + steps[axis]) % sizes[axis]) * scale
            scale *= sizes[axis]
        pairs.append((index, target))
    return lax.ppermute(value, axes, pairs)


def swapped(value, axis, size, distance):
    return lax.ppermute(value, axis, [(i, i ^ distance) for i in range(size)])


def power_of_two(size):
    return size & (size - 1) == 0


def gather_blocks(value, axis, size):
    if power_of_two(size):
        blocks, distance = [value], 1
        while distance < size:
            arrived = swapped(jnp.stack(blocks), axis, size, distance)
            blocks = blocks + [arrived[k] for k in range(distance)]
            distance *= 2
        return blocks, lambda k: ("xor", k)
    blocks = [value] + [shifted(value, axis, (size,), (k,)) for k in range(1, size)]
    return blocks, lambda k: ("shift", k)


def scatter_sum(pieces, axis, size):
    if power_of_two(size):
        held = {k: piece.astype(jnp.float32) for k, piece in enumerate(pieces)}
        distance = size // 2
        while distance >= 1:
            leaving = sorted(k for k in held if k & distance)
            arrived = swapped(
                jnp.stack([held[k] for k in leaving]).astype(jnp.bfloat16), axis, size, distance
            )
            for position, k in enumerate(leaving):
                held[k ^ distance] = held[k ^ distance] + arrived[position].astype(jnp.float32)
            held = {k: v for k, v in held.items() if not k & distance}
            distance //= 2
        return held[0]
    total = pieces[0].astype(jnp.float32)
    for k in range(1, size):
        total = total + shifted(pieces[k], axis, (size,), (-k,)).astype(jnp.float32)
    return total


def all_sum(value, axis, size):
    if power_of_two(size):
        total, distance = value, 1
        while distance < size:
            total = total + swapped(total.astype(jnp.bfloat16), axis, size, distance).astype(jnp.float32)
            distance *= 2
        return total
    total = value
    for k in range(1, size):
        total = total + shifted(value.astype(jnp.bfloat16), axis, (size,), (k,)).astype(jnp.float32)
    return total


def exchange_blocks(blocks, axis, size):
    index = lax.axis_index(axis)
    if power_of_two(size):
        stacked = jnp.stack(blocks)
        held = {(0, k): lax.dynamic_index_in_dim(stacked, index ^ k, 0, keepdims=False) for k in range(size)}
        distance = 1
        while distance < size:
            leaving = sorted(key for key in held if key[1] & distance)
            arrived = swapped(jnp.stack([held[key] for key in leaving]), axis, size, distance)
            held = {key: v for key, v in held.items() if not key[1] & distance}
            for position, (origin, target) in enumerate(leaving):
                held[(origin ^ distance, target ^ distance)] = arrived[position]
            distance *= 2
        return [held[(k, 0)] for k in range(size)]
    stacked = jnp.stack(blocks)
    out = [lax.dynamic_index_in_dim(stacked, index, 0, keepdims=False)]
    for k in range(1, size):
        outgoing = lax.dynamic_index_in_dim(stacked, (index + k) % size, 0, keepdims=False)
        out.append(shifted(outgoing, axis, (size,), (k,)))
    return out


def weight_pass_kernel(normed_ref, masked_ref, gate_w_ref, up_w_ref, down_w_ref,
                       gate_rows_ref, up_rows_ref, hidden_ref, features_ref):
    step = pl.program_id(0)
    normed = normed_ref[...]
    gate_w = gate_w_ref[...]
    up_w = up_w_ref[...]
    gate = jnp.dot(normed, gate_w, preferred_element_type=jnp.float32)
    up = jnp.dot(normed, up_w, preferred_element_type=jnp.float32)
    hidden_grad = contract_last(masked_ref[...], down_w_ref[...])
    sigmoid_gate = 1.0 / (1.0 + jnp.exp(-gate))
    swished = gate * sigmoid_gate
    gate_rows = (hidden_grad * up * sigmoid_gate * (1.0 + gate * (1.0 - sigmoid_gate))).astype(
        jnp.bfloat16
    )
    up_rows = (hidden_grad * swished).astype(jnp.bfloat16)
    hidden_ref[...] = (swished * up).astype(jnp.bfloat16)
    gate_rows_ref[...] = gate_rows
    up_rows_ref[...] = up_rows
    partial_features = contract_last(gate_rows, gate_w) + contract_last(up_rows, up_w)

    @pl.when(step == 0)
    def _():
        features_ref[...] = partial_features

    @pl.when(step > 0)
    def _():
        features_ref[...] += partial_features


def weight_pass(window_normed, window_masked, gate_weight, up_weight, down_weight):
    rows, features = window_normed.shape
    units = gate_weight.shape[1]
    chunk = next((size for size in (512, 256, 128) if units % size == 0), units)
    factor_shape = jax.ShapeDtypeStruct((rows, units), jnp.bfloat16)
    return pl.pallas_call(
        weight_pass_kernel,
        grid=(units // chunk,),
        in_specs=[
            pl.BlockSpec((rows, features), lambda j: (0, 0)),
            pl.BlockSpec((rows, features), lambda j: (0, 0)),
            pl.BlockSpec((features, chunk), lambda j: (0, j)),
            pl.BlockSpec((features, chunk), lambda j: (0, j)),
            pl.BlockSpec((chunk, features), lambda j: (j, 0)),
        ],
        out_specs=[
            pl.BlockSpec((rows, chunk), lambda j: (0, j)),
            pl.BlockSpec((rows, chunk), lambda j: (0, j)),
            pl.BlockSpec((rows, chunk), lambda j: (0, j)),
            pl.BlockSpec((rows, features), lambda j: (0, 0)),
        ],
        out_shape=[
            factor_shape,
            factor_shape,
            factor_shape,
            jax.ShapeDtypeStruct((rows, features), jnp.float32),
        ],
        compiler_params=pltpu.CompilerParams(vmem_limit_bytes=56 * 1024 * 1024),
        cost_estimate=pl.CostEstimate(
            flops=10 * rows * features * units,
            transcendentals=rows * units,
            bytes_accessed=6 * features * units + 4 * rows * features * 2,
        ),
    )(window_normed, window_masked, gate_weight, up_weight, down_weight)


def local(tokens, cotangent, norm_gain, gate_weight, up_weight, down_weight, depths):
    parts = lax.axis_size("fsdp")
    place = lax.axis_index("fsdp")
    replicas = lax.axis_size("rep")
    replica = lax.axis_index("rep")
    shards = lax.axis_size("seq")
    features = tokens.shape[1]
    feature_share = features // replicas
    rows_here = tokens.shape[0]
    own_rows = rows_here // parts
    active = depths > REC
    ordinal = jnp.cumsum(active.astype(jnp.int32)) - 1
    selector = (ordinal[None, :] == jnp.arange(MAXACT, dtype=jnp.int32)[:, None]) & active[None, :]
    picker = selector.astype(jnp.bfloat16)
    source = jnp.dot(picker, tokens, preferred_element_type=jnp.float32)
    send_masked = jnp.dot(picker, cotangent, preferred_element_type=jnp.float32).astype(jnp.bfloat16)
    send_normed = normalize(source, norm_gain).astype(jnp.bfloat16)
    packed = jnp.concatenate([send_normed, send_masked], axis=0)
    blocks = [packed] + [shifted(packed, "seq", (shards,), (k,)) for k in range(1, shards)]
    window_normed = jnp.concatenate([b[:MAXACT] for b in blocks], axis=0)
    window_masked = jnp.concatenate([b[MAXACT:] for b in blocks], axis=0)
    window = window_normed.shape[0]
    columns = jnp.concatenate([window_normed, window_masked], axis=0)
    columns = columns.reshape(2 * window, replicas, feature_share)
    every_columns = [lax.dynamic_index_in_dim(columns, replica, 1, keepdims=False)]
    for j in range(1, replicas):
        outgoing = lax.dynamic_index_in_dim(columns, (replica + j) % replicas, 1, keepdims=False)
        every_columns.append(shifted(outgoing, "rep", (replicas,), (j,)))
    gate_rows, up_rows, hidden, partial_features = weight_pass(
        window_normed, window_masked, gate_weight, up_weight, down_weight
    )
    factors = jnp.concatenate([gate_rows, up_rows, hidden], axis=0)
    every_factors = [factors] + [shifted(factors, "rep", (replicas,), (j,)) for j in range(1, replicas)]
    partial_features = partial_features.astype(jnp.bfloat16)
    feature_grad = partial_features[:MAXACT].astype(jnp.float32)
    for k in range(1, shards):
        piece = partial_features[k * MAXACT : (k + 1) * MAXACT]
        feature_grad = feature_grad + shifted(piece, "seq", (shards,), (-k,)).astype(jnp.float32)
    every_gate = jnp.concatenate([f[:window] for f in every_factors], axis=0)
    every_up = jnp.concatenate([f[window : 2 * window] for f in every_factors], axis=0)
    every_hidden = jnp.concatenate([f[2 * window :] for f in every_factors], axis=0)
    normed_cols = jnp.concatenate([c[:window] for c in every_columns], axis=0)
    masked_cols = jnp.concatenate([c[window:] for c in every_columns], axis=0)
    gate_grad = contract_first(normed_cols, every_gate)
    up_grad = contract_first(normed_cols, every_up)
    down_grad = contract_first(every_hidden, masked_cols)
    feature_grad, gate_grad, up_grad, down_grad = lax.optimization_barrier(
        (feature_grad, gate_grad, up_grad, down_grad)
    )
    seq_sum = feature_grad.astype(jnp.bfloat16)
    for step in range(1, parts):
        feature_grad = feature_grad + shifted(seq_sum, "fsdp", (parts,), (step,)).astype(jnp.float32)
    _, pullback = jax.vjp(partial(normalize, norm_gain=norm_gain), source)
    slot_grad = pullback(feature_grad)[0].astype(jnp.bfloat16)
    own_columns = lax.dynamic_slice_in_dim(picker, place * own_rows, own_rows, 1)
    branch_grad = contract_first(own_columns, slot_grad).astype(jnp.bfloat16)
    return (branch_grad, gate_grad, up_grad, down_grad)


def solution(mesh):
    in_specs = (
        P(("rep", "seq"), None),
        P(("rep", "seq"), None),
        P(),
        P(None, ("seq", "fsdp")),
        P(None, ("seq", "fsdp")),
        P(("seq", "fsdp"), None),
        P(("rep", "seq")),
    )
    out_specs = (
        P(("rep", "seq", "fsdp"), None),
        P("rep", ("seq", "fsdp")),
        P("rep", ("seq", "fsdp")),
        P(("seq", "fsdp"), "rep"),
    )
    return jax.shard_map(local, mesh=mesh, in_specs=in_specs, out_specs=out_specs, check_vma=False)
```

```python
from functools import partial

import jax
import jax.numpy as jnp
from jax import lax
from jax.experimental import pallas as pl
from jax.experimental.pallas import tpu as pltpu
from jax.sharding import PartitionSpec as P

REC = 1
MAXACT = 8


EPSILON = 1e-05


def normalize(widened, norm_gain):
    factor = lax.rsqrt(jnp.mean(widened * widened, axis=-1, keepdims=True) + EPSILON)
    return widened * factor * norm_gain


def contract_first(left, right):
    return lax.dot_general(
        left, right, (((0,), (0,)), ((), ())), preferred_element_type=jnp.float32
    )


def contract_last(left, right):
    return lax.dot_general(
        left, right, (((1,), (1,)), ((), ())), preferred_element_type=jnp.float32
    )


def shifted(value, axes, sizes, steps):
    total = 1
    for size in sizes:
        total *= size
    pairs = []
    for index in range(total):
        coords, rest = [], index
        for size in reversed(sizes):
            coords.append(rest % size)
            rest //= size
        coords = coords[::-1]
        target, scale = 0, 1
        for axis in reversed(range(len(sizes))):
            target += ((coords[axis] + steps[axis]) % sizes[axis]) * scale
            scale *= sizes[axis]
        pairs.append((index, target))
    return lax.ppermute(value, axes, pairs)


def swapped(value, axis, size, distance):
    return lax.ppermute(value, axis, [(i, i ^ distance) for i in range(size)])


def power_of_two(size):
    return size & (size - 1) == 0


def gather_blocks(value, axis, size):
    if power_of_two(size):
        blocks, distance = [value], 1
        while distance < size:
            arrived = swapped(jnp.stack(blocks), axis, size, distance)
            blocks = blocks + [arrived[k] for k in range(distance)]
            distance *= 2
        return blocks, lambda k: ("xor", k)
    blocks = [value] + [shifted(value, axis, (size,), (k,)) for k in range(1, size)]
    return blocks, lambda k: ("shift", k)


def scatter_sum(pieces, axis, size):
    if power_of_two(size):
        held = {k: piece.astype(jnp.float32) for k, piece in enumerate(pieces)}
        distance = size // 2
        while distance >= 1:
            leaving = sorted(k for k in held if k & distance)
            arrived = swapped(
                jnp.stack([held[k] for k in leaving]).astype(jnp.bfloat16), axis, size, distance
            )
            for position, k in enumerate(leaving):
                held[k ^ distance] = held[k ^ distance] + arrived[position].astype(jnp.float32)
            held = {k: v for k, v in held.items() if not k & distance}
            distance //= 2
        return held[0]
    total = pieces[0].astype(jnp.float32)
    for k in range(1, size):
        total = total + shifted(pieces[k], axis, (size,), (-k,)).astype(jnp.float32)
    return total


def all_sum(value, axis, size):
    if power_of_two(size):
        total, distance = value, 1
        while distance < size:
            total = total + swapped(total.astype(jnp.bfloat16), axis, size, distance).astype(jnp.float32)
            distance *= 2
        return total
    total = value
    for k in range(1, size):
        total = total + shifted(value.astype(jnp.bfloat16), axis, (size,), (k,)).astype(jnp.float32)
    return total


def exchange_blocks(blocks, axis, size):
    index = lax.axis_index(axis)
    if power_of_two(size):
        stacked = jnp.stack(blocks)
        held = {(0, k): lax.dynamic_index_in_dim(stacked, index ^ k, 0, keepdims=False) for k in range(size)}
        distance = 1
        while distance < size:
            leaving = sorted(key for key in held if key[1] & distance)
            arrived = swapped(jnp.stack([held[key] for key in leaving]), axis, size, distance)
            held = {key: v for key, v in held.items() if not key[1] & distance}
            for position, (origin, target) in enumerate(leaving):
                held[(origin ^ distance, target ^ distance)] = arrived[position]
            distance *= 2
        return [held[(k, 0)] for k in range(size)]
    stacked = jnp.stack(blocks)
    out = [lax.dynamic_index_in_dim(stacked, index, 0, keepdims=False)]
    for k in range(1, size):
        outgoing = lax.dynamic_index_in_dim(stacked, (index + k) % size, 0, keepdims=False)
        out.append(shifted(outgoing, axis, (size,), (k,)))
    return out


def weight_pass_kernel(normed_ref, masked_ref, gate_w_ref, up_w_ref, down_w_ref,
                       gate_rows_ref, up_rows_ref, hidden_ref, features_ref):
    step = pl.program_id(0)
    normed = normed_ref[...]
    gate_w = gate_w_ref[...]
    up_w = up_w_ref[...]
    gate = jnp.dot(normed, gate_w, preferred_element_type=jnp.float32)
    up = jnp.dot(normed, up_w, preferred_element_type=jnp.float32)
    hidden_grad = contract_last(masked_ref[...], down_w_ref[...])
    sigmoid_gate = 1.0 / (1.0 + jnp.exp(-gate))
    swished = gate * sigmoid_gate
    gate_rows = (hidden_grad * up * sigmoid_gate * (1.0 + gate * (1.0 - sigmoid_gate))).astype(
        jnp.bfloat16
    )
    up_rows = (hidden_grad * swished).astype(jnp.bfloat16)
    hidden_ref[...] = (swished * up).astype(jnp.bfloat16)
    gate_rows_ref[...] = gate_rows
    up_rows_ref[...] = up_rows
    partial_features = contract_last(gate_rows, gate_w) + contract_last(up_rows, up_w)

    @pl.when(step == 0)
    def _():
        features_ref[...] = partial_features

    @pl.when(step > 0)
    def _():
        features_ref[...] += partial_features


def weight_pass(window_normed, window_masked, gate_weight, up_weight, down_weight):
    rows, features = window_normed.shape
    units = gate_weight.shape[1]
    chunk = next((size for size in (512, 256, 128) if units % size == 0), units)
    factor_shape = jax.ShapeDtypeStruct((rows, units), jnp.bfloat16)
    return pl.pallas_call(
        weight_pass_kernel,
        grid=(units // chunk,),
        in_specs=[
            pl.BlockSpec((rows, features), lambda j: (0, 0)),
            pl.BlockSpec((rows, features), lambda j: (0, 0)),
            pl.BlockSpec((features, chunk), lambda j: (0, j)),
            pl.BlockSpec((features, chunk), lambda j: (0, j)),
            pl.BlockSpec((chunk, features), lambda j: (j, 0)),
        ],
        out_specs=[
            pl.BlockSpec((rows, chunk), lambda j: (0, j)),
            pl.BlockSpec((rows, chunk), lambda j: (0, j)),
            pl.BlockSpec((rows, chunk), lambda j: (0, j)),
            pl.BlockSpec((rows, features), lambda j: (0, 0)),
        ],
        out_shape=[
            factor_shape,
            factor_shape,
            factor_shape,
            jax.ShapeDtypeStruct((rows, features), jnp.float32),
        ],
        compiler_params=pltpu.CompilerParams(vmem_limit_bytes=56 * 1024 * 1024),
        cost_estimate=pl.CostEstimate(
            flops=10 * rows * features * units,
            transcendentals=rows * units,
            bytes_accessed=6 * features * units + 4 * rows * features * 2,
        ),
    )(window_normed, window_masked, gate_weight, up_weight, down_weight)


def local(tokens, cotangent, norm_gain, gate_weight, up_weight, down_weight, depths):
    parts = lax.axis_size("fsdp")
    place = lax.axis_index("fsdp")
    replicas = lax.axis_size("rep")
    replica = lax.axis_index("rep")
    shards = lax.axis_size("seq")
    features = tokens.shape[1]
    feature_share = features // replicas
    rows_here = tokens.shape[0]
    own_rows = rows_here // parts
    active = depths > REC
    ordinal = jnp.cumsum(active.astype(jnp.int32)) - 1
    selector = (ordinal[None, :] == jnp.arange(MAXACT, dtype=jnp.int32)[:, None]) & active[None, :]
    picker = selector.astype(jnp.bfloat16)
    source = jnp.dot(picker, tokens, preferred_element_type=jnp.float32)
    send_masked = jnp.dot(picker, cotangent, preferred_element_type=jnp.float32).astype(jnp.bfloat16)
    send_normed = normalize(source, norm_gain).astype(jnp.bfloat16)
    packed = jnp.concatenate([send_normed, send_masked], axis=0)
    blocks = [packed] + [shifted(packed, "seq", (shards,), (k,)) for k in range(1, shards)]
    window_normed = jnp.concatenate([b[:MAXACT] for b in blocks], axis=0)
    window_masked = jnp.concatenate([b[MAXACT:] for b in blocks], axis=0)
    window = window_normed.shape[0]
    gate_rows, up_rows, hidden, partial_features = weight_pass(
        window_normed, window_masked, gate_weight, up_weight, down_weight
    )
    units = gate_rows.shape[1]
    factors = jnp.concatenate([gate_rows, up_rows, hidden], axis=1)

    def message(target):
        start = target * feature_share
        return jnp.concatenate(
            [
                factors,
                lax.dynamic_slice_in_dim(window_normed, start, feature_share, 1),
                lax.dynamic_slice_in_dim(window_masked, start, feature_share, 1),
            ],
            axis=1,
        )

    every_message = [message(replica)] + [
        shifted(message((replica + j) % replicas), "rep", (replicas,), (j,))
        for j in range(1, replicas)
    ]
    partial_features = partial_features.astype(jnp.bfloat16)
    feature_grad = partial_features[:MAXACT].astype(jnp.float32)
    for k in range(1, shards):
        piece = partial_features[k * MAXACT : (k + 1) * MAXACT]
        feature_grad = feature_grad + shifted(piece, "seq", (shards,), (-k,)).astype(jnp.float32)
    received = jnp.concatenate(every_message, axis=0)
    every_gate = received[:, :units]
    every_up = received[:, units : 2 * units]
    every_hidden = received[:, 2 * units : 3 * units]
    normed_cols = received[:, 3 * units : 3 * units + feature_share]
    masked_cols = received[:, 3 * units + feature_share :]
    gate_grad = contract_first(normed_cols, every_gate)
    up_grad = contract_first(normed_cols, every_up)
    down_grad = contract_first(every_hidden, masked_cols)
    feature_grad, gate_grad, up_grad, down_grad = lax.optimization_barrier(
        (feature_grad, gate_grad, up_grad, down_grad)
    )
    seq_sum = feature_grad.astype(jnp.bfloat16)
    for step in range(1, parts):
        feature_grad = feature_grad + shifted(seq_sum, "fsdp", (parts,), (step,)).astype(jnp.float32)
    _, pullback = jax.vjp(partial(normalize, norm_gain=norm_gain), source)
    slot_grad = pullback(feature_grad)[0].astype(jnp.bfloat16)
    own_columns = lax.dynamic_slice_in_dim(picker, place * own_rows, own_rows, 1)
    branch_grad = contract_first(own_columns, slot_grad).astype(jnp.bfloat16)
    return (branch_grad, gate_grad, up_grad, down_grad)


def solution(mesh):
    in_specs = (
        P(("rep", "seq"), None),
        P(("rep", "seq"), None),
        P(),
        P(None, ("seq", "fsdp")),
        P(None, ("seq", "fsdp")),
        P(("seq", "fsdp"), None),
        P(("rep", "seq")),
    )
    out_specs = (
        P(("rep", "seq", "fsdp"), None),
        P("rep", ("seq", "fsdp")),
        P("rep", ("seq", "fsdp")),
        P(("seq", "fsdp"), "rep"),
    )
    return jax.shard_map(local, mesh=mesh, in_specs=in_specs, out_specs=out_specs, check_vma=False)
```

```python
from functools import partial

import jax
import jax.numpy as jnp
from jax import lax
from jax.experimental import pallas as pl
from jax.experimental.pallas import tpu as pltpu
from jax.sharding import PartitionSpec as P

REC = 1
MAXACT = 8


EPSILON = 1e-05


def normalize(widened, norm_gain):
    factor = lax.rsqrt(jnp.mean(widened * widened, axis=-1, keepdims=True) + EPSILON)
    return widened * factor * norm_gain


def contract_first(left, right):
    return lax.dot_general(
        left, right, (((0,), (0,)), ((), ())), preferred_element_type=jnp.float32
    )


def contract_last(left, right):
    return lax.dot_general(
        left, right, (((1,), (1,)), ((), ())), preferred_element_type=jnp.float32
    )


def shifted(value, axes, sizes, steps):
    total = 1
    for size in sizes:
        total *= size
    pairs = []
    for index in range(total):
        coords, rest = [], index
        for size in reversed(sizes):
            coords.append(rest % size)
            rest //= size
        coords = coords[::-1]
        target, scale = 0, 1
        for axis in reversed(range(len(sizes))):
            target += ((coords[axis] + steps[axis]) % sizes[axis]) * scale
            scale *= sizes[axis]
        pairs.append((index, target))
    return lax.ppermute(value, axes, pairs)


def swapped(value, axis, size, distance):
    return lax.ppermute(value, axis, [(i, i ^ distance) for i in range(size)])


def power_of_two(size):
    return size & (size - 1) == 0


def gather_blocks(value, axis, size):
    if power_of_two(size):
        blocks, distance = [value], 1
        while distance < size:
            arrived = swapped(jnp.stack(blocks), axis, size, distance)
            blocks = blocks + [arrived[k] for k in range(distance)]
            distance *= 2
        return blocks, lambda k: ("xor", k)
    blocks = [value] + [shifted(value, axis, (size,), (k,)) for k in range(1, size)]
    return blocks, lambda k: ("shift", k)


def scatter_sum(pieces, axis, size):
    if power_of_two(size):
        held = {k: piece.astype(jnp.float32) for k, piece in enumerate(pieces)}
        distance = size // 2
        while distance >= 1:
            leaving = sorted(k for k in held if k & distance)
            arrived = swapped(
                jnp.stack([held[k] for k in leaving]).astype(jnp.bfloat16), axis, size, distance
            )
            for position, k in enumerate(leaving):
                held[k ^ distance] = held[k ^ distance] + arrived[position].astype(jnp.float32)
            held = {k: v for k, v in held.items() if not k & distance}
            distance //= 2
        return held[0]
    total = pieces[0].astype(jnp.float32)
    for k in range(1, size):
        total = total + shifted(pieces[k], axis, (size,), (-k,)).astype(jnp.float32)
    return total


def all_sum(value, axis, size):
    if power_of_two(size):
        total, distance = value, 1
        while distance < size:
            total = total + swapped(total.astype(jnp.bfloat16), axis, size, distance).astype(jnp.float32)
            distance *= 2
        return total
    total = value
    for k in range(1, size):
        total = total + shifted(value.astype(jnp.bfloat16), axis, (size,), (k,)).astype(jnp.float32)
    return total


def exchange_blocks(blocks, axis, size):
    index = lax.axis_index(axis)
    if power_of_two(size):
        stacked = jnp.stack(blocks)
        held = {(0, k): lax.dynamic_index_in_dim(stacked, index ^ k, 0, keepdims=False) for k in range(size)}
        distance = 1
        while distance < size:
            leaving = sorted(key for key in held if key[1] & distance)
            arrived = swapped(jnp.stack([held[key] for key in leaving]), axis, size, distance)
            held = {key: v for key, v in held.items() if not key[1] & distance}
            for position, (origin, target) in enumerate(leaving):
                held[(origin ^ distance, target ^ distance)] = arrived[position]
            distance *= 2
        return [held[(k, 0)] for k in range(size)]
    stacked = jnp.stack(blocks)
    out = [lax.dynamic_index_in_dim(stacked, index, 0, keepdims=False)]
    for k in range(1, size):
        outgoing = lax.dynamic_index_in_dim(stacked, (index + k) % size, 0, keepdims=False)
        out.append(shifted(outgoing, axis, (size,), (k,)))
    return out


def rep_exchange(factors, column_blocks, axis, size):
    index = lax.axis_index(axis)
    stacked = jnp.stack(column_blocks)
    if power_of_two(size):
        gathered = {0: factors}
        held = {(0, k): lax.dynamic_index_in_dim(stacked, index ^ k, 0, keepdims=False) for k in range(size)}
        distance = size // 2
        while distance >= 1:
            origins = sorted(gathered)
            arrived = swapped(jnp.stack([gathered[o] for o in origins]), axis, size, distance)
            for position, origin in enumerate(origins):
                gathered[origin ^ distance] = arrived[position]
            leaving = sorted(key for key in held if key[1] & distance)
            arrived = swapped(jnp.stack([held[key] for key in leaving]), axis, size, distance)
            held = {key: v for key, v in held.items() if not key[1] & distance}
            for position, (origin, target) in enumerate(leaving):
                held[(origin ^ distance, target ^ distance)] = arrived[position]
            distance //= 2
        return [gathered[o] for o in range(size)], [held[(o, 0)] for o in range(size)]
    every_factors = [factors]
    every_columns = [lax.dynamic_index_in_dim(stacked, index, 0, keepdims=False)]
    for k in range(1, size):
        every_factors.append(shifted(factors, axis, (size,), (k,)))
        outgoing = lax.dynamic_index_in_dim(stacked, (index + k) % size, 0, keepdims=False)
        every_columns.append(shifted(outgoing, axis, (size,), (k,)))
    return every_factors, every_columns


def weight_pass_kernel(normed_ref, masked_ref, gate_w_ref, up_w_ref, down_w_ref,
                       gate_rows_ref, up_rows_ref, hidden_ref, features_ref):
    step = pl.program_id(0)
    normed = normed_ref[...]
    gate_w = gate_w_ref[...]
    up_w = up_w_ref[...]
    gate = jnp.dot(normed, gate_w, preferred_element_type=jnp.float32)
    up = jnp.dot(normed, up_w, preferred_element_type=jnp.float32)
    hidden_grad = contract_last(masked_ref[...], down_w_ref[...])
    sigmoid_gate = 1.0 / (1.0 + jnp.exp(-gate))
    swished = gate * sigmoid_gate
    gate_rows = (hidden_grad * up * sigmoid_gate * (1.0 + gate * (1.0 - sigmoid_gate))).astype(
        jnp.bfloat16
    )
    up_rows = (hidden_grad * swished).astype(jnp.bfloat16)
    hidden_ref[...] = (swished * up).astype(jnp.bfloat16)
    gate_rows_ref[...] = gate_rows
    up_rows_ref[...] = up_rows
    partial_features = contract_last(gate_rows, gate_w) + contract_last(up_rows, up_w)

    @pl.when(step == 0)
    def _():
        features_ref[...] = partial_features

    @pl.when(step > 0)
    def _():
        features_ref[...] += partial_features


def weight_pass(window_normed, window_masked, gate_weight, up_weight, down_weight):
    rows, features = window_normed.shape
    units = gate_weight.shape[1]
    chunk = next((size for size in (512, 256, 128) if units % size == 0), units)
    factor_shape = jax.ShapeDtypeStruct((rows, units), jnp.bfloat16)
    return pl.pallas_call(
        weight_pass_kernel,
        grid=(units // chunk,),
        in_specs=[
            pl.BlockSpec((rows, features), lambda j: (0, 0)),
            pl.BlockSpec((rows, features), lambda j: (0, 0)),
            pl.BlockSpec((features, chunk), lambda j: (0, j)),
            pl.BlockSpec((features, chunk), lambda j: (0, j)),
            pl.BlockSpec((chunk, features), lambda j: (j, 0)),
        ],
        out_specs=[
            pl.BlockSpec((rows, chunk), lambda j: (0, j)),
            pl.BlockSpec((rows, chunk), lambda j: (0, j)),
            pl.BlockSpec((rows, chunk), lambda j: (0, j)),
            pl.BlockSpec((rows, features), lambda j: (0, 0)),
        ],
        out_shape=[
            factor_shape,
            factor_shape,
            factor_shape,
            jax.ShapeDtypeStruct((rows, features), jnp.float32),
        ],
        compiler_params=pltpu.CompilerParams(vmem_limit_bytes=56 * 1024 * 1024),
        cost_estimate=pl.CostEstimate(
            flops=10 * rows * features * units,
            transcendentals=rows * units,
            bytes_accessed=6 * features * units + 4 * rows * features * 2,
        ),
    )(window_normed, window_masked, gate_weight, up_weight, down_weight)


def local(tokens, cotangent, norm_gain, gate_weight, up_weight, down_weight, depths):
    parts = lax.axis_size("fsdp")
    place = lax.axis_index("fsdp")
    replicas = lax.axis_size("rep")
    replica = lax.axis_index("rep")
    shards = lax.axis_size("seq")
    features = tokens.shape[1]
    feature_share = features // replicas
    rows_here = tokens.shape[0]
    own_rows = rows_here // parts
    active = depths > REC
    ordinal = jnp.cumsum(active.astype(jnp.int32)) - 1
    selector = (ordinal[None, :] == jnp.arange(MAXACT, dtype=jnp.int32)[:, None]) & active[None, :]
    picker = selector.astype(jnp.bfloat16)
    source = jnp.dot(picker, tokens, preferred_element_type=jnp.float32)
    send_masked = jnp.dot(picker, cotangent, preferred_element_type=jnp.float32).astype(jnp.bfloat16)
    send_normed = normalize(source, norm_gain).astype(jnp.bfloat16)
    packed = jnp.concatenate([send_normed, send_masked], axis=0)
    blocks = [packed] + [shifted(packed, "seq", (shards,), (k,)) for k in range(1, shards)]
    window_normed = jnp.concatenate([b[:MAXACT] for b in blocks], axis=0)
    window_masked = jnp.concatenate([b[MAXACT:] for b in blocks], axis=0)
    window = window_normed.shape[0]
    gate_rows, up_rows, hidden, partial_features = weight_pass(
        window_normed, window_masked, gate_weight, up_weight, down_weight
    )
    columns = jnp.concatenate([window_normed, window_masked], axis=0)
    columns = columns.reshape(2 * window, replicas, feature_share)
    every_factors, every_columns = rep_exchange(
        jnp.concatenate([gate_rows, up_rows, hidden], axis=0),
        [columns[:, b] for b in range(replicas)],
        "rep",
        replicas,
    )
    partial_features = partial_features.astype(jnp.bfloat16)
    feature_grad = partial_features[:MAXACT].astype(jnp.float32)
    for k in range(1, shards):
        piece = partial_features[k * MAXACT : (k + 1) * MAXACT]
        feature_grad = feature_grad + shifted(piece, "seq", (shards,), (-k,)).astype(jnp.float32)
    every_gate = jnp.concatenate([f[:window] for f in every_factors], axis=0)
    every_up = jnp.concatenate([f[window : 2 * window] for f in every_factors], axis=0)
    every_hidden = jnp.concatenate([f[2 * window :] for f in every_factors], axis=0)
    normed_cols = jnp.concatenate([c[:window] for c in every_columns], axis=0)
    masked_cols = jnp.concatenate([c[window:] for c in every_columns], axis=0)
    gate_grad = contract_first(normed_cols, every_gate)
    up_grad = contract_first(normed_cols, every_up)
    down_grad = contract_first(every_hidden, masked_cols)
    feature_grad, gate_grad, up_grad, down_grad = lax.optimization_barrier(
        (feature_grad, gate_grad, up_grad, down_grad)
    )
    seq_sum = feature_grad.astype(jnp.bfloat16)
    for step in range(1, parts):
        feature_grad = feature_grad + shifted(seq_sum, "fsdp", (parts,), (step,)).astype(jnp.float32)
    _, pullback = jax.vjp(partial(normalize, norm_gain=norm_gain), source)
    slot_grad = pullback(feature_grad)[0].astype(jnp.bfloat16)
    own_columns = lax.dynamic_slice_in_dim(picker, place * own_rows, own_rows, 1)
    branch_grad = contract_first(own_columns, slot_grad).astype(jnp.bfloat16)
    return (branch_grad, gate_grad, up_grad, down_grad)


def solution(mesh):
    in_specs = (
        P(("rep", "seq"), None),
        P(("rep", "seq"), None),
        P(),
        P(None, ("seq", "fsdp")),
        P(None, ("seq", "fsdp")),
        P(("seq", "fsdp"), None),
        P(("rep", "seq")),
    )
    out_specs = (
        P(("rep", "seq", "fsdp"), None),
        P("rep", ("seq", "fsdp")),
        P("rep", ("seq", "fsdp")),
        P(("seq", "fsdp"), "rep"),
    )
    return jax.shard_map(local, mesh=mesh, in_specs=in_specs, out_specs=out_specs, check_vma=False)
```

```python
from functools import partial

import jax
import jax.numpy as jnp
from jax import lax
from jax.experimental import pallas as pl
from jax.experimental.pallas import tpu as pltpu
from jax.sharding import PartitionSpec as P

REC = 1
MAXACT = 8


EPSILON = 1e-05


def normalize(widened, norm_gain):
    factor = lax.rsqrt(jnp.mean(widened * widened, axis=-1, keepdims=True) + EPSILON)
    return widened * factor * norm_gain


def contract_first(left, right):
    return lax.dot_general(
        left, right, (((0,), (0,)), ((), ())), preferred_element_type=jnp.float32
    )


def contract_last(left, right):
    return lax.dot_general(
        left, right, (((1,), (1,)), ((), ())), preferred_element_type=jnp.float32
    )


def shifted(value, axes, sizes, steps):
    total = 1
    for size in sizes:
        total *= size
    pairs = []
    for index in range(total):
        coords, rest = [], index
        for size in reversed(sizes):
            coords.append(rest % size)
            rest //= size
        coords = coords[::-1]
        target, scale = 0, 1
        for axis in reversed(range(len(sizes))):
            target += ((coords[axis] + steps[axis]) % sizes[axis]) * scale
            scale *= sizes[axis]
        pairs.append((index, target))
    return lax.ppermute(value, axes, pairs)


def swapped(value, axis, size, distance):
    return lax.ppermute(value, axis, [(i, i ^ distance) for i in range(size)])


def power_of_two(size):
    return size & (size - 1) == 0


def gather_blocks(value, axis, size):
    if power_of_two(size):
        blocks, distance = [value], 1
        while distance < size:
            arrived = swapped(jnp.stack(blocks), axis, size, distance)
            blocks = blocks + [arrived[k] for k in range(distance)]
            distance *= 2
        return blocks, lambda k: ("xor", k)
    blocks = [value] + [shifted(value, axis, (size,), (k,)) for k in range(1, size)]
    return blocks, lambda k: ("shift", k)


def scatter_sum(pieces, axis, size):
    if power_of_two(size):
        held = {k: piece.astype(jnp.float32) for k, piece in enumerate(pieces)}
        distance = size // 2
        while distance >= 1:
            leaving = sorted(k for k in held if k & distance)
            arrived = swapped(
                jnp.stack([held[k] for k in leaving]).astype(jnp.bfloat16), axis, size, distance
            )
            for position, k in enumerate(leaving):
                held[k ^ distance] = held[k ^ distance] + arrived[position].astype(jnp.float32)
            held = {k: v for k, v in held.items() if not k & distance}
            distance //= 2
        return held[0]
    total = pieces[0].astype(jnp.float32)
    for k in range(1, size):
        total = total + shifted(pieces[k], axis, (size,), (-k,)).astype(jnp.float32)
    return total


def all_sum(value, axis, size):
    if power_of_two(size):
        total, distance = value, 1
        while distance < size:
            total = total + swapped(total.astype(jnp.bfloat16), axis, size, distance).astype(jnp.float32)
            distance *= 2
        return total
    total = value
    for k in range(1, size):
        total = total + shifted(value.astype(jnp.bfloat16), axis, (size,), (k,)).astype(jnp.float32)
    return total


def exchange_blocks(blocks, axis, size):
    index = lax.axis_index(axis)
    if power_of_two(size):
        stacked = jnp.stack(blocks)
        held = {(0, k): lax.dynamic_index_in_dim(stacked, index ^ k, 0, keepdims=False) for k in range(size)}
        distance = 1
        while distance < size:
            leaving = sorted(key for key in held if key[1] & distance)
            arrived = swapped(jnp.stack([held[key] for key in leaving]), axis, size, distance)
            held = {key: v for key, v in held.items() if not key[1] & distance}
            for position, (origin, target) in enumerate(leaving):
                held[(origin ^ distance, target ^ distance)] = arrived[position]
            distance *= 2
        return [held[(k, 0)] for k in range(size)]
    stacked = jnp.stack(blocks)
    out = [lax.dynamic_index_in_dim(stacked, index, 0, keepdims=False)]
    for k in range(1, size):
        outgoing = lax.dynamic_index_in_dim(stacked, (index + k) % size, 0, keepdims=False)
        out.append(shifted(outgoing, axis, (size,), (k,)))
    return out


def rep_exchange(factors, column_blocks, axis, size):
    index = lax.axis_index(axis)
    stacked = jnp.stack(column_blocks)
    if power_of_two(size):
        gathered = {0: factors}
        held = {(0, k): lax.dynamic_index_in_dim(stacked, index ^ k, 0, keepdims=False) for k in range(size)}
        distance = size // 2
        while distance >= 1:
            origins = sorted(gathered)
            arrived = swapped(jnp.stack([gathered[o] for o in origins]), axis, size, distance)
            for position, origin in enumerate(origins):
                gathered[origin ^ distance] = arrived[position]
            leaving = sorted(key for key in held if key[1] & distance)
            arrived = swapped(jnp.stack([held[key] for key in leaving]), axis, size, distance)
            held = {key: v for key, v in held.items() if not key[1] & distance}
            for position, (origin, target) in enumerate(leaving):
                held[(origin ^ distance, target ^ distance)] = arrived[position]
            distance //= 2
        return [gathered[o] for o in range(size)], [held[(o, 0)] for o in range(size)]
    every_factors = [factors]
    every_columns = [lax.dynamic_index_in_dim(stacked, index, 0, keepdims=False)]
    for k in range(1, size):
        every_factors.append(shifted(factors, axis, (size,), (k,)))
        outgoing = lax.dynamic_index_in_dim(stacked, (index + k) % size, 0, keepdims=False)
        every_columns.append(shifted(outgoing, axis, (size,), (k,)))
    return every_factors, every_columns


def weight_pass_kernel(normed_ref, masked_ref, gate_w_ref, up_w_ref, down_w_ref,
                       gate_rows_ref, up_rows_ref, hidden_ref, features_ref):
    step = pl.program_id(0)
    normed = normed_ref[...]
    gate_w = gate_w_ref[...]
    up_w = up_w_ref[...]
    gate = jnp.dot(normed, gate_w, preferred_element_type=jnp.float32)
    up = jnp.dot(normed, up_w, preferred_element_type=jnp.float32)
    hidden_grad = contract_last(masked_ref[...], down_w_ref[...])
    sigmoid_gate = 1.0 / (1.0 + jnp.exp(-gate))
    swished = gate * sigmoid_gate
    gate_rows = (hidden_grad * up * sigmoid_gate * (1.0 + gate * (1.0 - sigmoid_gate))).astype(
        jnp.bfloat16
    )
    up_rows = (hidden_grad * swished).astype(jnp.bfloat16)
    hidden_ref[...] = (swished * up).astype(jnp.bfloat16)
    gate_rows_ref[...] = gate_rows
    up_rows_ref[...] = up_rows
    partial_features = contract_last(gate_rows, gate_w) + contract_last(up_rows, up_w)

    @pl.when(step == 0)
    def _():
        features_ref[...] = partial_features

    @pl.when(step > 0)
    def _():
        features_ref[...] += partial_features


def weight_pass(window_normed, window_masked, gate_weight, up_weight, down_weight):
    rows, features = window_normed.shape
    units = gate_weight.shape[1]
    chunk = next((size for size in (512, 256, 128) if units % size == 0), units)
    factor_shape = jax.ShapeDtypeStruct((rows, units), jnp.bfloat16)
    return pl.pallas_call(
        weight_pass_kernel,
        grid=(units // chunk,),
        in_specs=[
            pl.BlockSpec((rows, features), lambda j: (0, 0)),
            pl.BlockSpec((rows, features), lambda j: (0, 0)),
            pl.BlockSpec((features, chunk), lambda j: (0, j)),
            pl.BlockSpec((features, chunk), lambda j: (0, j)),
            pl.BlockSpec((chunk, features), lambda j: (j, 0)),
        ],
        out_specs=[
            pl.BlockSpec((rows, chunk), lambda j: (0, j)),
            pl.BlockSpec((rows, chunk), lambda j: (0, j)),
            pl.BlockSpec((rows, chunk), lambda j: (0, j)),
            pl.BlockSpec((rows, features), lambda j: (0, 0)),
        ],
        out_shape=[
            factor_shape,
            factor_shape,
            factor_shape,
            jax.ShapeDtypeStruct((rows, features), jnp.float32),
        ],
        compiler_params=pltpu.CompilerParams(vmem_limit_bytes=56 * 1024 * 1024),
        cost_estimate=pl.CostEstimate(
            flops=10 * rows * features * units,
            transcendentals=rows * units,
            bytes_accessed=6 * features * units + 4 * rows * features * 2,
        ),
    )(window_normed, window_masked, gate_weight, up_weight, down_weight)


def grads_kernel(normed_t_ref, gate_ref, up_ref, hidden_t_ref, masked_ref,
                 gate_grad_ref, up_grad_ref, down_grad_ref):
    normed_t = normed_t_ref[...]
    gate_grad_ref[...] = jnp.dot(normed_t, gate_ref[...], preferred_element_type=jnp.float32)
    up_grad_ref[...] = jnp.dot(normed_t, up_ref[...], preferred_element_type=jnp.float32)
    down_grad_ref[...] = jnp.dot(hidden_t_ref[...], masked_ref[...], preferred_element_type=jnp.float32)


def weight_grads(normed_cols, every_gate, every_up, every_hidden, masked_cols):
    rows, share = normed_cols.shape
    units = every_gate.shape[1]
    steps = 4 if share % 32 == 0 and units % 32 == 0 else 1
    share_block, unit_block = share // steps, units // steps
    return pl.pallas_call(
        grads_kernel,
        grid=(steps,),
        in_specs=[
            pl.BlockSpec((share_block, rows), lambda i: (i, 0)),
            pl.BlockSpec((rows, units), lambda i: (0, 0)),
            pl.BlockSpec((rows, units), lambda i: (0, 0)),
            pl.BlockSpec((unit_block, rows), lambda i: (i, 0)),
            pl.BlockSpec((rows, share), lambda i: (0, 0)),
        ],
        out_specs=[
            pl.BlockSpec((share_block, units), lambda i: (i, 0)),
            pl.BlockSpec((share_block, units), lambda i: (i, 0)),
            pl.BlockSpec((unit_block, share), lambda i: (i, 0)),
        ],
        out_shape=[
            jax.ShapeDtypeStruct((share, units), jnp.float32),
            jax.ShapeDtypeStruct((share, units), jnp.float32),
            jax.ShapeDtypeStruct((units, share), jnp.float32),
        ],
        compiler_params=pltpu.CompilerParams(vmem_limit_bytes=48 * 1024 * 1024),
        cost_estimate=pl.CostEstimate(
            flops=6 * rows * share * units,
            transcendentals=0,
            bytes_accessed=12 * share * units + 2 * rows * (2 * share + 3 * units),
        ),
    )(normed_cols.T, every_gate, every_up, every_hidden.T, masked_cols)


def local(tokens, cotangent, norm_gain, gate_weight, up_weight, down_weight, depths):
    parts = lax.axis_size("fsdp")
    place = lax.axis_index("fsdp")
    replicas = lax.axis_size("rep")
    replica = lax.axis_index("rep")
    shards = lax.axis_size("seq")
    features = tokens.shape[1]
    feature_share = features // replicas
    rows_here = tokens.shape[0]
    own_rows = rows_here // parts
    active = depths > REC
    ordinal = jnp.cumsum(active.astype(jnp.int32)) - 1
    selector = (ordinal[None, :] == jnp.arange(MAXACT, dtype=jnp.int32)[:, None]) & active[None, :]
    picker = selector.astype(jnp.bfloat16)
    source = jnp.dot(picker, tokens, preferred_element_type=jnp.float32)
    send_masked = jnp.dot(picker, cotangent, preferred_element_type=jnp.float32).astype(jnp.bfloat16)
    send_normed = normalize(source, norm_gain).astype(jnp.bfloat16)
    packed = jnp.concatenate([send_normed, send_masked], axis=0)
    blocks = [packed] + [shifted(packed, "seq", (shards,), (k,)) for k in range(1, shards)]
    window_normed = jnp.concatenate([b[:MAXACT] for b in blocks], axis=0)
    window_masked = jnp.concatenate([b[MAXACT:] for b in blocks], axis=0)
    window = window_normed.shape[0]
    gate_rows, up_rows, hidden, partial_features = weight_pass(
        window_normed, window_masked, gate_weight, up_weight, down_weight
    )
    columns = jnp.concatenate([window_normed, window_masked], axis=0)
    columns = columns.reshape(2 * window, replicas, feature_share)
    every_factors, every_columns = rep_exchange(
        jnp.concatenate([gate_rows, up_rows, hidden], axis=0),
        [columns[:, b] for b in range(replicas)],
        "rep",
        replicas,
    )
    partial_features = partial_features.astype(jnp.bfloat16)
    feature_grad = partial_features[:MAXACT].astype(jnp.float32)
    for k in range(1, shards):
        piece = partial_features[k * MAXACT : (k + 1) * MAXACT]
        feature_grad = feature_grad + shifted(piece, "seq", (shards,), (-k,)).astype(jnp.float32)
    every_gate = jnp.concatenate([f[:window] for f in every_factors], axis=0)
    every_up = jnp.concatenate([f[window : 2 * window] for f in every_factors], axis=0)
    every_hidden = jnp.concatenate([f[2 * window :] for f in every_factors], axis=0)
    normed_cols = jnp.concatenate([c[:window] for c in every_columns], axis=0)
    masked_cols = jnp.concatenate([c[window:] for c in every_columns], axis=0)
    gate_grad, up_grad, down_grad = weight_grads(
        normed_cols, every_gate, every_up, every_hidden, masked_cols
    )
    feature_grad, gate_grad, up_grad, down_grad = lax.optimization_barrier(
        (feature_grad, gate_grad, up_grad, down_grad)
    )
    seq_sum = feature_grad.astype(jnp.bfloat16)
    for step in range(1, parts):
        feature_grad = feature_grad + shifted(seq_sum, "fsdp", (parts,), (step,)).astype(jnp.float32)
    _, pullback = jax.vjp(partial(normalize, norm_gain=norm_gain), source)
    slot_grad = pullback(feature_grad)[0].astype(jnp.bfloat16)
    own_columns = lax.dynamic_slice_in_dim(picker, place * own_rows, own_rows, 1)
    branch_grad = contract_first(own_columns, slot_grad).astype(jnp.bfloat16)
    return (branch_grad, gate_grad, up_grad, down_grad)


def solution(mesh):
    in_specs = (
        P(("rep", "seq"), None),
        P(("rep", "seq"), None),
        P(),
        P(None, ("seq", "fsdp")),
        P(None, ("seq", "fsdp")),
        P(("seq", "fsdp"), None),
        P(("rep", "seq")),
    )
    out_specs = (
        P(("rep", "seq", "fsdp"), None),
        P("rep", ("seq", "fsdp")),
        P("rep", ("seq", "fsdp")),
        P(("seq", "fsdp"), "rep"),
    )
    return jax.shard_map(local, mesh=mesh, in_specs=in_specs, out_specs=out_specs, check_vma=False)
```

```python
from functools import partial

import jax
import jax.numpy as jnp
from jax import lax
from jax.experimental import pallas as pl
from jax.experimental.pallas import tpu as pltpu
from jax.sharding import PartitionSpec as P

REC = 1
MAXACT = 8


EPSILON = 1e-05


def normalize(widened, norm_gain):
    factor = lax.rsqrt(jnp.mean(widened * widened, axis=-1, keepdims=True) + EPSILON)
    return widened * factor * norm_gain


def contract_first(left, right):
    return lax.dot_general(
        left, right, (((0,), (0,)), ((), ())), preferred_element_type=jnp.float32
    )


def contract_last(left, right):
    return lax.dot_general(
        left, right, (((1,), (1,)), ((), ())), preferred_element_type=jnp.float32
    )


def shifted(value, axes, sizes, steps):
    total = 1
    for size in sizes:
        total *= size
    pairs = []
    for index in range(total):
        coords, rest = [], index
        for size in reversed(sizes):
            coords.append(rest % size)
            rest //= size
        coords = coords[::-1]
        target, scale = 0, 1
        for axis in reversed(range(len(sizes))):
            target += ((coords[axis] + steps[axis]) % sizes[axis]) * scale
            scale *= sizes[axis]
        pairs.append((index, target))
    return lax.ppermute(value, axes, pairs)


def swapped(value, axis, size, distance):
    return lax.ppermute(value, axis, [(i, i ^ distance) for i in range(size)])


def power_of_two(size):
    return size & (size - 1) == 0


def gather_blocks(value, axis, size):
    if power_of_two(size):
        blocks, distance = [value], 1
        while distance < size:
            arrived = swapped(jnp.stack(blocks), axis, size, distance)
            blocks = blocks + [arrived[k] for k in range(distance)]
            distance *= 2
        return blocks, lambda k: ("xor", k)
    blocks = [value] + [shifted(value, axis, (size,), (k,)) for k in range(1, size)]
    return blocks, lambda k: ("shift", k)


def scatter_sum(pieces, axis, size):
    if power_of_two(size):
        held = {k: piece.astype(jnp.float32) for k, piece in enumerate(pieces)}
        distance = size // 2
        while distance >= 1:
            leaving = sorted(k for k in held if k & distance)
            arrived = swapped(
                jnp.stack([held[k] for k in leaving]).astype(jnp.bfloat16), axis, size, distance
            )
            for position, k in enumerate(leaving):
                held[k ^ distance] = held[k ^ distance] + arrived[position].astype(jnp.float32)
            held = {k: v for k, v in held.items() if not k & distance}
            distance //= 2
        return held[0]
    total = pieces[0].astype(jnp.float32)
    for k in range(1, size):
        total = total + shifted(pieces[k], axis, (size,), (-k,)).astype(jnp.float32)
    return total


def all_sum(value, axis, size):
    if power_of_two(size):
        total, distance = value, 1
        while distance < size:
            total = total + swapped(total.astype(jnp.bfloat16), axis, size, distance).astype(jnp.float32)
            distance *= 2
        return total
    total = value
    for k in range(1, size):
        total = total + shifted(value.astype(jnp.bfloat16), axis, (size,), (k,)).astype(jnp.float32)
    return total


def exchange_blocks(blocks, axis, size):
    index = lax.axis_index(axis)
    if power_of_two(size):
        stacked = jnp.stack(blocks)
        held = {(0, k): lax.dynamic_index_in_dim(stacked, index ^ k, 0, keepdims=False) for k in range(size)}
        distance = 1
        while distance < size:
            leaving = sorted(key for key in held if key[1] & distance)
            arrived = swapped(jnp.stack([held[key] for key in leaving]), axis, size, distance)
            held = {key: v for key, v in held.items() if not key[1] & distance}
            for position, (origin, target) in enumerate(leaving):
                held[(origin ^ distance, target ^ distance)] = arrived[position]
            distance *= 2
        return [held[(k, 0)] for k in range(size)]
    stacked = jnp.stack(blocks)
    out = [lax.dynamic_index_in_dim(stacked, index, 0, keepdims=False)]
    for k in range(1, size):
        outgoing = lax.dynamic_index_in_dim(stacked, (index + k) % size, 0, keepdims=False)
        out.append(shifted(outgoing, axis, (size,), (k,)))
    return out


def rep_exchange(factors, column_blocks, axis, size):
    index = lax.axis_index(axis)
    stacked = jnp.stack(column_blocks)
    if power_of_two(size):
        gathered = {0: factors}
        held = {(0, k): lax.dynamic_index_in_dim(stacked, index ^ k, 0, keepdims=False) for k in range(size)}
        distance = size // 2
        while distance >= 1:
            origins = sorted(gathered)
            arrived = swapped(jnp.stack([gathered[o] for o in origins]), axis, size, distance)
            for position, origin in enumerate(origins):
                gathered[origin ^ distance] = arrived[position]
            leaving = sorted(key for key in held if key[1] & distance)
            arrived = swapped(jnp.stack([held[key] for key in leaving]), axis, size, distance)
            held = {key: v for key, v in held.items() if not key[1] & distance}
            for position, (origin, target) in enumerate(leaving):
                held[(origin ^ distance, target ^ distance)] = arrived[position]
            distance //= 2
        return [gathered[o] for o in range(size)], [held[(o, 0)] for o in range(size)]
    every_factors = [factors]
    every_columns = [lax.dynamic_index_in_dim(stacked, index, 0, keepdims=False)]
    for k in range(1, size):
        every_factors.append(shifted(factors, axis, (size,), (k,)))
        outgoing = lax.dynamic_index_in_dim(stacked, (index + k) % size, 0, keepdims=False)
        every_columns.append(shifted(outgoing, axis, (size,), (k,)))
    return every_factors, every_columns


def weight_pass_kernel(normed_ref, masked_ref, gate_w_ref, up_w_ref, down_w_ref,
                       gate_rows_ref, up_rows_ref, hidden_ref, features_ref):
    step = pl.program_id(0)
    normed = normed_ref[...]
    gate_w = gate_w_ref[...]
    up_w = up_w_ref[...]
    gate = jnp.dot(normed, gate_w, preferred_element_type=jnp.float32)
    up = jnp.dot(normed, up_w, preferred_element_type=jnp.float32)
    hidden_grad = contract_last(masked_ref[...], down_w_ref[...])
    sigmoid_gate = 1.0 / (1.0 + jnp.exp(-gate))
    swished = gate * sigmoid_gate
    gate_rows = (hidden_grad * up * sigmoid_gate * (1.0 + gate * (1.0 - sigmoid_gate))).astype(
        jnp.bfloat16
    )
    up_rows = (hidden_grad * swished).astype(jnp.bfloat16)
    hidden_ref[...] = (swished * up).astype(jnp.bfloat16)
    gate_rows_ref[...] = gate_rows
    up_rows_ref[...] = up_rows
    partial_features = contract_last(gate_rows, gate_w) + contract_last(up_rows, up_w)

    @pl.when(step == 0)
    def _():
        features_ref[...] = partial_features

    @pl.when(step > 0)
    def _():
        features_ref[...] += partial_features


def weight_pass(window_normed, window_masked, gate_weight, up_weight, down_weight):
    rows, features = window_normed.shape
    units = gate_weight.shape[1]
    chunk = next((size for size in (512, 256, 128) if units % size == 0), units)
    factor_shape = jax.ShapeDtypeStruct((rows, units), jnp.bfloat16)
    return pl.pallas_call(
        weight_pass_kernel,
        grid=(units // chunk,),
        in_specs=[
            pl.BlockSpec((rows, features), lambda j: (0, 0)),
            pl.BlockSpec((rows, features), lambda j: (0, 0)),
            pl.BlockSpec((features, chunk), lambda j: (0, j)),
            pl.BlockSpec((features, chunk), lambda j: (0, j)),
            pl.BlockSpec((chunk, features), lambda j: (j, 0)),
        ],
        out_specs=[
            pl.BlockSpec((rows, chunk), lambda j: (0, j)),
            pl.BlockSpec((rows, chunk), lambda j: (0, j)),
            pl.BlockSpec((rows, chunk), lambda j: (0, j)),
            pl.BlockSpec((rows, features), lambda j: (0, 0)),
        ],
        out_shape=[
            factor_shape,
            factor_shape,
            factor_shape,
            jax.ShapeDtypeStruct((rows, features), jnp.float32),
        ],
        compiler_params=pltpu.CompilerParams(vmem_limit_bytes=56 * 1024 * 1024),
        cost_estimate=pl.CostEstimate(
            flops=10 * rows * features * units,
            transcendentals=rows * units,
            bytes_accessed=6 * features * units + 4 * rows * features * 2,
        ),
    )(window_normed, window_masked, gate_weight, up_weight, down_weight)


def grads_kernel(normed_ref, gate_ref, up_ref, hidden_ref, masked_ref,
                 gate_grad_ref, up_grad_ref, down_grad_ref):
    normed = normed_ref[...]
    gate_grad_ref[...] = contract_first(normed, gate_ref[...])
    up_grad_ref[...] = contract_first(normed, up_ref[...])
    down_grad_ref[...] = contract_first(hidden_ref[...], masked_ref[...])


def weight_grads(normed_cols, every_gate, every_up, every_hidden, masked_cols):
    rows, share = normed_cols.shape
    units = every_gate.shape[1]
    steps = 4 if share % 512 == 0 and units % 512 == 0 else 1
    share_block, unit_block = share // steps, units // steps
    return pl.pallas_call(
        grads_kernel,
        grid=(steps,),
        in_specs=[
            pl.BlockSpec((rows, share_block), lambda i: (0, i)),
            pl.BlockSpec((rows, units), lambda i: (0, 0)),
            pl.BlockSpec((rows, units), lambda i: (0, 0)),
            pl.BlockSpec((rows, unit_block), lambda i: (0, i)),
            pl.BlockSpec((rows, share), lambda i: (0, 0)),
        ],
        out_specs=[
            pl.BlockSpec((share_block, units), lambda i: (i, 0)),
            pl.BlockSpec((share_block, units), lambda i: (i, 0)),
            pl.BlockSpec((unit_block, share), lambda i: (i, 0)),
        ],
        out_shape=[
            jax.ShapeDtypeStruct((share, units), jnp.float32),
            jax.ShapeDtypeStruct((share, units), jnp.float32),
            jax.ShapeDtypeStruct((units, share), jnp.float32),
        ],
        compiler_params=pltpu.CompilerParams(vmem_limit_bytes=48 * 1024 * 1024),
        cost_estimate=pl.CostEstimate(
            flops=6 * rows * share * units,
            transcendentals=0,
            bytes_accessed=12 * share * units + 2 * rows * (2 * share + 3 * units),
        ),
    )(normed_cols, every_gate, every_up, every_hidden, masked_cols)


def local(tokens, cotangent, norm_gain, gate_weight, up_weight, down_weight, depths):
    parts = lax.axis_size("fsdp")
    place = lax.axis_index("fsdp")
    replicas = lax.axis_size("rep")
    replica = lax.axis_index("rep")
    shards = lax.axis_size("seq")
    features = tokens.shape[1]
    feature_share = features // replicas
    rows_here = tokens.shape[0]
    own_rows = rows_here // parts
    active = depths > REC
    ordinal = jnp.cumsum(active.astype(jnp.int32)) - 1
    selector = (ordinal[None, :] == jnp.arange(MAXACT, dtype=jnp.int32)[:, None]) & active[None, :]
    picker = selector.astype(jnp.bfloat16)
    source = jnp.dot(picker, tokens, preferred_element_type=jnp.float32)
    send_masked = jnp.dot(picker, cotangent, preferred_element_type=jnp.float32).astype(jnp.bfloat16)
    send_normed = normalize(source, norm_gain).astype(jnp.bfloat16)
    packed = jnp.concatenate([send_normed, send_masked], axis=0)
    blocks = [packed] + [shifted(packed, "seq", (shards,), (k,)) for k in range(1, shards)]
    window_normed = jnp.concatenate([b[:MAXACT] for b in blocks], axis=0)
    window_masked = jnp.concatenate([b[MAXACT:] for b in blocks], axis=0)
    window = window_normed.shape[0]
    gate_rows, up_rows, hidden, partial_features = weight_pass(
        window_normed, window_masked, gate_weight, up_weight, down_weight
    )
    columns = jnp.concatenate([window_normed, window_masked], axis=0)
    columns = columns.reshape(2 * window, replicas, feature_share)
    every_factors, every_columns = rep_exchange(
        jnp.concatenate([gate_rows, up_rows, hidden], axis=0),
        [columns[:, b] for b in range(replicas)],
        "rep",
        replicas,
    )
    partial_features = partial_features.astype(jnp.bfloat16)
    feature_grad = partial_features[:MAXACT].astype(jnp.float32)
    for k in range(1, shards):
        piece = partial_features[k * MAXACT : (k + 1) * MAXACT]
        feature_grad = feature_grad + shifted(piece, "seq", (shards,), (-k,)).astype(jnp.float32)
    every_gate = jnp.concatenate([f[:window] for f in every_factors], axis=0)
    every_up = jnp.concatenate([f[window : 2 * window] for f in every_factors], axis=0)
    every_hidden = jnp.concatenate([f[2 * window :] for f in every_factors], axis=0)
    normed_cols = jnp.concatenate([c[:window] for c in every_columns], axis=0)
    masked_cols = jnp.concatenate([c[window:] for c in every_columns], axis=0)
    gate_grad, up_grad, down_grad = weight_grads(
        normed_cols, every_gate, every_up, every_hidden, masked_cols
    )
    feature_grad, gate_grad, up_grad, down_grad = lax.optimization_barrier(
        (feature_grad, gate_grad, up_grad, down_grad)
    )
    seq_sum = feature_grad.astype(jnp.bfloat16)
    for step in range(1, parts):
        feature_grad = feature_grad + shifted(seq_sum, "fsdp", (parts,), (step,)).astype(jnp.float32)
    _, pullback = jax.vjp(partial(normalize, norm_gain=norm_gain), source)
    slot_grad = pullback(feature_grad)[0].astype(jnp.bfloat16)
    own_columns = lax.dynamic_slice_in_dim(picker, place * own_rows, own_rows, 1)
    branch_grad = contract_first(own_columns, slot_grad).astype(jnp.bfloat16)
    return (branch_grad, gate_grad, up_grad, down_grad)


def solution(mesh):
    in_specs = (
        P(("rep", "seq"), None),
        P(("rep", "seq"), None),
        P(),
        P(None, ("seq", "fsdp")),
        P(None, ("seq", "fsdp")),
        P(("seq", "fsdp"), None),
        P(("rep", "seq")),
    )
    out_specs = (
        P(("rep", "seq", "fsdp"), None),
        P("rep", ("seq", "fsdp")),
        P("rep", ("seq", "fsdp")),
        P(("seq", "fsdp"), "rep"),
    )
    return jax.shard_map(local, mesh=mesh, in_specs=in_specs, out_specs=out_specs, check_vma=False)
```

```python
from functools import partial

import jax
import jax.numpy as jnp
from jax import lax
from jax.experimental import pallas as pl
from jax.experimental.pallas import tpu as pltpu
from jax.sharding import PartitionSpec as P

REC = 1
MAXACT = 8


EPSILON = 1e-05


def normalize(widened, norm_gain):
    factor = lax.rsqrt(jnp.mean(widened * widened, axis=-1, keepdims=True) + EPSILON)
    return widened * factor * norm_gain


def contract_first(left, right):
    return lax.dot_general(
        left, right, (((0,), (0,)), ((), ())), preferred_element_type=jnp.float32
    )


def contract_last(left, right):
    return lax.dot_general(
        left, right, (((1,), (1,)), ((), ())), preferred_element_type=jnp.float32
    )


def shifted(value, axes, sizes, steps):
    total = 1
    for size in sizes:
        total *= size
    pairs = []
    for index in range(total):
        coords, rest = [], index
        for size in reversed(sizes):
            coords.append(rest % size)
            rest //= size
        coords = coords[::-1]
        target, scale = 0, 1
        for axis in reversed(range(len(sizes))):
            target += ((coords[axis] + steps[axis]) % sizes[axis]) * scale
            scale *= sizes[axis]
        pairs.append((index, target))
    return lax.ppermute(value, axes, pairs)


def swapped(value, axis, size, distance):
    return lax.ppermute(value, axis, [(i, i ^ distance) for i in range(size)])


def power_of_two(size):
    return size & (size - 1) == 0


def gather_blocks(value, axis, size):
    if power_of_two(size):
        blocks, distance = [value], 1
        while distance < size:
            arrived = swapped(jnp.stack(blocks), axis, size, distance)
            blocks = blocks + [arrived[k] for k in range(distance)]
            distance *= 2
        return blocks, lambda k: ("xor", k)
    blocks = [value] + [shifted(value, axis, (size,), (k,)) for k in range(1, size)]
    return blocks, lambda k: ("shift", k)


def scatter_sum(pieces, axis, size):
    if power_of_two(size):
        held = {k: piece.astype(jnp.float32) for k, piece in enumerate(pieces)}
        distance = size // 2
        while distance >= 1:
            leaving = sorted(k for k in held if k & distance)
            arrived = swapped(
                jnp.stack([held[k] for k in leaving]).astype(jnp.bfloat16), axis, size, distance
            )
            for position, k in enumerate(leaving):
                held[k ^ distance] = held[k ^ distance] + arrived[position].astype(jnp.float32)
            held = {k: v for k, v in held.items() if not k & distance}
            distance //= 2
        return held[0]
    total = pieces[0].astype(jnp.float32)
    for k in range(1, size):
        total = total + shifted(pieces[k], axis, (size,), (-k,)).astype(jnp.float32)
    return total


def all_sum(value, axis, size):
    if power_of_two(size):
        total, distance = value, 1
        while distance < size:
            total = total + swapped(total.astype(jnp.bfloat16), axis, size, distance).astype(jnp.float32)
            distance *= 2
        return total
    total = value
    for k in range(1, size):
        total = total + shifted(value.astype(jnp.bfloat16), axis, (size,), (k,)).astype(jnp.float32)
    return total


def exchange_blocks(blocks, axis, size):
    index = lax.axis_index(axis)
    if power_of_two(size):
        stacked = jnp.stack(blocks)
        held = {(0, k): lax.dynamic_index_in_dim(stacked, index ^ k, 0, keepdims=False) for k in range(size)}
        distance = 1
        while distance < size:
            leaving = sorted(key for key in held if key[1] & distance)
            arrived = swapped(jnp.stack([held[key] for key in leaving]), axis, size, distance)
            held = {key: v for key, v in held.items() if not key[1] & distance}
            for position, (origin, target) in enumerate(leaving):
                held[(origin ^ distance, target ^ distance)] = arrived[position]
            distance *= 2
        return [held[(k, 0)] for k in range(size)]
    stacked = jnp.stack(blocks)
    out = [lax.dynamic_index_in_dim(stacked, index, 0, keepdims=False)]
    for k in range(1, size):
        outgoing = lax.dynamic_index_in_dim(stacked, (index + k) % size, 0, keepdims=False)
        out.append(shifted(outgoing, axis, (size,), (k,)))
    return out


def rep_exchange(factors, column_blocks, axis, size):
    index = lax.axis_index(axis)
    stacked = jnp.stack(column_blocks)
    if power_of_two(size):
        gathered = {0: factors}
        held = {(0, k): lax.dynamic_index_in_dim(stacked, index ^ k, 0, keepdims=False) for k in range(size)}
        distance = size // 2
        while distance >= 1:
            origins = sorted(gathered)
            arrived = swapped(jnp.stack([gathered[o] for o in origins]), axis, size, distance)
            for position, origin in enumerate(origins):
                gathered[origin ^ distance] = arrived[position]
            leaving = sorted(key for key in held if key[1] & distance)
            arrived = swapped(jnp.stack([held[key] for key in leaving]), axis, size, distance)
            held = {key: v for key, v in held.items() if not key[1] & distance}
            for position, (origin, target) in enumerate(leaving):
                held[(origin ^ distance, target ^ distance)] = arrived[position]
            distance //= 2
        return [gathered[o] for o in range(size)], [held[(o, 0)] for o in range(size)]
    every_factors = [factors]
    every_columns = [lax.dynamic_index_in_dim(stacked, index, 0, keepdims=False)]
    for k in range(1, size):
        every_factors.append(shifted(factors, axis, (size,), (k,)))
        outgoing = lax.dynamic_index_in_dim(stacked, (index + k) % size, 0, keepdims=False)
        every_columns.append(shifted(outgoing, axis, (size,), (k,)))
    return every_factors, every_columns


def weight_pass_kernel(normed_ref, masked_ref, gate_w_ref, up_w_ref, down_w_ref,
                       gate_rows_ref, up_rows_ref, hidden_ref, features_ref):
    step = pl.program_id(0)
    normed = normed_ref[...]
    gate_w = gate_w_ref[...]
    up_w = up_w_ref[...]
    gate = jnp.dot(normed, gate_w, preferred_element_type=jnp.float32)
    up = jnp.dot(normed, up_w, preferred_element_type=jnp.float32)
    hidden_grad = contract_last(masked_ref[...], down_w_ref[...])
    sigmoid_gate = 1.0 / (1.0 + jnp.exp(-gate))
    swished = gate * sigmoid_gate
    gate_rows = (hidden_grad * up * sigmoid_gate * (1.0 + gate * (1.0 - sigmoid_gate))).astype(
        jnp.bfloat16
    )
    up_rows = (hidden_grad * swished).astype(jnp.bfloat16)
    hidden_ref[...] = (swished * up).astype(jnp.bfloat16)
    gate_rows_ref[...] = gate_rows
    up_rows_ref[...] = up_rows
    partial_features = contract_last(gate_rows, gate_w) + contract_last(up_rows, up_w)

    @pl.when(step == 0)
    def _():
        features_ref[...] = partial_features

    @pl.when(step > 0)
    def _():
        features_ref[...] += partial_features


def weight_pass(window_normed, window_masked, gate_weight, up_weight, down_weight):
    rows, features = window_normed.shape
    units = gate_weight.shape[1]
    chunk = next((size for size in (512, 256, 128) if units % size == 0), units)
    factor_shape = jax.ShapeDtypeStruct((rows, units), jnp.bfloat16)
    return pl.pallas_call(
        weight_pass_kernel,
        grid=(units // chunk,),
        in_specs=[
            pl.BlockSpec((rows, features), lambda j: (0, 0)),
            pl.BlockSpec((rows, features), lambda j: (0, 0)),
            pl.BlockSpec((features, chunk), lambda j: (0, j)),
            pl.BlockSpec((features, chunk), lambda j: (0, j)),
            pl.BlockSpec((chunk, features), lambda j: (j, 0)),
        ],
        out_specs=[
            pl.BlockSpec((rows, chunk), lambda j: (0, j)),
            pl.BlockSpec((rows, chunk), lambda j: (0, j)),
            pl.BlockSpec((rows, chunk), lambda j: (0, j)),
            pl.BlockSpec((rows, features), lambda j: (0, 0)),
        ],
        out_shape=[
            factor_shape,
            factor_shape,
            factor_shape,
            jax.ShapeDtypeStruct((rows, features), jnp.float32),
        ],
        compiler_params=pltpu.CompilerParams(vmem_limit_bytes=56 * 1024 * 1024),
        cost_estimate=pl.CostEstimate(
            flops=10 * rows * features * units,
            transcendentals=rows * units,
            bytes_accessed=6 * features * units + 4 * rows * features * 2,
        ),
    )(window_normed, window_masked, gate_weight, up_weight, down_weight)


def grads_kernel(normed_ref, gate_ref, up_ref, hidden_ref, masked_ref,
                 gate_grad_ref, up_grad_ref, down_grad_ref):
    normed = normed_ref[...]
    gate_grad_ref[...] = contract_first(normed, gate_ref[...])
    up_grad_ref[...] = contract_first(normed, up_ref[...])
    down_grad_ref[...] = contract_first(hidden_ref[...], masked_ref[...])


def weight_grads(normed_cols, every_gate, every_up, every_hidden, masked_cols):
    rows, share = normed_cols.shape
    units = every_gate.shape[1]
    steps = 4 if share % 512 == 0 and units % 512 == 0 else 1
    share_block, unit_block = share // steps, units // steps
    return pl.pallas_call(
        grads_kernel,
        grid=(steps,),
        in_specs=[
            pl.BlockSpec((rows, share_block), lambda i: (0, i)),
            pl.BlockSpec((rows, units), lambda i: (0, 0)),
            pl.BlockSpec((rows, units), lambda i: (0, 0)),
            pl.BlockSpec((rows, unit_block), lambda i: (0, i)),
            pl.BlockSpec((rows, share), lambda i: (0, 0)),
        ],
        out_specs=[
            pl.BlockSpec((share_block, units), lambda i: (i, 0)),
            pl.BlockSpec((share_block, units), lambda i: (i, 0)),
            pl.BlockSpec((unit_block, share), lambda i: (i, 0)),
        ],
        out_shape=[
            jax.ShapeDtypeStruct((share, units), jnp.float32),
            jax.ShapeDtypeStruct((share, units), jnp.float32),
            jax.ShapeDtypeStruct((units, share), jnp.float32),
        ],
        compiler_params=pltpu.CompilerParams(vmem_limit_bytes=48 * 1024 * 1024),
        cost_estimate=pl.CostEstimate(
            flops=6 * rows * share * units,
            transcendentals=0,
            bytes_accessed=12 * share * units + 2 * rows * (2 * share + 3 * units),
        ),
    )(normed_cols, every_gate, every_up, every_hidden, masked_cols)


def local(tokens, cotangent, norm_gain, gate_weight, up_weight, down_weight, depths):
    parts = lax.axis_size("fsdp")
    place = lax.axis_index("fsdp")
    replicas = lax.axis_size("rep")
    replica = lax.axis_index("rep")
    shards = lax.axis_size("seq")
    features = tokens.shape[1]
    feature_share = features // replicas
    rows_here = tokens.shape[0]
    own_rows = rows_here // parts
    active = depths > REC
    ordinal = jnp.cumsum(active.astype(jnp.int32)) - 1
    selector = (ordinal[None, :] == jnp.arange(MAXACT, dtype=jnp.int32)[:, None]) & active[None, :]
    picker = selector.astype(jnp.bfloat16)
    source = jnp.dot(picker, tokens, preferred_element_type=jnp.float32)
    send_masked = jnp.dot(picker, cotangent, preferred_element_type=jnp.float32).astype(jnp.bfloat16)
    send_normed = normalize(source, norm_gain).astype(jnp.bfloat16)
    packed = jnp.concatenate([send_normed, send_masked], axis=0)
    blocks = [packed] + [shifted(packed, "seq", (shards,), (k,)) for k in range(1, shards)]
    window_normed = jnp.concatenate([b[:MAXACT] for b in blocks], axis=0)
    window_masked = jnp.concatenate([b[MAXACT:] for b in blocks], axis=0)
    window = window_normed.shape[0]
    gate_rows, up_rows, hidden, partial_features = weight_pass(
        window_normed, window_masked, gate_weight, up_weight, down_weight
    )
    columns = jnp.concatenate([window_normed, window_masked], axis=0)
    columns = columns.reshape(2 * window, replicas, feature_share)
    every_factors, every_columns = rep_exchange(
        jnp.concatenate([gate_rows, up_rows, hidden], axis=0),
        [columns[:, b] for b in range(replicas)],
        "rep",
        replicas,
    )
    partial_features = partial_features.astype(jnp.bfloat16)
    feature_grad = partial_features[:MAXACT].astype(jnp.float32)
    for k in range(1, shards):
        piece = partial_features[k * MAXACT : (k + 1) * MAXACT]
        feature_grad = feature_grad + shifted(piece, "seq", (shards,), (-k,)).astype(jnp.float32)
    every_gate = jnp.concatenate([f[:window] for f in every_factors], axis=0)
    every_up = jnp.concatenate([f[window : 2 * window] for f in every_factors], axis=0)
    every_hidden = jnp.concatenate([f[2 * window :] for f in every_factors], axis=0)
    normed_cols = jnp.concatenate([c[:window] for c in every_columns], axis=0)
    masked_cols = jnp.concatenate([c[window:] for c in every_columns], axis=0)
    gate_grad, up_grad, down_grad = weight_grads(
        normed_cols, every_gate, every_up, every_hidden, masked_cols
    )
    seq_sum = feature_grad.astype(jnp.bfloat16)
    for step in range(1, parts):
        feature_grad = feature_grad + shifted(seq_sum, "fsdp", (parts,), (step,)).astype(jnp.float32)
    _, pullback = jax.vjp(partial(normalize, norm_gain=norm_gain), source)
    slot_grad = pullback(feature_grad)[0].astype(jnp.bfloat16)
    own_columns = lax.dynamic_slice_in_dim(picker, place * own_rows, own_rows, 1)
    branch_grad = contract_first(own_columns, slot_grad).astype(jnp.bfloat16)
    return (branch_grad, gate_grad, up_grad, down_grad)


def solution(mesh):
    in_specs = (
        P(("rep", "seq"), None),
        P(("rep", "seq"), None),
        P(),
        P(None, ("seq", "fsdp")),
        P(None, ("seq", "fsdp")),
        P(("seq", "fsdp"), None),
        P(("rep", "seq")),
    )
    out_specs = (
        P(("rep", "seq", "fsdp"), None),
        P("rep", ("seq", "fsdp")),
        P("rep", ("seq", "fsdp")),
        P(("seq", "fsdp"), "rep"),
    )
    return jax.shard_map(local, mesh=mesh, in_specs=in_specs, out_specs=out_specs, check_vma=False)
```

```python
from functools import partial

import jax
import jax.numpy as jnp
from jax import lax
from jax.experimental import pallas as pl
from jax.experimental.pallas import tpu as pltpu
from jax.sharding import PartitionSpec as P

REC = 1
MAXACT = 8


EPSILON = 1e-05


def normalize(widened, norm_gain):
    factor = lax.rsqrt(jnp.mean(widened * widened, axis=-1, keepdims=True) + EPSILON)
    return widened * factor * norm_gain


def contract_first(left, right):
    return lax.dot_general(
        left, right, (((0,), (0,)), ((), ())), preferred_element_type=jnp.float32
    )


def contract_last(left, right):
    return lax.dot_general(
        left, right, (((1,), (1,)), ((), ())), preferred_element_type=jnp.float32
    )


def shifted(value, axes, sizes, steps):
    total = 1
    for size in sizes:
        total *= size
    pairs = []
    for index in range(total):
        coords, rest = [], index
        for size in reversed(sizes):
            coords.append(rest % size)
            rest //= size
        coords = coords[::-1]
        target, scale = 0, 1
        for axis in reversed(range(len(sizes))):
            target += ((coords[axis] + steps[axis]) % sizes[axis]) * scale
            scale *= sizes[axis]
        pairs.append((index, target))
    return lax.ppermute(value, axes, pairs)


def swapped(value, axis, size, distance):
    return lax.ppermute(value, axis, [(i, i ^ distance) for i in range(size)])


def power_of_two(size):
    return size & (size - 1) == 0


def gather_blocks(value, axis, size):
    if power_of_two(size):
        blocks, distance = [value], 1
        while distance < size:
            arrived = swapped(jnp.stack(blocks), axis, size, distance)
            blocks = blocks + [arrived[k] for k in range(distance)]
            distance *= 2
        return blocks, lambda k: ("xor", k)
    blocks = [value] + [shifted(value, axis, (size,), (k,)) for k in range(1, size)]
    return blocks, lambda k: ("shift", k)


def scatter_sum(pieces, axis, size):
    if power_of_two(size):
        held = {k: piece.astype(jnp.float32) for k, piece in enumerate(pieces)}
        distance = size // 2
        while distance >= 1:
            leaving = sorted(k for k in held if k & distance)
            arrived = swapped(
                jnp.stack([held[k] for k in leaving]).astype(jnp.bfloat16), axis, size, distance
            )
            for position, k in enumerate(leaving):
                held[k ^ distance] = held[k ^ distance] + arrived[position].astype(jnp.float32)
            held = {k: v for k, v in held.items() if not k & distance}
            distance //= 2
        return held[0]
    total = pieces[0].astype(jnp.float32)
    for k in range(1, size):
        total = total + shifted(pieces[k], axis, (size,), (-k,)).astype(jnp.float32)
    return total


def all_sum(value, axis, size):
    if power_of_two(size):
        total, distance = value, 1
        while distance < size:
            total = total + swapped(total.astype(jnp.bfloat16), axis, size, distance).astype(jnp.float32)
            distance *= 2
        return total
    total = value
    for k in range(1, size):
        total = total + shifted(value.astype(jnp.bfloat16), axis, (size,), (k,)).astype(jnp.float32)
    return total


def exchange_blocks(blocks, axis, size):
    index = lax.axis_index(axis)
    if power_of_two(size):
        stacked = jnp.stack(blocks)
        held = {(0, k): lax.dynamic_index_in_dim(stacked, index ^ k, 0, keepdims=False) for k in range(size)}
        distance = 1
        while distance < size:
            leaving = sorted(key for key in held if key[1] & distance)
            arrived = swapped(jnp.stack([held[key] for key in leaving]), axis, size, distance)
            held = {key: v for key, v in held.items() if not key[1] & distance}
            for position, (origin, target) in enumerate(leaving):
                held[(origin ^ distance, target ^ distance)] = arrived[position]
            distance *= 2
        return [held[(k, 0)] for k in range(size)]
    stacked = jnp.stack(blocks)
    out = [lax.dynamic_index_in_dim(stacked, index, 0, keepdims=False)]
    for k in range(1, size):
        outgoing = lax.dynamic_index_in_dim(stacked, (index + k) % size, 0, keepdims=False)
        out.append(shifted(outgoing, axis, (size,), (k,)))
    return out


def rep_exchange(factors, column_blocks, axis, size):
    index = lax.axis_index(axis)
    stacked = jnp.stack(column_blocks) if column_blocks is not None else None
    if power_of_two(size):
        gathered = {0: factors}
        held = {}
        if stacked is not None:
            held = {(0, k): lax.dynamic_index_in_dim(stacked, index ^ k, 0, keepdims=False) for k in range(size)}
        distance = size // 2
        while distance >= 1:
            origins = sorted(gathered)
            arrived = swapped(jnp.stack([gathered[o] for o in origins]), axis, size, distance)
            for position, origin in enumerate(origins):
                gathered[origin ^ distance] = arrived[position]
            if held:
                leaving = sorted(key for key in held if key[1] & distance)
                arrived = swapped(jnp.stack([held[key] for key in leaving]), axis, size, distance)
                held = {key: v for key, v in held.items() if not key[1] & distance}
                for position, (origin, target) in enumerate(leaving):
                    held[(origin ^ distance, target ^ distance)] = arrived[position]
            distance //= 2
        every_columns = [held[(o, 0)] for o in range(size)] if held else None
        return [gathered[o] for o in range(size)], every_columns
    every_factors = [factors]
    every_columns = None
    if stacked is not None:
        every_columns = [lax.dynamic_index_in_dim(stacked, index, 0, keepdims=False)]
    for k in range(1, size):
        every_factors.append(shifted(factors, axis, (size,), (k,)))
        if stacked is not None:
            outgoing = lax.dynamic_index_in_dim(stacked, (index + k) % size, 0, keepdims=False)
            every_columns.append(shifted(outgoing, axis, (size,), (k,)))
    return every_factors, every_columns


def weight_pass_kernel(normed_ref, masked_ref, gate_w_ref, up_w_ref, down_w_ref,
                       gate_rows_ref, up_rows_ref, hidden_ref, features_ref):
    step = pl.program_id(0)
    normed = normed_ref[...]
    gate_w = gate_w_ref[...]
    up_w = up_w_ref[...]
    gate = jnp.dot(normed, gate_w, preferred_element_type=jnp.float32)
    up = jnp.dot(normed, up_w, preferred_element_type=jnp.float32)
    hidden_grad = contract_last(masked_ref[...], down_w_ref[...])
    sigmoid_gate = 1.0 / (1.0 + jnp.exp(-gate))
    swished = gate * sigmoid_gate
    gate_rows = (hidden_grad * up * sigmoid_gate * (1.0 + gate * (1.0 - sigmoid_gate))).astype(
        jnp.bfloat16
    )
    up_rows = (hidden_grad * swished).astype(jnp.bfloat16)
    hidden_ref[...] = (swished * up).astype(jnp.bfloat16)
    gate_rows_ref[...] = gate_rows
    up_rows_ref[...] = up_rows
    partial_features = contract_last(gate_rows, gate_w) + contract_last(up_rows, up_w)

    @pl.when(step == 0)
    def _():
        features_ref[...] = partial_features

    @pl.when(step > 0)
    def _():
        features_ref[...] += partial_features


def weight_pass(window_normed, window_masked, gate_weight, up_weight, down_weight, first, count, chunk):
    rows, features = window_normed.shape
    units = count * chunk
    factor_shape = jax.ShapeDtypeStruct((rows, units), jnp.bfloat16)
    return pl.pallas_call(
        weight_pass_kernel,
        grid=(count,),
        in_specs=[
            pl.BlockSpec((rows, features), lambda j: (0, 0)),
            pl.BlockSpec((rows, features), lambda j: (0, 0)),
            pl.BlockSpec((features, chunk), lambda j: (0, j + first)),
            pl.BlockSpec((features, chunk), lambda j: (0, j + first)),
            pl.BlockSpec((chunk, features), lambda j: (j + first, 0)),
        ],
        out_specs=[
            pl.BlockSpec((rows, chunk), lambda j: (0, j)),
            pl.BlockSpec((rows, chunk), lambda j: (0, j)),
            pl.BlockSpec((rows, chunk), lambda j: (0, j)),
            pl.BlockSpec((rows, features), lambda j: (0, 0)),
        ],
        out_shape=[
            factor_shape,
            factor_shape,
            factor_shape,
            jax.ShapeDtypeStruct((rows, features), jnp.float32),
        ],
        compiler_params=pltpu.CompilerParams(vmem_limit_bytes=56 * 1024 * 1024),
        cost_estimate=pl.CostEstimate(
            flops=10 * rows * features * units,
            transcendentals=rows * units,
            bytes_accessed=6 * features * units + 4 * rows * features * 2,
        ),
    )(window_normed, window_masked, gate_weight, up_weight, down_weight)


def grads_kernel(normed_ref, gate_ref, up_ref, hidden_ref, masked_ref,
                 gate_grad_ref, up_grad_ref, down_grad_ref):
    normed = normed_ref[...]
    gate_grad_ref[...] = contract_first(normed, gate_ref[...])
    up_grad_ref[...] = contract_first(normed, up_ref[...])
    down_grad_ref[...] = contract_first(hidden_ref[...], masked_ref[...])


def weight_grads(normed_cols, every_gate, every_up, every_hidden, masked_cols):
    rows, share = normed_cols.shape
    units = every_gate.shape[1]
    steps = 4 if share % 512 == 0 and units % 512 == 0 else 1
    share_block, unit_block = share // steps, units // steps
    return pl.pallas_call(
        grads_kernel,
        grid=(steps,),
        in_specs=[
            pl.BlockSpec((rows, share_block), lambda i: (0, i)),
            pl.BlockSpec((rows, units), lambda i: (0, 0)),
            pl.BlockSpec((rows, units), lambda i: (0, 0)),
            pl.BlockSpec((rows, unit_block), lambda i: (0, i)),
            pl.BlockSpec((rows, share), lambda i: (0, 0)),
        ],
        out_specs=[
            pl.BlockSpec((share_block, units), lambda i: (i, 0)),
            pl.BlockSpec((share_block, units), lambda i: (i, 0)),
            pl.BlockSpec((unit_block, share), lambda i: (i, 0)),
        ],
        out_shape=[
            jax.ShapeDtypeStruct((share, units), jnp.float32),
            jax.ShapeDtypeStruct((share, units), jnp.float32),
            jax.ShapeDtypeStruct((units, share), jnp.float32),
        ],
        compiler_params=pltpu.CompilerParams(vmem_limit_bytes=48 * 1024 * 1024),
        cost_estimate=pl.CostEstimate(
            flops=6 * rows * share * units,
            transcendentals=0,
            bytes_accessed=12 * share * units + 2 * rows * (2 * share + 3 * units),
        ),
    )(normed_cols, every_gate, every_up, every_hidden, masked_cols)


def local(tokens, cotangent, norm_gain, gate_weight, up_weight, down_weight, depths):
    parts = lax.axis_size("fsdp")
    place = lax.axis_index("fsdp")
    replicas = lax.axis_size("rep")
    replica = lax.axis_index("rep")
    shards = lax.axis_size("seq")
    features = tokens.shape[1]
    feature_share = features // replicas
    rows_here = tokens.shape[0]
    own_rows = rows_here // parts
    active = depths > REC
    ordinal = jnp.cumsum(active.astype(jnp.int32)) - 1
    selector = (ordinal[None, :] == jnp.arange(MAXACT, dtype=jnp.int32)[:, None]) & active[None, :]
    picker = selector.astype(jnp.bfloat16)
    source = jnp.dot(picker, tokens, preferred_element_type=jnp.float32)
    send_masked = jnp.dot(picker, cotangent, preferred_element_type=jnp.float32).astype(jnp.bfloat16)
    send_normed = normalize(source, norm_gain).astype(jnp.bfloat16)
    packed = jnp.concatenate([send_normed, send_masked], axis=0)
    blocks = [packed] + [shifted(packed, "seq", (shards,), (k,)) for k in range(1, shards)]
    window_normed = jnp.concatenate([b[:MAXACT] for b in blocks], axis=0)
    window_masked = jnp.concatenate([b[MAXACT:] for b in blocks], axis=0)
    window = window_normed.shape[0]
    units = gate_weight.shape[1]
    chunk = next((size for size in (512, 256, 128) if units % size == 0), units)
    chunks = units // chunk
    leading = chunks * 2 // 3
    calls = [(0, leading), (leading, chunks - leading)] if leading else [(0, chunks)]
    columns = jnp.concatenate([window_normed, window_masked], axis=0)
    columns = columns.reshape(2 * window, replicas, feature_share)
    column_blocks = [columns[:, b] for b in range(replicas)]
    factor_parts, feature_parts, every_columns = [], [], None
    for first, count in calls:
        gate_rows, up_rows, hidden, features_part = weight_pass(
            window_normed, window_masked, gate_weight, up_weight, down_weight, first, count, chunk
        )
        feature_parts.append(features_part)
        every_part, columns_now = rep_exchange(
            jnp.concatenate([gate_rows, up_rows, hidden], axis=0),
            column_blocks if every_columns is None else None,
            "rep",
            replicas,
        )
        every_columns = columns_now if every_columns is None else every_columns
        factor_parts.append(every_part)
    partial_features = sum(feature_parts[1:], feature_parts[0])
    partial_features = partial_features.astype(jnp.bfloat16)
    feature_grad = partial_features[:MAXACT].astype(jnp.float32)
    for k in range(1, shards):
        piece = partial_features[k * MAXACT : (k + 1) * MAXACT]
        feature_grad = feature_grad + shifted(piece, "seq", (shards,), (-k,)).astype(jnp.float32)
    every_factors = [
        jnp.concatenate([part[o] for part in factor_parts], axis=1) for o in range(replicas)
    ]
    every_gate = jnp.concatenate([f[:window] for f in every_factors], axis=0)
    every_up = jnp.concatenate([f[window : 2 * window] for f in every_factors], axis=0)
    every_hidden = jnp.concatenate([f[2 * window :] for f in every_factors], axis=0)
    normed_cols = jnp.concatenate([c[:window] for c in every_columns], axis=0)
    masked_cols = jnp.concatenate([c[window:] for c in every_columns], axis=0)
    gate_grad, up_grad, down_grad = weight_grads(
        normed_cols, every_gate, every_up, every_hidden, masked_cols
    )
    seq_sum = feature_grad.astype(jnp.bfloat16)
    for step in range(1, parts):
        feature_grad = feature_grad + shifted(seq_sum, "fsdp", (parts,), (step,)).astype(jnp.float32)
    _, pullback = jax.vjp(partial(normalize, norm_gain=norm_gain), source)
    slot_grad = pullback(feature_grad)[0].astype(jnp.bfloat16)
    own_columns = lax.dynamic_slice_in_dim(picker, place * own_rows, own_rows, 1)
    branch_grad = contract_first(own_columns, slot_grad).astype(jnp.bfloat16)
    return (branch_grad, gate_grad, up_grad, down_grad)


def solution(mesh):
    in_specs = (
        P(("rep", "seq"), None),
        P(("rep", "seq"), None),
        P(),
        P(None, ("seq", "fsdp")),
        P(None, ("seq", "fsdp")),
        P(("seq", "fsdp"), None),
        P(("rep", "seq")),
    )
    out_specs = (
        P(("rep", "seq", "fsdp"), None),
        P("rep", ("seq", "fsdp")),
        P("rep", ("seq", "fsdp")),
        P(("seq", "fsdp"), "rep"),
    )
    return jax.shard_map(local, mesh=mesh, in_specs=in_specs, out_specs=out_specs, check_vma=False)
```

```python
from functools import partial

import jax
import jax.numpy as jnp
from jax import lax
from jax.experimental import pallas as pl
from jax.experimental.pallas import tpu as pltpu
from jax.sharding import PartitionSpec as P

REC = 1
MAXACT = 8


EPSILON = 1e-05


def normalize(widened, norm_gain):
    factor = lax.rsqrt(jnp.mean(widened * widened, axis=-1, keepdims=True) + EPSILON)
    return widened * factor * norm_gain


def contract_first(left, right):
    return lax.dot_general(
        left, right, (((0,), (0,)), ((), ())), preferred_element_type=jnp.float32
    )


def contract_last(left, right):
    return lax.dot_general(
        left, right, (((1,), (1,)), ((), ())), preferred_element_type=jnp.float32
    )


def shifted(value, axes, sizes, steps):
    total = 1
    for size in sizes:
        total *= size
    pairs = []
    for index in range(total):
        coords, rest = [], index
        for size in reversed(sizes):
            coords.append(rest % size)
            rest //= size
        coords = coords[::-1]
        target, scale = 0, 1
        for axis in reversed(range(len(sizes))):
            target += ((coords[axis] + steps[axis]) % sizes[axis]) * scale
            scale *= sizes[axis]
        pairs.append((index, target))
    return lax.ppermute(value, axes, pairs)


def swapped(value, axis, size, distance):
    return lax.ppermute(value, axis, [(i, i ^ distance) for i in range(size)])


def power_of_two(size):
    return size & (size - 1) == 0


def gather_blocks(value, axis, size):
    if power_of_two(size):
        blocks, distance = [value], 1
        while distance < size:
            arrived = swapped(jnp.stack(blocks), axis, size, distance)
            blocks = blocks + [arrived[k] for k in range(distance)]
            distance *= 2
        return blocks, lambda k: ("xor", k)
    blocks = [value] + [shifted(value, axis, (size,), (k,)) for k in range(1, size)]
    return blocks, lambda k: ("shift", k)


def scatter_sum(pieces, axis, size):
    if power_of_two(size):
        held = {k: piece.astype(jnp.float32) for k, piece in enumerate(pieces)}
        distance = size // 2
        while distance >= 1:
            leaving = sorted(k for k in held if k & distance)
            arrived = swapped(
                jnp.stack([held[k] for k in leaving]).astype(jnp.bfloat16), axis, size, distance
            )
            for position, k in enumerate(leaving):
                held[k ^ distance] = held[k ^ distance] + arrived[position].astype(jnp.float32)
            held = {k: v for k, v in held.items() if not k & distance}
            distance //= 2
        return held[0]
    total = pieces[0].astype(jnp.float32)
    for k in range(1, size):
        total = total + shifted(pieces[k], axis, (size,), (-k,)).astype(jnp.float32)
    return total


def all_sum(value, axis, size):
    if power_of_two(size):
        total, distance = value, 1
        while distance < size:
            total = total + swapped(total.astype(jnp.bfloat16), axis, size, distance).astype(jnp.float32)
            distance *= 2
        return total
    total = value
    for k in range(1, size):
        total = total + shifted(value.astype(jnp.bfloat16), axis, (size,), (k,)).astype(jnp.float32)
    return total


def exchange_blocks(blocks, axis, size):
    index = lax.axis_index(axis)
    if power_of_two(size):
        stacked = jnp.stack(blocks)
        held = {(0, k): lax.dynamic_index_in_dim(stacked, index ^ k, 0, keepdims=False) for k in range(size)}
        distance = 1
        while distance < size:
            leaving = sorted(key for key in held if key[1] & distance)
            arrived = swapped(jnp.stack([held[key] for key in leaving]), axis, size, distance)
            held = {key: v for key, v in held.items() if not key[1] & distance}
            for position, (origin, target) in enumerate(leaving):
                held[(origin ^ distance, target ^ distance)] = arrived[position]
            distance *= 2
        return [held[(k, 0)] for k in range(size)]
    stacked = jnp.stack(blocks)
    out = [lax.dynamic_index_in_dim(stacked, index, 0, keepdims=False)]
    for k in range(1, size):
        outgoing = lax.dynamic_index_in_dim(stacked, (index + k) % size, 0, keepdims=False)
        out.append(shifted(outgoing, axis, (size,), (k,)))
    return out


def rep_exchange(factors, column_blocks, axis, size):
    index = lax.axis_index(axis)
    stacked = jnp.stack(column_blocks)
    if power_of_two(size):
        gathered = {0: factors}
        held = {(0, k): lax.dynamic_index_in_dim(stacked, index ^ k, 0, keepdims=False) for k in range(size)}
        distance = size // 2
        while distance >= 1:
            origins = sorted(gathered)
            arrived = swapped(jnp.stack([gathered[o] for o in origins]), axis, size, distance)
            for position, origin in enumerate(origins):
                gathered[origin ^ distance] = arrived[position]
            leaving = sorted(key for key in held if key[1] & distance)
            arrived = swapped(jnp.stack([held[key] for key in leaving]), axis, size, distance)
            held = {key: v for key, v in held.items() if not key[1] & distance}
            for position, (origin, target) in enumerate(leaving):
                held[(origin ^ distance, target ^ distance)] = arrived[position]
            distance //= 2
        return [gathered[o] for o in range(size)], [held[(o, 0)] for o in range(size)]
    every_factors = [factors]
    every_columns = [lax.dynamic_index_in_dim(stacked, index, 0, keepdims=False)]
    for k in range(1, size):
        every_factors.append(shifted(factors, axis, (size,), (k,)))
        outgoing = lax.dynamic_index_in_dim(stacked, (index + k) % size, 0, keepdims=False)
        every_columns.append(shifted(outgoing, axis, (size,), (k,)))
    return every_factors, every_columns


def weight_pass_kernel(normed_ref, masked_ref, gate_w_ref, up_w_ref, down_w_ref,
                       gate_rows_ref, up_rows_ref, hidden_ref, features_ref):
    step = pl.program_id(0)
    normed = normed_ref[...]
    gate_w = gate_w_ref[...]
    up_w = up_w_ref[...]
    gate = jnp.dot(normed, gate_w, preferred_element_type=jnp.float32)
    up = jnp.dot(normed, up_w, preferred_element_type=jnp.float32)
    hidden_grad = contract_last(masked_ref[...], down_w_ref[...])
    sigmoid_gate = 1.0 / (1.0 + jnp.exp(-gate))
    swished = gate * sigmoid_gate
    gate_rows = (hidden_grad * up * sigmoid_gate * (1.0 + gate * (1.0 - sigmoid_gate))).astype(
        jnp.bfloat16
    )
    up_rows = (hidden_grad * swished).astype(jnp.bfloat16)
    hidden_ref[...] = (swished * up).astype(jnp.bfloat16)
    gate_rows_ref[...] = gate_rows
    up_rows_ref[...] = up_rows
    partial_features = contract_last(gate_rows, gate_w) + contract_last(up_rows, up_w)

    @pl.when(step == 0)
    def _():
        features_ref[...] = partial_features

    @pl.when(step > 0)
    def _():
        features_ref[...] += partial_features


def weight_pass(window_normed, window_masked, gate_weight, up_weight, down_weight):
    rows, features = window_normed.shape
    units = gate_weight.shape[1]
    chunk = next((size for size in (512, 256, 128) if units % size == 0), units)
    factor_shape = jax.ShapeDtypeStruct((rows, units), jnp.bfloat16)
    return pl.pallas_call(
        weight_pass_kernel,
        grid=(units // chunk,),
        in_specs=[
            pl.BlockSpec((rows, features), lambda j: (0, 0)),
            pl.BlockSpec((rows, features), lambda j: (0, 0)),
            pl.BlockSpec((features, chunk), lambda j: (0, j)),
            pl.BlockSpec((features, chunk), lambda j: (0, j)),
            pl.BlockSpec((chunk, features), lambda j: (j, 0)),
        ],
        out_specs=[
            pl.BlockSpec((rows, chunk), lambda j: (0, j)),
            pl.BlockSpec((rows, chunk), lambda j: (0, j)),
            pl.BlockSpec((rows, chunk), lambda j: (0, j)),
            pl.BlockSpec((rows, features), lambda j: (0, 0)),
        ],
        out_shape=[
            factor_shape,
            factor_shape,
            factor_shape,
            jax.ShapeDtypeStruct((rows, features), jnp.float32),
        ],
        compiler_params=pltpu.CompilerParams(vmem_limit_bytes=56 * 1024 * 1024),
        cost_estimate=pl.CostEstimate(
            flops=10 * rows * features * units,
            transcendentals=rows * units,
            bytes_accessed=6 * features * units + 4 * rows * features * 2,
        ),
    )(window_normed, window_masked, gate_weight, up_weight, down_weight)


def grads_kernel(normed_ref, gate_ref, up_ref, hidden_ref, masked_ref,
                 gate_grad_ref, up_grad_ref, down_grad_ref):
    normed = normed_ref[...]
    gate_grad_ref[...] = contract_first(normed, gate_ref[...])
    up_grad_ref[...] = contract_first(normed, up_ref[...])
    down_grad_ref[...] = contract_first(hidden_ref[...], masked_ref[...])


def weight_grads(normed_cols, every_gate, every_up, every_hidden, masked_cols):
    rows, share = normed_cols.shape
    units = every_gate.shape[1]
    steps = 4 if share % 512 == 0 and units % 512 == 0 else 1
    share_block, unit_block = share // steps, units // steps
    return pl.pallas_call(
        grads_kernel,
        grid=(steps,),
        in_specs=[
            pl.BlockSpec((rows, share_block), lambda i: (0, i)),
            pl.BlockSpec((rows, units), lambda i: (0, 0)),
            pl.BlockSpec((rows, units), lambda i: (0, 0)),
            pl.BlockSpec((rows, unit_block), lambda i: (0, i)),
            pl.BlockSpec((rows, share), lambda i: (0, 0)),
        ],
        out_specs=[
            pl.BlockSpec((share_block, units), lambda i: (i, 0)),
            pl.BlockSpec((share_block, units), lambda i: (i, 0)),
            pl.BlockSpec((unit_block, share), lambda i: (i, 0)),
        ],
        out_shape=[
            jax.ShapeDtypeStruct((share, units), jnp.float32),
            jax.ShapeDtypeStruct((share, units), jnp.float32),
            jax.ShapeDtypeStruct((units, share), jnp.float32),
        ],
        compiler_params=pltpu.CompilerParams(vmem_limit_bytes=48 * 1024 * 1024),
        cost_estimate=pl.CostEstimate(
            flops=6 * rows * share * units,
            transcendentals=0,
            bytes_accessed=12 * share * units + 2 * rows * (2 * share + 3 * units),
        ),
    )(normed_cols, every_gate, every_up, every_hidden, masked_cols)


def local(tokens, cotangent, norm_gain, gate_weight, up_weight, down_weight, depths):
    parts = lax.axis_size("fsdp")
    place = lax.axis_index("fsdp")
    replicas = lax.axis_size("rep")
    replica = lax.axis_index("rep")
    shards = lax.axis_size("seq")
    features = tokens.shape[1]
    feature_share = features // replicas
    rows_here = tokens.shape[0]
    own_rows = rows_here // parts
    active = depths > REC
    ordinal = jnp.cumsum(active.astype(jnp.int32)) - 1
    selector = (ordinal[None, :] == jnp.arange(MAXACT, dtype=jnp.int32)[:, None]) & active[None, :]
    picker = selector.astype(jnp.bfloat16)
    source = jnp.dot(picker, tokens, preferred_element_type=jnp.float32)
    send_masked = jnp.dot(picker, cotangent, preferred_element_type=jnp.float32).astype(jnp.bfloat16)
    send_normed = normalize(source, norm_gain).astype(jnp.bfloat16)
    if parts % 2 == 0:
        carries_normed = place % 2 == 0
        mine = jnp.where(carries_normed, send_normed, send_masked)
        blocks = [mine] + [shifted(mine, "seq", (shards,), (k,)) for k in range(1, shards)]
        gathered = jnp.concatenate(blocks, axis=0)
        swapped_half = lax.ppermute(gathered, "fsdp", [(i, i ^ 1) for i in range(parts)])
        window_normed = jnp.where(carries_normed, gathered, swapped_half)
        window_masked = jnp.where(carries_normed, swapped_half, gathered)
    else:
        packed = jnp.concatenate([send_normed, send_masked], axis=0)
        blocks = [packed] + [shifted(packed, "seq", (shards,), (k,)) for k in range(1, shards)]
        window_normed = jnp.concatenate([b[:MAXACT] for b in blocks], axis=0)
        window_masked = jnp.concatenate([b[MAXACT:] for b in blocks], axis=0)
    window = window_normed.shape[0]
    gate_rows, up_rows, hidden, partial_features = weight_pass(
        window_normed, window_masked, gate_weight, up_weight, down_weight
    )
    columns = jnp.concatenate([window_normed, window_masked], axis=0)
    columns = columns.reshape(2 * window, replicas, feature_share)
    every_factors, every_columns = rep_exchange(
        jnp.concatenate([gate_rows, up_rows, hidden], axis=0),
        [columns[:, b] for b in range(replicas)],
        "rep",
        replicas,
    )
    partial_features = partial_features.astype(jnp.bfloat16)
    feature_grad = partial_features[:MAXACT].astype(jnp.float32)
    for k in range(1, shards):
        piece = partial_features[k * MAXACT : (k + 1) * MAXACT]
        feature_grad = feature_grad + shifted(piece, "seq", (shards,), (-k,)).astype(jnp.float32)
    every_gate = jnp.concatenate([f[:window] for f in every_factors], axis=0)
    every_up = jnp.concatenate([f[window : 2 * window] for f in every_factors], axis=0)
    every_hidden = jnp.concatenate([f[2 * window :] for f in every_factors], axis=0)
    normed_cols = jnp.concatenate([c[:window] for c in every_columns], axis=0)
    masked_cols = jnp.concatenate([c[window:] for c in every_columns], axis=0)
    gate_grad, up_grad, down_grad = weight_grads(
        normed_cols, every_gate, every_up, every_hidden, masked_cols
    )
    seq_sum = feature_grad.astype(jnp.bfloat16)
    for step in range(1, parts):
        feature_grad = feature_grad + shifted(seq_sum, "fsdp", (parts,), (step,)).astype(jnp.float32)
    _, pullback = jax.vjp(partial(normalize, norm_gain=norm_gain), source)
    slot_grad = pullback(feature_grad)[0].astype(jnp.bfloat16)
    own_columns = lax.dynamic_slice_in_dim(picker, place * own_rows, own_rows, 1)
    branch_grad = contract_first(own_columns, slot_grad).astype(jnp.bfloat16)
    return (branch_grad, gate_grad, up_grad, down_grad)


def solution(mesh):
    in_specs = (
        P(("rep", "seq"), None),
        P(("rep", "seq"), None),
        P(),
        P(None, ("seq", "fsdp")),
        P(None, ("seq", "fsdp")),
        P(("seq", "fsdp"), None),
        P(("rep", "seq")),
    )
    out_specs = (
        P(("rep", "seq", "fsdp"), None),
        P("rep", ("seq", "fsdp")),
        P("rep", ("seq", "fsdp")),
        P(("seq", "fsdp"), "rep"),
    )
    return jax.shard_map(local, mesh=mesh, in_specs=in_specs, out_specs=out_specs, check_vma=False)
```

```python
from functools import partial

import jax
import jax.numpy as jnp
from jax import lax
from jax.experimental import pallas as pl
from jax.experimental.pallas import tpu as pltpu
from jax.sharding import PartitionSpec as P

REC = 1
MAXACT = 8


EPSILON = 1e-05


def normalize(widened, norm_gain):
    factor = lax.rsqrt(jnp.mean(widened * widened, axis=-1, keepdims=True) + EPSILON)
    return widened * factor * norm_gain


def contract_first(left, right):
    return lax.dot_general(
        left, right, (((0,), (0,)), ((), ())), preferred_element_type=jnp.float32
    )


def contract_last(left, right):
    return lax.dot_general(
        left, right, (((1,), (1,)), ((), ())), preferred_element_type=jnp.float32
    )


def shifted(value, axes, sizes, steps):
    total = 1
    for size in sizes:
        total *= size
    pairs = []
    for index in range(total):
        coords, rest = [], index
        for size in reversed(sizes):
            coords.append(rest % size)
            rest //= size
        coords = coords[::-1]
        target, scale = 0, 1
        for axis in reversed(range(len(sizes))):
            target += ((coords[axis] + steps[axis]) % sizes[axis]) * scale
            scale *= sizes[axis]
        pairs.append((index, target))
    return lax.ppermute(value, axes, pairs)


def swapped(value, axis, size, distance):
    return lax.ppermute(value, axis, [(i, i ^ distance) for i in range(size)])


def power_of_two(size):
    return size & (size - 1) == 0


def gather_blocks(value, axis, size):
    if power_of_two(size):
        blocks, distance = [value], 1
        while distance < size:
            arrived = swapped(jnp.stack(blocks), axis, size, distance)
            blocks = blocks + [arrived[k] for k in range(distance)]
            distance *= 2
        return blocks, lambda k: ("xor", k)
    blocks = [value] + [shifted(value, axis, (size,), (k,)) for k in range(1, size)]
    return blocks, lambda k: ("shift", k)


def scatter_sum(pieces, axis, size):
    if power_of_two(size):
        held = {k: piece.astype(jnp.float32) for k, piece in enumerate(pieces)}
        distance = size // 2
        while distance >= 1:
            leaving = sorted(k for k in held if k & distance)
            arrived = swapped(
                jnp.stack([held[k] for k in leaving]).astype(jnp.bfloat16), axis, size, distance
            )
            for position, k in enumerate(leaving):
                held[k ^ distance] = held[k ^ distance] + arrived[position].astype(jnp.float32)
            held = {k: v for k, v in held.items() if not k & distance}
            distance //= 2
        return held[0]
    total = pieces[0].astype(jnp.float32)
    for k in range(1, size):
        total = total + shifted(pieces[k], axis, (size,), (-k,)).astype(jnp.float32)
    return total


def all_sum(value, axis, size):
    if power_of_two(size):
        total, distance = value, 1
        while distance < size:
            total = total + swapped(total.astype(jnp.bfloat16), axis, size, distance).astype(jnp.float32)
            distance *= 2
        return total
    total = value
    for k in range(1, size):
        total = total + shifted(value.astype(jnp.bfloat16), axis, (size,), (k,)).astype(jnp.float32)
    return total


def exchange_blocks(blocks, axis, size):
    index = lax.axis_index(axis)
    if power_of_two(size):
        stacked = jnp.stack(blocks)
        held = {(0, k): lax.dynamic_index_in_dim(stacked, index ^ k, 0, keepdims=False) for k in range(size)}
        distance = 1
        while distance < size:
            leaving = sorted(key for key in held if key[1] & distance)
            arrived = swapped(jnp.stack([held[key] for key in leaving]), axis, size, distance)
            held = {key: v for key, v in held.items() if not key[1] & distance}
            for position, (origin, target) in enumerate(leaving):
                held[(origin ^ distance, target ^ distance)] = arrived[position]
            distance *= 2
        return [held[(k, 0)] for k in range(size)]
    stacked = jnp.stack(blocks)
    out = [lax.dynamic_index_in_dim(stacked, index, 0, keepdims=False)]
    for k in range(1, size):
        outgoing = lax.dynamic_index_in_dim(stacked, (index + k) % size, 0, keepdims=False)
        out.append(shifted(outgoing, axis, (size,), (k,)))
    return out


def rep_exchange(factors, column_blocks, axis, size, tied):
    index = lax.axis_index(axis)
    stacked = jnp.stack(column_blocks)
    if power_of_two(size):
        gathered = {0: factors}
        held = {(0, k): lax.dynamic_index_in_dim(stacked, index ^ k, 0, keepdims=False) for k in range(size)}
        distance = size // 2
        while distance >= 1:
            origins = sorted(gathered)
            arrived = swapped(jnp.stack([gathered[o] for o in origins]), axis, size, distance)
            for position, origin in enumerate(origins):
                gathered[origin ^ distance] = arrived[position]
            leaving = sorted(key for key in held if key[1] & distance)
            arrived = swapped(jnp.stack([held[key] for key in leaving]), axis, size, distance)
            held = {key: v for key, v in held.items() if not key[1] & distance}
            for position, (origin, target) in enumerate(leaving):
                held[(origin ^ distance, target ^ distance)] = arrived[position]
            if distance == size // 2:
                gathered, held, tied = lax.optimization_barrier((gathered, held, tied))
            distance //= 2
        return [gathered[o] for o in range(size)], [held[(o, 0)] for o in range(size)], tied
    every_factors = [factors]
    every_columns = [lax.dynamic_index_in_dim(stacked, index, 0, keepdims=False)]
    for k in range(1, size):
        every_factors.append(shifted(factors, axis, (size,), (k,)))
        outgoing = lax.dynamic_index_in_dim(stacked, (index + k) % size, 0, keepdims=False)
        every_columns.append(shifted(outgoing, axis, (size,), (k,)))
    return every_factors, every_columns, tied


def weight_pass_kernel(normed_ref, masked_ref, gate_w_ref, up_w_ref, down_w_ref,
                       gate_rows_ref, up_rows_ref, hidden_ref, features_ref):
    step = pl.program_id(0)
    normed = normed_ref[...]
    gate_w = gate_w_ref[...]
    up_w = up_w_ref[...]
    gate = jnp.dot(normed, gate_w, preferred_element_type=jnp.float32)
    up = jnp.dot(normed, up_w, preferred_element_type=jnp.float32)
    hidden_grad = contract_last(masked_ref[...], down_w_ref[...])
    sigmoid_gate = 1.0 / (1.0 + jnp.exp(-gate))
    swished = gate * sigmoid_gate
    gate_rows = (hidden_grad * up * sigmoid_gate * (1.0 + gate * (1.0 - sigmoid_gate))).astype(
        jnp.bfloat16
    )
    up_rows = (hidden_grad * swished).astype(jnp.bfloat16)
    hidden_ref[...] = (swished * up).astype(jnp.bfloat16)
    gate_rows_ref[...] = gate_rows
    up_rows_ref[...] = up_rows
    partial_features = contract_last(gate_rows, gate_w) + contract_last(up_rows, up_w)

    @pl.when(step == 0)
    def _():
        features_ref[...] = partial_features

    @pl.when(step > 0)
    def _():
        features_ref[...] += partial_features


def weight_pass(window_normed, window_masked, gate_weight, up_weight, down_weight):
    rows, features = window_normed.shape
    units = gate_weight.shape[1]
    chunk = next((size for size in (512, 256, 128) if units % size == 0), units)
    factor_shape = jax.ShapeDtypeStruct((rows, units), jnp.bfloat16)
    return pl.pallas_call(
        weight_pass_kernel,
        grid=(units // chunk,),
        in_specs=[
            pl.BlockSpec((rows, features), lambda j: (0, 0)),
            pl.BlockSpec((rows, features), lambda j: (0, 0)),
            pl.BlockSpec((features, chunk), lambda j: (0, j)),
            pl.BlockSpec((features, chunk), lambda j: (0, j)),
            pl.BlockSpec((chunk, features), lambda j: (j, 0)),
        ],
        out_specs=[
            pl.BlockSpec((rows, chunk), lambda j: (0, j)),
            pl.BlockSpec((rows, chunk), lambda j: (0, j)),
            pl.BlockSpec((rows, chunk), lambda j: (0, j)),
            pl.BlockSpec((rows, features), lambda j: (0, 0)),
        ],
        out_shape=[
            factor_shape,
            factor_shape,
            factor_shape,
            jax.ShapeDtypeStruct((rows, features), jnp.float32),
        ],
        compiler_params=pltpu.CompilerParams(vmem_limit_bytes=56 * 1024 * 1024),
        cost_estimate=pl.CostEstimate(
            flops=10 * rows * features * units,
            transcendentals=rows * units,
            bytes_accessed=6 * features * units + 4 * rows * features * 2,
        ),
    )(window_normed, window_masked, gate_weight, up_weight, down_weight)


def grads_kernel(normed_ref, gate_ref, up_ref, hidden_ref, masked_ref,
                 gate_grad_ref, up_grad_ref, down_grad_ref):
    normed = normed_ref[...]
    gate_grad_ref[...] = contract_first(normed, gate_ref[...])
    up_grad_ref[...] = contract_first(normed, up_ref[...])
    down_grad_ref[...] = contract_first(hidden_ref[...], masked_ref[...])


def weight_grads(normed_cols, every_gate, every_up, every_hidden, masked_cols):
    rows, share = normed_cols.shape
    units = every_gate.shape[1]
    steps = 4 if share % 512 == 0 and units % 512 == 0 else 1
    share_block, unit_block = share // steps, units // steps
    return pl.pallas_call(
        grads_kernel,
        grid=(steps,),
        in_specs=[
            pl.BlockSpec((rows, share_block), lambda i: (0, i)),
            pl.BlockSpec((rows, units), lambda i: (0, 0)),
            pl.BlockSpec((rows, units), lambda i: (0, 0)),
            pl.BlockSpec((rows, unit_block), lambda i: (0, i)),
            pl.BlockSpec((rows, share), lambda i: (0, 0)),
        ],
        out_specs=[
            pl.BlockSpec((share_block, units), lambda i: (i, 0)),
            pl.BlockSpec((share_block, units), lambda i: (i, 0)),
            pl.BlockSpec((unit_block, share), lambda i: (i, 0)),
        ],
        out_shape=[
            jax.ShapeDtypeStruct((share, units), jnp.float32),
            jax.ShapeDtypeStruct((share, units), jnp.float32),
            jax.ShapeDtypeStruct((units, share), jnp.float32),
        ],
        compiler_params=pltpu.CompilerParams(vmem_limit_bytes=48 * 1024 * 1024),
        cost_estimate=pl.CostEstimate(
            flops=6 * rows * share * units,
            transcendentals=0,
            bytes_accessed=12 * share * units + 2 * rows * (2 * share + 3 * units),
        ),
    )(normed_cols, every_gate, every_up, every_hidden, masked_cols)


def local(tokens, cotangent, norm_gain, gate_weight, up_weight, down_weight, depths):
    parts = lax.axis_size("fsdp")
    place = lax.axis_index("fsdp")
    replicas = lax.axis_size("rep")
    replica = lax.axis_index("rep")
    shards = lax.axis_size("seq")
    features = tokens.shape[1]
    feature_share = features // replicas
    rows_here = tokens.shape[0]
    own_rows = rows_here // parts
    active = depths > REC
    ordinal = jnp.cumsum(active.astype(jnp.int32)) - 1
    selector = (ordinal[None, :] == jnp.arange(MAXACT, dtype=jnp.int32)[:, None]) & active[None, :]
    picker = selector.astype(jnp.bfloat16)
    source = jnp.dot(picker, tokens, preferred_element_type=jnp.float32)
    send_masked = jnp.dot(picker, cotangent, preferred_element_type=jnp.float32).astype(jnp.bfloat16)
    send_normed = normalize(source, norm_gain).astype(jnp.bfloat16)
    packed = jnp.concatenate([send_normed, send_masked], axis=0)
    blocks = [packed] + [shifted(packed, "seq", (shards,), (k,)) for k in range(1, shards)]
    window_normed = jnp.concatenate([b[:MAXACT] for b in blocks], axis=0)
    window_masked = jnp.concatenate([b[MAXACT:] for b in blocks], axis=0)
    window = window_normed.shape[0]
    gate_rows, up_rows, hidden, partial_features = weight_pass(
        window_normed, window_masked, gate_weight, up_weight, down_weight
    )
    columns = jnp.concatenate([window_normed, window_masked], axis=0)
    columns = columns.reshape(2 * window, replicas, feature_share)
    every_factors, every_columns, partial_features = rep_exchange(
        jnp.concatenate([gate_rows, up_rows, hidden], axis=0),
        [columns[:, b] for b in range(replicas)],
        "rep",
        replicas,
        partial_features,
    )
    partial_features = partial_features.astype(jnp.bfloat16)
    feature_grad = partial_features[:MAXACT].astype(jnp.float32)
    for k in range(1, shards):
        piece = partial_features[k * MAXACT : (k + 1) * MAXACT]
        feature_grad = feature_grad + shifted(piece, "seq", (shards,), (-k,)).astype(jnp.float32)
    every_gate = jnp.concatenate([f[:window] for f in every_factors], axis=0)
    every_up = jnp.concatenate([f[window : 2 * window] for f in every_factors], axis=0)
    every_hidden = jnp.concatenate([f[2 * window :] for f in every_factors], axis=0)
    normed_cols = jnp.concatenate([c[:window] for c in every_columns], axis=0)
    masked_cols = jnp.concatenate([c[window:] for c in every_columns], axis=0)
    gate_grad, up_grad, down_grad = weight_grads(
        normed_cols, every_gate, every_up, every_hidden, masked_cols
    )
    seq_sum = feature_grad.astype(jnp.bfloat16)
    for step in range(1, parts):
        feature_grad = feature_grad + shifted(seq_sum, "fsdp", (parts,), (step,)).astype(jnp.float32)
    _, pullback = jax.vjp(partial(normalize, norm_gain=norm_gain), source)
    slot_grad = pullback(feature_grad)[0].astype(jnp.bfloat16)
    own_columns = lax.dynamic_slice_in_dim(picker, place * own_rows, own_rows, 1)
    branch_grad = contract_first(own_columns, slot_grad).astype(jnp.bfloat16)
    return (branch_grad, gate_grad, up_grad, down_grad)


def solution(mesh):
    in_specs = (
        P(("rep", "seq"), None),
        P(("rep", "seq"), None),
        P(),
        P(None, ("seq", "fsdp")),
        P(None, ("seq", "fsdp")),
        P(("seq", "fsdp"), None),
        P(("rep", "seq")),
    )
    out_specs = (
        P(("rep", "seq", "fsdp"), None),
        P("rep", ("seq", "fsdp")),
        P("rep", ("seq", "fsdp")),
        P(("seq", "fsdp"), "rep"),
    )
    return jax.shard_map(local, mesh=mesh, in_specs=in_specs, out_specs=out_specs, check_vma=False)
```

```python
from functools import partial

import jax
import jax.numpy as jnp
from jax import lax
from jax.experimental import pallas as pl
from jax.experimental.pallas import tpu as pltpu
from jax.sharding import PartitionSpec as P

REC = 1
MAXACT = 8


EPSILON = 1e-05


def normalize(widened, norm_gain):
    factor = lax.rsqrt(jnp.mean(widened * widened, axis=-1, keepdims=True) + EPSILON)
    return widened * factor * norm_gain


def contract_first(left, right):
    return lax.dot_general(
        left, right, (((0,), (0,)), ((), ())), preferred_element_type=jnp.float32
    )


def contract_last(left, right):
    return lax.dot_general(
        left, right, (((1,), (1,)), ((), ())), preferred_element_type=jnp.float32
    )


def shifted(value, axes, sizes, steps):
    total = 1
    for size in sizes:
        total *= size
    pairs = []
    for index in range(total):
        coords, rest = [], index
        for size in reversed(sizes):
            coords.append(rest % size)
            rest //= size
        coords = coords[::-1]
        target, scale = 0, 1
        for axis in reversed(range(len(sizes))):
            target += ((coords[axis] + steps[axis]) % sizes[axis]) * scale
            scale *= sizes[axis]
        pairs.append((index, target))
    return lax.ppermute(value, axes, pairs)


def swapped(value, axis, size, distance):
    return lax.ppermute(value, axis, [(i, i ^ distance) for i in range(size)])


def power_of_two(size):
    return size & (size - 1) == 0


def gather_blocks(value, axis, size):
    if power_of_two(size):
        blocks, distance = [value], 1
        while distance < size:
            arrived = swapped(jnp.stack(blocks), axis, size, distance)
            blocks = blocks + [arrived[k] for k in range(distance)]
            distance *= 2
        return blocks, lambda k: ("xor", k)
    blocks = [value] + [shifted(value, axis, (size,), (k,)) for k in range(1, size)]
    return blocks, lambda k: ("shift", k)


def scatter_sum(pieces, axis, size):
    if power_of_two(size):
        held = {k: piece.astype(jnp.float32) for k, piece in enumerate(pieces)}
        distance = size // 2
        while distance >= 1:
            leaving = sorted(k for k in held if k & distance)
            arrived = swapped(
                jnp.stack([held[k] for k in leaving]).astype(jnp.bfloat16), axis, size, distance
            )
            for position, k in enumerate(leaving):
                held[k ^ distance] = held[k ^ distance] + arrived[position].astype(jnp.float32)
            held = {k: v for k, v in held.items() if not k & distance}
            distance //= 2
        return held[0]
    total = pieces[0].astype(jnp.float32)
    for k in range(1, size):
        total = total + shifted(pieces[k], axis, (size,), (-k,)).astype(jnp.float32)
    return total


def all_sum(value, axis, size):
    if power_of_two(size):
        total, distance = value, 1
        while distance < size:
            total = total + swapped(total.astype(jnp.bfloat16), axis, size, distance).astype(jnp.float32)
            distance *= 2
        return total
    total = value
    for k in range(1, size):
        total = total + shifted(value.astype(jnp.bfloat16), axis, (size,), (k,)).astype(jnp.float32)
    return total


def exchange_blocks(blocks, axis, size):
    index = lax.axis_index(axis)
    if power_of_two(size):
        stacked = jnp.stack(blocks)
        held = {(0, k): lax.dynamic_index_in_dim(stacked, index ^ k, 0, keepdims=False) for k in range(size)}
        distance = 1
        while distance < size:
            leaving = sorted(key for key in held if key[1] & distance)
            arrived = swapped(jnp.stack([held[key] for key in leaving]), axis, size, distance)
            held = {key: v for key, v in held.items() if not key[1] & distance}
            for position, (origin, target) in enumerate(leaving):
                held[(origin ^ distance, target ^ distance)] = arrived[position]
            distance *= 2
        return [held[(k, 0)] for k in range(size)]
    stacked = jnp.stack(blocks)
    out = [lax.dynamic_index_in_dim(stacked, index, 0, keepdims=False)]
    for k in range(1, size):
        outgoing = lax.dynamic_index_in_dim(stacked, (index + k) % size, 0, keepdims=False)
        out.append(shifted(outgoing, axis, (size,), (k,)))
    return out


def rep_exchange(factors, column_blocks, axis, size):
    index = lax.axis_index(axis)
    stacked = jnp.stack(column_blocks)
    if power_of_two(size):
        gathered = {0: factors}
        held = {(0, k): lax.dynamic_index_in_dim(stacked, index ^ k, 0, keepdims=False) for k in range(size)}
        distance = size // 2
        while distance >= 1:
            origins = sorted(gathered)
            arrived = swapped(jnp.stack([gathered[o] for o in origins]), axis, size, distance)
            for position, origin in enumerate(origins):
                gathered[origin ^ distance] = arrived[position]
            leaving = sorted(key for key in held if key[1] & distance)
            arrived = swapped(jnp.stack([held[key] for key in leaving]), axis, size, distance)
            held = {key: v for key, v in held.items() if not key[1] & distance}
            for position, (origin, target) in enumerate(leaving):
                held[(origin ^ distance, target ^ distance)] = arrived[position]
            distance //= 2
        return [gathered[o] for o in range(size)], [held[(o, 0)] for o in range(size)]
    every_factors = [factors]
    every_columns = [lax.dynamic_index_in_dim(stacked, index, 0, keepdims=False)]
    for k in range(1, size):
        every_factors.append(shifted(factors, axis, (size,), (k,)))
        outgoing = lax.dynamic_index_in_dim(stacked, (index + k) % size, 0, keepdims=False)
        every_columns.append(shifted(outgoing, axis, (size,), (k,)))
    return every_factors, every_columns


def weight_pass_kernel(normed_ref, masked_ref, gate_w_ref, up_w_ref, down_w_ref,
                       gate_rows_ref, up_rows_ref, hidden_ref, features_ref):
    step = pl.program_id(0)
    normed = normed_ref[...]
    gate_w = gate_w_ref[...]
    up_w = up_w_ref[...]
    gate = jnp.dot(normed, gate_w, preferred_element_type=jnp.float32)
    up = jnp.dot(normed, up_w, preferred_element_type=jnp.float32)
    hidden_grad = contract_last(masked_ref[...], down_w_ref[...])
    sigmoid_gate = 1.0 / (1.0 + jnp.exp(-gate))
    swished = gate * sigmoid_gate
    gate_rows = (hidden_grad * up * sigmoid_gate * (1.0 + gate * (1.0 - sigmoid_gate))).astype(
        jnp.bfloat16
    )
    up_rows = (hidden_grad * swished).astype(jnp.bfloat16)
    hidden_ref[...] = (swished * up).astype(jnp.bfloat16)
    gate_rows_ref[...] = gate_rows
    up_rows_ref[...] = up_rows
    partial_features = contract_last(gate_rows, gate_w) + contract_last(up_rows, up_w)

    @pl.when(step == 0)
    def _():
        features_ref[...] = partial_features

    @pl.when(step > 0)
    def _():
        features_ref[...] += partial_features


def weight_pass(window_normed, window_masked, gate_weight, up_weight, down_weight):
    rows, features = window_normed.shape
    units = gate_weight.shape[1]
    chunk = next((size for size in (512, 256, 128) if units % size == 0), units)
    factor_shape = jax.ShapeDtypeStruct((rows, units), jnp.bfloat16)
    return pl.pallas_call(
        weight_pass_kernel,
        grid=(units // chunk,),
        in_specs=[
            pl.BlockSpec((rows, features), lambda j: (0, 0)),
            pl.BlockSpec((rows, features), lambda j: (0, 0)),
            pl.BlockSpec((features, chunk), lambda j: (0, j)),
            pl.BlockSpec((features, chunk), lambda j: (0, j)),
            pl.BlockSpec((chunk, features), lambda j: (j, 0)),
        ],
        out_specs=[
            pl.BlockSpec((rows, chunk), lambda j: (0, j)),
            pl.BlockSpec((rows, chunk), lambda j: (0, j)),
            pl.BlockSpec((rows, chunk), lambda j: (0, j)),
            pl.BlockSpec((rows, features), lambda j: (0, 0)),
        ],
        out_shape=[
            factor_shape,
            factor_shape,
            factor_shape,
            jax.ShapeDtypeStruct((rows, features), jnp.float32),
        ],
        compiler_params=pltpu.CompilerParams(vmem_limit_bytes=56 * 1024 * 1024),
        cost_estimate=pl.CostEstimate(
            flops=10 * rows * features * units,
            transcendentals=rows * units,
            bytes_accessed=6 * features * units + 4 * rows * features * 2,
        ),
    )(window_normed, window_masked, gate_weight, up_weight, down_weight)


def grads_kernel(normed_ref, gate_ref, up_ref, hidden_ref, masked_ref,
                 gate_grad_ref, up_grad_ref, down_grad_ref):
    normed = normed_ref[...]
    gate_grad_ref[...] = contract_first(normed, gate_ref[...])
    up_grad_ref[...] = contract_first(normed, up_ref[...])
    down_grad_ref[...] = contract_first(hidden_ref[...], masked_ref[...])


def weight_grads(normed_cols, every_gate, every_up, every_hidden, masked_cols):
    rows, share = normed_cols.shape
    units = every_gate.shape[1]
    steps = 4 if share % 512 == 0 and units % 512 == 0 else 1
    share_block, unit_block = share // steps, units // steps
    return pl.pallas_call(
        grads_kernel,
        grid=(steps,),
        in_specs=[
            pl.BlockSpec((rows, share_block), lambda i: (0, i)),
            pl.BlockSpec((rows, units), lambda i: (0, 0)),
            pl.BlockSpec((rows, units), lambda i: (0, 0)),
            pl.BlockSpec((rows, unit_block), lambda i: (0, i)),
            pl.BlockSpec((rows, share), lambda i: (0, 0)),
        ],
        out_specs=[
            pl.BlockSpec((share_block, units), lambda i: (i, 0)),
            pl.BlockSpec((share_block, units), lambda i: (i, 0)),
            pl.BlockSpec((unit_block, share), lambda i: (i, 0)),
        ],
        out_shape=[
            jax.ShapeDtypeStruct((share, units), jnp.float32),
            jax.ShapeDtypeStruct((share, units), jnp.float32),
            jax.ShapeDtypeStruct((units, share), jnp.float32),
        ],
        compiler_params=pltpu.CompilerParams(vmem_limit_bytes=48 * 1024 * 1024),
        cost_estimate=pl.CostEstimate(
            flops=6 * rows * share * units,
            transcendentals=0,
            bytes_accessed=12 * share * units + 2 * rows * (2 * share + 3 * units),
        ),
    )(normed_cols, every_gate, every_up, every_hidden, masked_cols)


def local(tokens, cotangent, norm_gain, gate_weight, up_weight, down_weight, depths):
    parts = lax.axis_size("fsdp")
    place = lax.axis_index("fsdp")
    replicas = lax.axis_size("rep")
    replica = lax.axis_index("rep")
    shards = lax.axis_size("seq")
    features = tokens.shape[1]
    feature_share = features // replicas
    rows_here = tokens.shape[0]
    own_rows = rows_here // parts
    active = depths > REC
    ordinal = jnp.cumsum(active.astype(jnp.int32)) - 1
    selector = (ordinal[None, :] == jnp.arange(MAXACT, dtype=jnp.int32)[:, None]) & active[None, :]
    picker = selector.astype(jnp.bfloat16)
    source = jnp.dot(picker, tokens, preferred_element_type=jnp.float32)
    send_masked = jnp.dot(picker, cotangent, preferred_element_type=jnp.float32).astype(jnp.bfloat16)
    send_normed = normalize(source, norm_gain).astype(jnp.bfloat16)
    packed = jnp.concatenate([send_normed, send_masked], axis=0)
    blocks = [packed] + [shifted(packed, "seq", (shards,), (k,)) for k in range(1, shards)]
    window_normed = jnp.concatenate([b[:MAXACT] for b in blocks], axis=0)
    window_masked = jnp.concatenate([b[MAXACT:] for b in blocks], axis=0)
    window = window_normed.shape[0]
    gate_rows, up_rows, hidden, partial_features = weight_pass(
        window_normed, window_masked, gate_weight, up_weight, down_weight
    )
    columns = jnp.concatenate([window_normed, window_masked], axis=0)
    columns = columns.reshape(2 * window, replicas, feature_share)
    every_factors, every_columns = rep_exchange(
        jnp.concatenate([gate_rows, up_rows, hidden], axis=0),
        [columns[:, b] for b in range(replicas)],
        "rep",
        replicas,
    )
    partial_features = partial_features.astype(jnp.bfloat16)
    feature_grad = partial_features[:MAXACT].astype(jnp.float32)
    for k in range(shards):
        piece = partial_features[k * MAXACT : (k + 1) * MAXACT]
        for step in range(parts):
            if k == 0 and step == 0:
                continue
            arrived = shifted(piece, ("seq", "fsdp"), (shards, parts), (-k, step))
            feature_grad = feature_grad + arrived.astype(jnp.float32)
    every_gate = jnp.concatenate([f[:window] for f in every_factors], axis=0)
    every_up = jnp.concatenate([f[window : 2 * window] for f in every_factors], axis=0)
    every_hidden = jnp.concatenate([f[2 * window :] for f in every_factors], axis=0)
    normed_cols = jnp.concatenate([c[:window] for c in every_columns], axis=0)
    masked_cols = jnp.concatenate([c[window:] for c in every_columns], axis=0)
    gate_grad, up_grad, down_grad = weight_grads(
        normed_cols, every_gate, every_up, every_hidden, masked_cols
    )
    _, pullback = jax.vjp(partial(normalize, norm_gain=norm_gain), source)
    slot_grad = pullback(feature_grad)[0].astype(jnp.bfloat16)
    own_columns = lax.dynamic_slice_in_dim(picker, place * own_rows, own_rows, 1)
    branch_grad = contract_first(own_columns, slot_grad).astype(jnp.bfloat16)
    return (branch_grad, gate_grad, up_grad, down_grad)


def solution(mesh):
    in_specs = (
        P(("rep", "seq"), None),
        P(("rep", "seq"), None),
        P(),
        P(None, ("seq", "fsdp")),
        P(None, ("seq", "fsdp")),
        P(("seq", "fsdp"), None),
        P(("rep", "seq")),
    )
    out_specs = (
        P(("rep", "seq", "fsdp"), None),
        P("rep", ("seq", "fsdp")),
        P("rep", ("seq", "fsdp")),
        P(("seq", "fsdp"), "rep"),
    )
    return jax.shard_map(local, mesh=mesh, in_specs=in_specs, out_specs=out_specs, check_vma=False)
```

```python
from functools import partial

import jax
import jax.numpy as jnp
from jax import lax
from jax.experimental import pallas as pl
from jax.experimental.pallas import tpu as pltpu
from jax.sharding import PartitionSpec as P

REC = 1
MAXACT = 8


EPSILON = 1e-05


def normalize(widened, norm_gain):
    factor = lax.rsqrt(jnp.mean(widened * widened, axis=-1, keepdims=True) + EPSILON)
    return widened * factor * norm_gain


def contract_first(left, right):
    return lax.dot_general(
        left, right, (((0,), (0,)), ((), ())), preferred_element_type=jnp.float32
    )


def contract_last(left, right):
    return lax.dot_general(
        left, right, (((1,), (1,)), ((), ())), preferred_element_type=jnp.float32
    )


def shifted(value, axes, sizes, steps):
    total = 1
    for size in sizes:
        total *= size
    pairs = []
    for index in range(total):
        coords, rest = [], index
        for size in reversed(sizes):
            coords.append(rest % size)
            rest //= size
        coords = coords[::-1]
        target, scale = 0, 1
        for axis in reversed(range(len(sizes))):
            target += ((coords[axis] + steps[axis]) % sizes[axis]) * scale
            scale *= sizes[axis]
        pairs.append((index, target))
    return lax.ppermute(value, axes, pairs)


def swapped(value, axis, size, distance):
    return lax.ppermute(value, axis, [(i, i ^ distance) for i in range(size)])


def power_of_two(size):
    return size & (size - 1) == 0


def gather_blocks(value, axis, size):
    if power_of_two(size):
        blocks, distance = [value], 1
        while distance < size:
            arrived = swapped(jnp.stack(blocks), axis, size, distance)
            blocks = blocks + [arrived[k] for k in range(distance)]
            distance *= 2
        return blocks, lambda k: ("xor", k)
    blocks = [value] + [shifted(value, axis, (size,), (k,)) for k in range(1, size)]
    return blocks, lambda k: ("shift", k)


def scatter_sum(pieces, axis, size):
    if power_of_two(size):
        held = {k: piece.astype(jnp.float32) for k, piece in enumerate(pieces)}
        distance = size // 2
        while distance >= 1:
            leaving = sorted(k for k in held if k & distance)
            arrived = swapped(
                jnp.stack([held[k] for k in leaving]).astype(jnp.bfloat16), axis, size, distance
            )
            for position, k in enumerate(leaving):
                held[k ^ distance] = held[k ^ distance] + arrived[position].astype(jnp.float32)
            held = {k: v for k, v in held.items() if not k & distance}
            distance //= 2
        return held[0]
    total = pieces[0].astype(jnp.float32)
    for k in range(1, size):
        total = total + shifted(pieces[k], axis, (size,), (-k,)).astype(jnp.float32)
    return total


def all_sum(value, axis, size):
    if power_of_two(size):
        total, distance = value, 1
        while distance < size:
            total = total + swapped(total.astype(jnp.bfloat16), axis, size, distance).astype(jnp.float32)
            distance *= 2
        return total
    total = value
    for k in range(1, size):
        total = total + shifted(value.astype(jnp.bfloat16), axis, (size,), (k,)).astype(jnp.float32)
    return total


def exchange_blocks(blocks, axis, size):
    index = lax.axis_index(axis)
    if power_of_two(size):
        stacked = jnp.stack(blocks)
        held = {(0, k): lax.dynamic_index_in_dim(stacked, index ^ k, 0, keepdims=False) for k in range(size)}
        distance = 1
        while distance < size:
            leaving = sorted(key for key in held if key[1] & distance)
            arrived = swapped(jnp.stack([held[key] for key in leaving]), axis, size, distance)
            held = {key: v for key, v in held.items() if not key[1] & distance}
            for position, (origin, target) in enumerate(leaving):
                held[(origin ^ distance, target ^ distance)] = arrived[position]
            distance *= 2
        return [held[(k, 0)] for k in range(size)]
    stacked = jnp.stack(blocks)
    out = [lax.dynamic_index_in_dim(stacked, index, 0, keepdims=False)]
    for k in range(1, size):
        outgoing = lax.dynamic_index_in_dim(stacked, (index + k) % size, 0, keepdims=False)
        out.append(shifted(outgoing, axis, (size,), (k,)))
    return out


def rep_exchange(factors, column_blocks, axis, size):
    index = lax.axis_index(axis)
    stacked = jnp.stack(column_blocks)
    if power_of_two(size):
        gathered = {0: factors}
        held = {(0, k): lax.dynamic_index_in_dim(stacked, index ^ k, 0, keepdims=False) for k in range(size)}
        distance = size // 2
        while distance >= 1:
            origins = sorted(gathered)
            arrived = swapped(jnp.stack([gathered[o] for o in origins]), axis, size, distance)
            for position, origin in enumerate(origins):
                gathered[origin ^ distance] = arrived[position]
            leaving = sorted(key for key in held if key[1] & distance)
            arrived = swapped(jnp.stack([held[key] for key in leaving]), axis, size, distance)
            held = {key: v for key, v in held.items() if not key[1] & distance}
            for position, (origin, target) in enumerate(leaving):
                held[(origin ^ distance, target ^ distance)] = arrived[position]
            distance //= 2
        return [gathered[o] for o in range(size)], [held[(o, 0)] for o in range(size)]
    every_factors = [factors]
    every_columns = [lax.dynamic_index_in_dim(stacked, index, 0, keepdims=False)]
    for k in range(1, size):
        every_factors.append(shifted(factors, axis, (size,), (k,)))
        outgoing = lax.dynamic_index_in_dim(stacked, (index + k) % size, 0, keepdims=False)
        every_columns.append(shifted(outgoing, axis, (size,), (k,)))
    return every_factors, every_columns


def weight_pass_kernel(normed_ref, masked_ref, gate_w_ref, up_w_ref, down_w_ref,
                       gate_rows_ref, up_rows_ref, hidden_ref, features_ref, total_ref):
    step = pl.program_id(0)
    normed = normed_ref[...]
    gate_w = gate_w_ref[...]
    up_w = up_w_ref[...]
    gate = jnp.dot(normed, gate_w, preferred_element_type=jnp.float32)
    up = jnp.dot(normed, up_w, preferred_element_type=jnp.float32)
    hidden_grad = contract_last(masked_ref[...], down_w_ref[...])
    sigmoid_gate = 1.0 / (1.0 + jnp.exp(-gate))
    swished = gate * sigmoid_gate
    gate_rows = (hidden_grad * up * sigmoid_gate * (1.0 + gate * (1.0 - sigmoid_gate))).astype(
        jnp.bfloat16
    )
    up_rows = (hidden_grad * swished).astype(jnp.bfloat16)
    hidden_ref[...] = (swished * up).astype(jnp.bfloat16)
    gate_rows_ref[...] = gate_rows
    up_rows_ref[...] = up_rows
    partial_features = contract_last(gate_rows, gate_w) + contract_last(up_rows, up_w)

    @pl.when(step == 0)
    def _():
        total_ref[...] = partial_features

    @pl.when(step > 0)
    def _():
        total_ref[...] += partial_features

    @pl.when(step == pl.num_programs(0) - 1)
    def _():
        features_ref[...] = total_ref[...].astype(features_ref.dtype)


def weight_pass(window_normed, window_masked, gate_weight, up_weight, down_weight):
    rows, features = window_normed.shape
    units = gate_weight.shape[1]
    chunk = next((size for size in (512, 256, 128) if units % size == 0), units)
    factor_shape = jax.ShapeDtypeStruct((rows, units), jnp.bfloat16)
    return pl.pallas_call(
        weight_pass_kernel,
        grid=(units // chunk,),
        in_specs=[
            pl.BlockSpec((rows, features), lambda j: (0, 0)),
            pl.BlockSpec((rows, features), lambda j: (0, 0)),
            pl.BlockSpec((features, chunk), lambda j: (0, j)),
            pl.BlockSpec((features, chunk), lambda j: (0, j)),
            pl.BlockSpec((chunk, features), lambda j: (j, 0)),
        ],
        out_specs=[
            pl.BlockSpec((rows, chunk), lambda j: (0, j)),
            pl.BlockSpec((rows, chunk), lambda j: (0, j)),
            pl.BlockSpec((rows, chunk), lambda j: (0, j)),
            pl.BlockSpec((rows, features), lambda j: (0, 0)),
        ],
        out_shape=[
            factor_shape,
            factor_shape,
            factor_shape,
            jax.ShapeDtypeStruct((rows, features), jnp.bfloat16),
        ],
        scratch_shapes=[pltpu.VMEM((rows, features), jnp.float32)],
        compiler_params=pltpu.CompilerParams(vmem_limit_bytes=56 * 1024 * 1024),
        cost_estimate=pl.CostEstimate(
            flops=10 * rows * features * units,
            transcendentals=rows * units,
            bytes_accessed=6 * features * units + 4 * rows * features * 2,
        ),
    )(window_normed, window_masked, gate_weight, up_weight, down_weight)


def grads_kernel(normed_ref, gate_ref, up_ref, hidden_ref, masked_ref,
                 gate_grad_ref, up_grad_ref, down_grad_ref):
    normed = normed_ref[...]
    gate_grad_ref[...] = contract_first(normed, gate_ref[...])
    up_grad_ref[...] = contract_first(normed, up_ref[...])
    down_grad_ref[...] = contract_first(hidden_ref[...], masked_ref[...])


def weight_grads(normed_cols, every_gate, every_up, every_hidden, masked_cols):
    rows, share = normed_cols.shape
    units = every_gate.shape[1]
    steps = 4 if share % 512 == 0 and units % 512 == 0 else 1
    share_block, unit_block = share // steps, units // steps
    return pl.pallas_call(
        grads_kernel,
        grid=(steps,),
        in_specs=[
            pl.BlockSpec((rows, share_block), lambda i: (0, i)),
            pl.BlockSpec((rows, units), lambda i: (0, 0)),
            pl.BlockSpec((rows, units), lambda i: (0, 0)),
            pl.BlockSpec((rows, unit_block), lambda i: (0, i)),
            pl.BlockSpec((rows, share), lambda i: (0, 0)),
        ],
        out_specs=[
            pl.BlockSpec((share_block, units), lambda i: (i, 0)),
            pl.BlockSpec((share_block, units), lambda i: (i, 0)),
            pl.BlockSpec((unit_block, share), lambda i: (i, 0)),
        ],
        out_shape=[
            jax.ShapeDtypeStruct((share, units), jnp.float32),
            jax.ShapeDtypeStruct((share, units), jnp.float32),
            jax.ShapeDtypeStruct((units, share), jnp.float32),
        ],
        compiler_params=pltpu.CompilerParams(vmem_limit_bytes=48 * 1024 * 1024),
        cost_estimate=pl.CostEstimate(
            flops=6 * rows * share * units,
            transcendentals=0,
            bytes_accessed=12 * share * units + 2 * rows * (2 * share + 3 * units),
        ),
    )(normed_cols, every_gate, every_up, every_hidden, masked_cols)


def local(tokens, cotangent, norm_gain, gate_weight, up_weight, down_weight, depths):
    parts = lax.axis_size("fsdp")
    place = lax.axis_index("fsdp")
    replicas = lax.axis_size("rep")
    replica = lax.axis_index("rep")
    shards = lax.axis_size("seq")
    features = tokens.shape[1]
    feature_share = features // replicas
    rows_here = tokens.shape[0]
    own_rows = rows_here // parts
    active = depths > REC
    ordinal = jnp.cumsum(active.astype(jnp.int32)) - 1
    selector = (ordinal[None, :] == jnp.arange(MAXACT, dtype=jnp.int32)[:, None]) & active[None, :]
    picker = selector.astype(jnp.bfloat16)
    source = jnp.dot(picker, tokens, preferred_element_type=jnp.float32)
    send_masked = jnp.dot(picker, cotangent, preferred_element_type=jnp.float32).astype(jnp.bfloat16)
    send_normed = normalize(source, norm_gain).astype(jnp.bfloat16)
    packed = jnp.concatenate([send_normed, send_masked], axis=0)
    blocks = [packed] + [shifted(packed, "seq", (shards,), (k,)) for k in range(1, shards)]
    window_normed = jnp.concatenate([b[:MAXACT] for b in blocks], axis=0)
    window_masked = jnp.concatenate([b[MAXACT:] for b in blocks], axis=0)
    window = window_normed.shape[0]
    gate_rows, up_rows, hidden, partial_features = weight_pass(
        window_normed, window_masked, gate_weight, up_weight, down_weight
    )
    columns = jnp.concatenate([window_normed, window_masked], axis=0)
    columns = columns.reshape(2 * window, replicas, feature_share)
    every_factors, every_columns = rep_exchange(
        jnp.concatenate([gate_rows, up_rows, hidden], axis=0),
        [columns[:, b] for b in range(replicas)],
        "rep",
        replicas,
    )
    feature_grad = partial_features[:MAXACT].astype(jnp.float32)
    for k in range(1, shards):
        piece = partial_features[k * MAXACT : (k + 1) * MAXACT]
        feature_grad = feature_grad + shifted(piece, "seq", (shards,), (-k,)).astype(jnp.float32)
    every_gate = jnp.concatenate([f[:window] for f in every_factors], axis=0)
    every_up = jnp.concatenate([f[window : 2 * window] for f in every_factors], axis=0)
    every_hidden = jnp.concatenate([f[2 * window :] for f in every_factors], axis=0)
    normed_cols = jnp.concatenate([c[:window] for c in every_columns], axis=0)
    masked_cols = jnp.concatenate([c[window:] for c in every_columns], axis=0)
    gate_grad, up_grad, down_grad = weight_grads(
        normed_cols, every_gate, every_up, every_hidden, masked_cols
    )
    seq_sum = feature_grad.astype(jnp.bfloat16)
    for step in range(1, parts):
        feature_grad = feature_grad + shifted(seq_sum, "fsdp", (parts,), (step,)).astype(jnp.float32)
    _, pullback = jax.vjp(partial(normalize, norm_gain=norm_gain), source)
    slot_grad = pullback(feature_grad)[0].astype(jnp.bfloat16)
    own_columns = lax.dynamic_slice_in_dim(picker, place * own_rows, own_rows, 1)
    branch_grad = contract_first(own_columns, slot_grad).astype(jnp.bfloat16)
    return (branch_grad, gate_grad, up_grad, down_grad)


def solution(mesh):
    in_specs = (
        P(("rep", "seq"), None),
        P(("rep", "seq"), None),
        P(),
        P(None, ("seq", "fsdp")),
        P(None, ("seq", "fsdp")),
        P(("seq", "fsdp"), None),
        P(("rep", "seq")),
    )
    out_specs = (
        P(("rep", "seq", "fsdp"), None),
        P("rep", ("seq", "fsdp")),
        P("rep", ("seq", "fsdp")),
        P(("seq", "fsdp"), "rep"),
    )
    return jax.shard_map(local, mesh=mesh, in_specs=in_specs, out_specs=out_specs, check_vma=False)
```

```python
from functools import partial

import jax
import jax.numpy as jnp
from jax import lax
from jax.experimental import pallas as pl
from jax.experimental.pallas import tpu as pltpu
from jax.sharding import PartitionSpec as P

REC = 1
MAXACT = 8


EPSILON = 1e-05


def normalize(widened, norm_gain):
    factor = lax.rsqrt(jnp.mean(widened * widened, axis=-1, keepdims=True) + EPSILON)
    return widened * factor * norm_gain


def contract_first(left, right):
    return lax.dot_general(
        left, right, (((0,), (0,)), ((), ())), preferred_element_type=jnp.float32
    )


def contract_last(left, right):
    return lax.dot_general(
        left, right, (((1,), (1,)), ((), ())), preferred_element_type=jnp.float32
    )


def shifted(value, axes, sizes, steps):
    total = 1
    for size in sizes:
        total *= size
    pairs = []
    for index in range(total):
        coords, rest = [], index
        for size in reversed(sizes):
            coords.append(rest % size)
            rest //= size
        coords = coords[::-1]
        target, scale = 0, 1
        for axis in reversed(range(len(sizes))):
            target += ((coords[axis] + steps[axis]) % sizes[axis]) * scale
            scale *= sizes[axis]
        pairs.append((index, target))
    return lax.ppermute(value, axes, pairs)


def swapped(value, axis, size, distance):
    return lax.ppermute(value, axis, [(i, i ^ distance) for i in range(size)])


def power_of_two(size):
    return size & (size - 1) == 0


def gather_blocks(value, axis, size):
    if power_of_two(size):
        blocks, distance = [value], 1
        while distance < size:
            arrived = swapped(jnp.stack(blocks), axis, size, distance)
            blocks = blocks + [arrived[k] for k in range(distance)]
            distance *= 2
        return blocks, lambda k: ("xor", k)
    blocks = [value] + [shifted(value, axis, (size,), (k,)) for k in range(1, size)]
    return blocks, lambda k: ("shift", k)


def scatter_sum(pieces, axis, size):
    if power_of_two(size):
        held = {k: piece.astype(jnp.float32) for k, piece in enumerate(pieces)}
        distance = size // 2
        while distance >= 1:
            leaving = sorted(k for k in held if k & distance)
            arrived = swapped(
                jnp.stack([held[k] for k in leaving]).astype(jnp.bfloat16), axis, size, distance
            )
            for position, k in enumerate(leaving):
                held[k ^ distance] = held[k ^ distance] + arrived[position].astype(jnp.float32)
            held = {k: v for k, v in held.items() if not k & distance}
            distance //= 2
        return held[0]
    total = pieces[0].astype(jnp.float32)
    for k in range(1, size):
        total = total + shifted(pieces[k], axis, (size,), (-k,)).astype(jnp.float32)
    return total


def all_sum(value, axis, size):
    if power_of_two(size):
        total, distance = value, 1
        while distance < size:
            total = total + swapped(total.astype(jnp.bfloat16), axis, size, distance).astype(jnp.float32)
            distance *= 2
        return total
    total = value
    for k in range(1, size):
        total = total + shifted(value.astype(jnp.bfloat16), axis, (size,), (k,)).astype(jnp.float32)
    return total


def exchange_blocks(blocks, axis, size):
    index = lax.axis_index(axis)
    if power_of_two(size):
        stacked = jnp.stack(blocks)
        held = {(0, k): lax.dynamic_index_in_dim(stacked, index ^ k, 0, keepdims=False) for k in range(size)}
        distance = 1
        while distance < size:
            leaving = sorted(key for key in held if key[1] & distance)
            arrived = swapped(jnp.stack([held[key] for key in leaving]), axis, size, distance)
            held = {key: v for key, v in held.items() if not key[1] & distance}
            for position, (origin, target) in enumerate(leaving):
                held[(origin ^ distance, target ^ distance)] = arrived[position]
            distance *= 2
        return [held[(k, 0)] for k in range(size)]
    stacked = jnp.stack(blocks)
    out = [lax.dynamic_index_in_dim(stacked, index, 0, keepdims=False)]
    for k in range(1, size):
        outgoing = lax.dynamic_index_in_dim(stacked, (index + k) % size, 0, keepdims=False)
        out.append(shifted(outgoing, axis, (size,), (k,)))
    return out


def rep_exchange(factors, column_blocks, axis, size):
    index = lax.axis_index(axis)
    stacked = jnp.stack(column_blocks)
    if power_of_two(size):
        columns = {0: lax.dynamic_index_in_dim(stacked, index, 0, keepdims=False)}
        for k in range(1, size):
            outgoing = lax.dynamic_index_in_dim(stacked, index ^ k, 0, keepdims=False)
            columns[k] = swapped(outgoing, axis, size, k)
        gathered = {0: factors}
        distance = size // 2
        while distance >= 1:
            origins = sorted(gathered)
            arrived = swapped(jnp.stack([gathered[o] for o in origins]), axis, size, distance)
            for position, origin in enumerate(origins):
                gathered[origin ^ distance] = arrived[position]
            distance //= 2
        return [gathered[o] for o in range(size)], [columns[o] for o in range(size)]
    every_factors = [factors]
    every_columns = [lax.dynamic_index_in_dim(stacked, index, 0, keepdims=False)]
    for k in range(1, size):
        every_factors.append(shifted(factors, axis, (size,), (k,)))
        outgoing = lax.dynamic_index_in_dim(stacked, (index + k) % size, 0, keepdims=False)
        every_columns.append(shifted(outgoing, axis, (size,), (k,)))
    return every_factors, every_columns


def weight_pass_kernel(normed_ref, masked_ref, gate_w_ref, up_w_ref, down_w_ref,
                       gate_rows_ref, up_rows_ref, hidden_ref, features_ref):
    step = pl.program_id(0)
    normed = normed_ref[...]
    gate_w = gate_w_ref[...]
    up_w = up_w_ref[...]
    gate = jnp.dot(normed, gate_w, preferred_element_type=jnp.float32)
    up = jnp.dot(normed, up_w, preferred_element_type=jnp.float32)
    hidden_grad = contract_last(masked_ref[...], down_w_ref[...])
    sigmoid_gate = 1.0 / (1.0 + jnp.exp(-gate))
    swished = gate * sigmoid_gate
    gate_rows = (hidden_grad * up * sigmoid_gate * (1.0 + gate * (1.0 - sigmoid_gate))).astype(
        jnp.bfloat16
    )
    up_rows = (hidden_grad * swished).astype(jnp.bfloat16)
    hidden_ref[...] = (swished * up).astype(jnp.bfloat16)
    gate_rows_ref[...] = gate_rows
    up_rows_ref[...] = up_rows
    partial_features = contract_last(gate_rows, gate_w) + contract_last(up_rows, up_w)

    @pl.when(step == 0)
    def _():
        features_ref[...] = partial_features

    @pl.when(step > 0)
    def _():
        features_ref[...] += partial_features


def weight_pass(window_normed, window_masked, gate_weight, up_weight, down_weight):
    rows, features = window_normed.shape
    units = gate_weight.shape[1]
    chunk = next((size for size in (512, 256, 128) if units % size == 0), units)
    factor_shape = jax.ShapeDtypeStruct((rows, units), jnp.bfloat16)
    return pl.pallas_call(
        weight_pass_kernel,
        grid=(units // chunk,),
        in_specs=[
            pl.BlockSpec((rows, features), lambda j: (0, 0)),
            pl.BlockSpec((rows, features), lambda j: (0, 0)),
            pl.BlockSpec((features, chunk), lambda j: (0, j)),
            pl.BlockSpec((features, chunk), lambda j: (0, j)),
            pl.BlockSpec((chunk, features), lambda j: (j, 0)),
        ],
        out_specs=[
            pl.BlockSpec((rows, chunk), lambda j: (0, j)),
            pl.BlockSpec((rows, chunk), lambda j: (0, j)),
            pl.BlockSpec((rows, chunk), lambda j: (0, j)),
            pl.BlockSpec((rows, features), lambda j: (0, 0)),
        ],
        out_shape=[
            factor_shape,
            factor_shape,
            factor_shape,
            jax.ShapeDtypeStruct((rows, features), jnp.float32),
        ],
        compiler_params=pltpu.CompilerParams(vmem_limit_bytes=56 * 1024 * 1024),
        cost_estimate=pl.CostEstimate(
            flops=10 * rows * features * units,
            transcendentals=rows * units,
            bytes_accessed=6 * features * units + 4 * rows * features * 2,
        ),
    )(window_normed, window_masked, gate_weight, up_weight, down_weight)


def grads_kernel(normed_ref, gate_ref, up_ref, hidden_ref, masked_ref,
                 gate_grad_ref, up_grad_ref, down_grad_ref):
    normed = normed_ref[...]
    gate_grad_ref[...] = contract_first(normed, gate_ref[...])
    up_grad_ref[...] = contract_first(normed, up_ref[...])
    down_grad_ref[...] = contract_first(hidden_ref[...], masked_ref[...])


def weight_grads(normed_cols, every_gate, every_up, every_hidden, masked_cols):
    rows, share = normed_cols.shape
    units = every_gate.shape[1]
    steps = 4 if share % 512 == 0 and units % 512 == 0 else 1
    share_block, unit_block = share // steps, units // steps
    return pl.pallas_call(
        grads_kernel,
        grid=(steps,),
        in_specs=[
            pl.BlockSpec((rows, share_block), lambda i: (0, i)),
            pl.BlockSpec((rows, units), lambda i: (0, 0)),
            pl.BlockSpec((rows, units), lambda i: (0, 0)),
            pl.BlockSpec((rows, unit_block), lambda i: (0, i)),
            pl.BlockSpec((rows, share), lambda i: (0, 0)),
        ],
        out_specs=[
            pl.BlockSpec((share_block, units), lambda i: (i, 0)),
            pl.BlockSpec((share_block, units), lambda i: (i, 0)),
            pl.BlockSpec((unit_block, share), lambda i: (i, 0)),
        ],
        out_shape=[
            jax.ShapeDtypeStruct((share, units), jnp.float32),
            jax.ShapeDtypeStruct((share, units), jnp.float32),
            jax.ShapeDtypeStruct((units, share), jnp.float32),
        ],
        compiler_params=pltpu.CompilerParams(vmem_limit_bytes=48 * 1024 * 1024),
        cost_estimate=pl.CostEstimate(
            flops=6 * rows * share * units,
            transcendentals=0,
            bytes_accessed=12 * share * units + 2 * rows * (2 * share + 3 * units),
        ),
    )(normed_cols, every_gate, every_up, every_hidden, masked_cols)


def local(tokens, cotangent, norm_gain, gate_weight, up_weight, down_weight, depths):
    parts = lax.axis_size("fsdp")
    place = lax.axis_index("fsdp")
    replicas = lax.axis_size("rep")
    replica = lax.axis_index("rep")
    shards = lax.axis_size("seq")
    features = tokens.shape[1]
    feature_share = features // replicas
    rows_here = tokens.shape[0]
    own_rows = rows_here // parts
    active = depths > REC
    ordinal = jnp.cumsum(active.astype(jnp.int32)) - 1
    selector = (ordinal[None, :] == jnp.arange(MAXACT, dtype=jnp.int32)[:, None]) & active[None, :]
    picker = selector.astype(jnp.bfloat16)
    source = jnp.dot(picker, tokens, preferred_element_type=jnp.float32)
    send_masked = jnp.dot(picker, cotangent, preferred_element_type=jnp.float32).astype(jnp.bfloat16)
    send_normed = normalize(source, norm_gain).astype(jnp.bfloat16)
    packed = jnp.concatenate([send_normed, send_masked], axis=0)
    blocks = [packed] + [shifted(packed, "seq", (shards,), (k,)) for k in range(1, shards)]
    window_normed = jnp.concatenate([b[:MAXACT] for b in blocks], axis=0)
    window_masked = jnp.concatenate([b[MAXACT:] for b in blocks], axis=0)
    window = window_normed.shape[0]
    gate_rows, up_rows, hidden, partial_features = weight_pass(
        window_normed, window_masked, gate_weight, up_weight, down_weight
    )
    columns = jnp.concatenate([window_normed, window_masked], axis=0)
    columns = columns.reshape(2 * window, replicas, feature_share)
    every_factors, every_columns = rep_exchange(
        jnp.concatenate([gate_rows, up_rows, hidden], axis=0),
        [columns[:, b] for b in range(replicas)],
        "rep",
        replicas,
    )
    partial_features = partial_features.astype(jnp.bfloat16)
    feature_grad = partial_features[:MAXACT].astype(jnp.float32)
    for k in range(1, shards):
        piece = partial_features[k * MAXACT : (k + 1) * MAXACT]
        feature_grad = feature_grad + shifted(piece, "seq", (shards,), (-k,)).astype(jnp.float32)
    every_gate = jnp.concatenate([f[:window] for f in every_factors], axis=0)
    every_up = jnp.concatenate([f[window : 2 * window] for f in every_factors], axis=0)
    every_hidden = jnp.concatenate([f[2 * window :] for f in every_factors], axis=0)
    normed_cols = jnp.concatenate([c[:window] for c in every_columns], axis=0)
    masked_cols = jnp.concatenate([c[window:] for c in every_columns], axis=0)
    gate_grad, up_grad, down_grad = weight_grads(
        normed_cols, every_gate, every_up, every_hidden, masked_cols
    )
    seq_sum = feature_grad.astype(jnp.bfloat16)
    for step in range(1, parts):
        feature_grad = feature_grad + shifted(seq_sum, "fsdp", (parts,), (step,)).astype(jnp.float32)
    _, pullback = jax.vjp(partial(normalize, norm_gain=norm_gain), source)
    slot_grad = pullback(feature_grad)[0].astype(jnp.bfloat16)
    own_columns = lax.dynamic_slice_in_dim(picker, place * own_rows, own_rows, 1)
    branch_grad = contract_first(own_columns, slot_grad).astype(jnp.bfloat16)
    return (branch_grad, gate_grad, up_grad, down_grad)


def solution(mesh):
    in_specs = (
        P(("rep", "seq"), None),
        P(("rep", "seq"), None),
        P(),
        P(None, ("seq", "fsdp")),
        P(None, ("seq", "fsdp")),
        P(("seq", "fsdp"), None),
        P(("rep", "seq")),
    )
    out_specs = (
        P(("rep", "seq", "fsdp"), None),
        P("rep", ("seq", "fsdp")),
        P("rep", ("seq", "fsdp")),
        P(("seq", "fsdp"), "rep"),
    )
    return jax.shard_map(local, mesh=mesh, in_specs=in_specs, out_specs=out_specs, check_vma=False)
```

```python
from functools import partial

import jax
import jax.numpy as jnp
from jax import lax
from jax.experimental import pallas as pl
from jax.experimental.pallas import tpu as pltpu
from jax.sharding import PartitionSpec as P

REC = 1
MAXACT = 8


EPSILON = 1e-05


def normalize(widened, norm_gain):
    factor = lax.rsqrt(jnp.mean(widened * widened, axis=-1, keepdims=True) + EPSILON)
    return widened * factor * norm_gain


def contract_first(left, right):
    return lax.dot_general(
        left, right, (((0,), (0,)), ((), ())), preferred_element_type=jnp.float32
    )


def contract_last(left, right):
    return lax.dot_general(
        left, right, (((1,), (1,)), ((), ())), preferred_element_type=jnp.float32
    )


def shifted(value, axes, sizes, steps):
    total = 1
    for size in sizes:
        total *= size
    pairs = []
    for index in range(total):
        coords, rest = [], index
        for size in reversed(sizes):
            coords.append(rest % size)
            rest //= size
        coords = coords[::-1]
        target, scale = 0, 1
        for axis in reversed(range(len(sizes))):
            target += ((coords[axis] + steps[axis]) % sizes[axis]) * scale
            scale *= sizes[axis]
        pairs.append((index, target))
    return lax.ppermute(value, axes, pairs)


def swapped(value, axis, size, distance):
    return lax.ppermute(value, axis, [(i, i ^ distance) for i in range(size)])


def power_of_two(size):
    return size & (size - 1) == 0


def gather_blocks(value, axis, size):
    if power_of_two(size):
        blocks, distance = [value], 1
        while distance < size:
            arrived = swapped(jnp.stack(blocks), axis, size, distance)
            blocks = blocks + [arrived[k] for k in range(distance)]
            distance *= 2
        return blocks, lambda k: ("xor", k)
    blocks = [value] + [shifted(value, axis, (size,), (k,)) for k in range(1, size)]
    return blocks, lambda k: ("shift", k)


def scatter_sum(pieces, axis, size):
    if power_of_two(size):
        held = {k: piece.astype(jnp.float32) for k, piece in enumerate(pieces)}
        distance = size // 2
        while distance >= 1:
            leaving = sorted(k for k in held if k & distance)
            arrived = swapped(
                jnp.stack([held[k] for k in leaving]).astype(jnp.bfloat16), axis, size, distance
            )
            for position, k in enumerate(leaving):
                held[k ^ distance] = held[k ^ distance] + arrived[position].astype(jnp.float32)
            held = {k: v for k, v in held.items() if not k & distance}
            distance //= 2
        return held[0]
    total = pieces[0].astype(jnp.float32)
    for k in range(1, size):
        total = total + shifted(pieces[k], axis, (size,), (-k,)).astype(jnp.float32)
    return total


def all_sum(value, axis, size):
    if power_of_two(size):
        total, distance = value, 1
        while distance < size:
            total = total + swapped(total.astype(jnp.bfloat16), axis, size, distance).astype(jnp.float32)
            distance *= 2
        return total
    total = value
    for k in range(1, size):
        total = total + shifted(value.astype(jnp.bfloat16), axis, (size,), (k,)).astype(jnp.float32)
    return total


def exchange_blocks(blocks, axis, size):
    index = lax.axis_index(axis)
    if power_of_two(size):
        stacked = jnp.stack(blocks)
        held = {(0, k): lax.dynamic_index_in_dim(stacked, index ^ k, 0, keepdims=False) for k in range(size)}
        distance = 1
        while distance < size:
            leaving = sorted(key for key in held if key[1] & distance)
            arrived = swapped(jnp.stack([held[key] for key in leaving]), axis, size, distance)
            held = {key: v for key, v in held.items() if not key[1] & distance}
            for position, (origin, target) in enumerate(leaving):
                held[(origin ^ distance, target ^ distance)] = arrived[position]
            distance *= 2
        return [held[(k, 0)] for k in range(size)]
    stacked = jnp.stack(blocks)
    out = [lax.dynamic_index_in_dim(stacked, index, 0, keepdims=False)]
    for k in range(1, size):
        outgoing = lax.dynamic_index_in_dim(stacked, (index + k) % size, 0, keepdims=False)
        out.append(shifted(outgoing, axis, (size,), (k,)))
    return out


def rep_exchange(factors, column_blocks, axis, size):
    index = lax.axis_index(axis)
    stacked = jnp.stack(column_blocks)
    if power_of_two(size):
        gathered = {0: factors}
        held = {(0, k): lax.dynamic_index_in_dim(stacked, index ^ k, 0, keepdims=False) for k in range(size)}
        distance = size // 2
        while distance >= 1:
            origins = sorted(gathered)
            arrived = swapped(jnp.stack([gathered[o] for o in origins]), axis, size, distance)
            for position, origin in enumerate(origins):
                gathered[origin ^ distance] = arrived[position]
            leaving = sorted(key for key in held if key[1] & distance)
            arrived = swapped(jnp.stack([held[key] for key in leaving]), axis, size, distance)
            held = {key: v for key, v in held.items() if not key[1] & distance}
            for position, (origin, target) in enumerate(leaving):
                held[(origin ^ distance, target ^ distance)] = arrived[position]
            distance //= 2
        return [gathered[o] for o in range(size)], [held[(o, 0)] for o in range(size)]
    every_factors = [factors]
    every_columns = [lax.dynamic_index_in_dim(stacked, index, 0, keepdims=False)]
    for k in range(1, size):
        every_factors.append(shifted(factors, axis, (size,), (k,)))
        outgoing = lax.dynamic_index_in_dim(stacked, (index + k) % size, 0, keepdims=False)
        every_columns.append(shifted(outgoing, axis, (size,), (k,)))
    return every_factors, every_columns


def weight_pass_kernel(normed_ref, masked_ref, gate_w_ref, up_w_ref, down_w_ref,
                       gate_rows_ref, up_rows_ref, hidden_ref, features_ref):
    step = pl.program_id(0)
    normed = normed_ref[...]
    gate_w = gate_w_ref[...]
    up_w = up_w_ref[...]
    gate = jnp.dot(normed, gate_w, preferred_element_type=jnp.float32)
    up = jnp.dot(normed, up_w, preferred_element_type=jnp.float32)
    hidden_grad = contract_last(masked_ref[...], down_w_ref[...])
    sigmoid_gate = 1.0 / (1.0 + jnp.exp(-gate))
    swished = gate * sigmoid_gate
    gate_rows = (hidden_grad * up * sigmoid_gate * (1.0 + gate * (1.0 - sigmoid_gate))).astype(
        jnp.bfloat16
    )
    up_rows = (hidden_grad * swished).astype(jnp.bfloat16)
    hidden_ref[...] = (swished * up).astype(jnp.bfloat16)
    gate_rows_ref[...] = gate_rows
    up_rows_ref[...] = up_rows
    partial_features = contract_last(gate_rows, gate_w) + contract_last(up_rows, up_w)

    @pl.when(step == 0)
    def _():
        features_ref[...] = partial_features

    @pl.when(step > 0)
    def _():
        features_ref[...] += partial_features


def weight_pass(window_normed, window_masked, gate_weight, up_weight, down_weight):
    rows, features = window_normed.shape
    units = gate_weight.shape[1]
    chunk = next((size for size in (384, 512, 256, 128) if units % size == 0), units)
    factor_shape = jax.ShapeDtypeStruct((rows, units), jnp.bfloat16)
    return pl.pallas_call(
        weight_pass_kernel,
        grid=(units // chunk,),
        in_specs=[
            pl.BlockSpec((rows, features), lambda j: (0, 0)),
            pl.BlockSpec((rows, features), lambda j: (0, 0)),
            pl.BlockSpec((features, chunk), lambda j: (0, j)),
            pl.BlockSpec((features, chunk), lambda j: (0, j)),
            pl.BlockSpec((chunk, features), lambda j: (j, 0)),
        ],
        out_specs=[
            pl.BlockSpec((rows, chunk), lambda j: (0, j)),
            pl.BlockSpec((rows, chunk), lambda j: (0, j)),
            pl.BlockSpec((rows, chunk), lambda j: (0, j)),
            pl.BlockSpec((rows, features), lambda j: (0, 0)),
        ],
        out_shape=[
            factor_shape,
            factor_shape,
            factor_shape,
            jax.ShapeDtypeStruct((rows, features), jnp.float32),
        ],
        compiler_params=pltpu.CompilerParams(vmem_limit_bytes=56 * 1024 * 1024),
        cost_estimate=pl.CostEstimate(
            flops=10 * rows * features * units,
            transcendentals=rows * units,
            bytes_accessed=6 * features * units + 4 * rows * features * 2,
        ),
    )(window_normed, window_masked, gate_weight, up_weight, down_weight)


def grads_kernel(normed_ref, gate_ref, up_ref, hidden_ref, masked_ref,
                 gate_grad_ref, up_grad_ref, down_grad_ref):
    normed = normed_ref[...]
    gate_grad_ref[...] = contract_first(normed, gate_ref[...])
    up_grad_ref[...] = contract_first(normed, up_ref[...])
    down_grad_ref[...] = contract_first(hidden_ref[...], masked_ref[...])


def weight_grads(normed_cols, every_gate, every_up, every_hidden, masked_cols):
    rows, share = normed_cols.shape
    units = every_gate.shape[1]
    steps = 4 if share % 512 == 0 and units % 512 == 0 else 1
    share_block, unit_block = share // steps, units // steps
    return pl.pallas_call(
        grads_kernel,
        grid=(steps,),
        in_specs=[
            pl.BlockSpec((rows, share_block), lambda i: (0, i)),
            pl.BlockSpec((rows, units), lambda i: (0, 0)),
            pl.BlockSpec((rows, units), lambda i: (0, 0)),
            pl.BlockSpec((rows, unit_block), lambda i: (0, i)),
            pl.BlockSpec((rows, share), lambda i: (0, 0)),
        ],
        out_specs=[
            pl.BlockSpec((share_block, units), lambda i: (i, 0)),
            pl.BlockSpec((share_block, units), lambda i: (i, 0)),
            pl.BlockSpec((unit_block, share), lambda i: (i, 0)),
        ],
        out_shape=[
            jax.ShapeDtypeStruct((share, units), jnp.float32),
            jax.ShapeDtypeStruct((share, units), jnp.float32),
            jax.ShapeDtypeStruct((units, share), jnp.float32),
        ],
        compiler_params=pltpu.CompilerParams(vmem_limit_bytes=48 * 1024 * 1024),
        cost_estimate=pl.CostEstimate(
            flops=6 * rows * share * units,
            transcendentals=0,
            bytes_accessed=12 * share * units + 2 * rows * (2 * share + 3 * units),
        ),
    )(normed_cols, every_gate, every_up, every_hidden, masked_cols)


def local(tokens, cotangent, norm_gain, gate_weight, up_weight, down_weight, depths):
    parts = lax.axis_size("fsdp")
    place = lax.axis_index("fsdp")
    replicas = lax.axis_size("rep")
    replica = lax.axis_index("rep")
    shards = lax.axis_size("seq")
    features = tokens.shape[1]
    feature_share = features // replicas
    rows_here = tokens.shape[0]
    own_rows = rows_here // parts
    active = depths > REC
    ordinal = jnp.cumsum(active.astype(jnp.int32)) - 1
    selector = (ordinal[None, :] == jnp.arange(MAXACT, dtype=jnp.int32)[:, None]) & active[None, :]
    picker = selector.astype(jnp.bfloat16)
    source = jnp.dot(picker, tokens, preferred_element_type=jnp.float32)
    send_masked = jnp.dot(picker, cotangent, preferred_element_type=jnp.float32).astype(jnp.bfloat16)
    send_normed = normalize(source, norm_gain).astype(jnp.bfloat16)
    packed = jnp.concatenate([send_normed, send_masked], axis=0)
    blocks = [packed] + [shifted(packed, "seq", (shards,), (k,)) for k in range(1, shards)]
    window_normed = jnp.concatenate([b[:MAXACT] for b in blocks], axis=0)
    window_masked = jnp.concatenate([b[MAXACT:] for b in blocks], axis=0)
    window = window_normed.shape[0]
    gate_rows, up_rows, hidden, partial_features = weight_pass(
        window_normed, window_masked, gate_weight, up_weight, down_weight
    )
    columns = jnp.concatenate([window_normed, window_masked], axis=0)
    columns = columns.reshape(2 * window, replicas, feature_share)
    every_factors, every_columns = rep_exchange(
        jnp.concatenate([gate_rows, up_rows, hidden], axis=0),
        [columns[:, b] for b in range(replicas)],
        "rep",
        replicas,
    )
    partial_features = partial_features.astype(jnp.bfloat16)
    feature_grad = partial_features[:MAXACT].astype(jnp.float32)
    for k in range(1, shards):
        piece = partial_features[k * MAXACT : (k + 1) * MAXACT]
        feature_grad = feature_grad + shifted(piece, "seq", (shards,), (-k,)).astype(jnp.float32)
    every_gate = jnp.concatenate([f[:window] for f in every_factors], axis=0)
    every_up = jnp.concatenate([f[window : 2 * window] for f in every_factors], axis=0)
    every_hidden = jnp.concatenate([f[2 * window :] for f in every_factors], axis=0)
    normed_cols = jnp.concatenate([c[:window] for c in every_columns], axis=0)
    masked_cols = jnp.concatenate([c[window:] for c in every_columns], axis=0)
    gate_grad, up_grad, down_grad = weight_grads(
        normed_cols, every_gate, every_up, every_hidden, masked_cols
    )
    seq_sum = feature_grad.astype(jnp.bfloat16)
    for step in range(1, parts):
        feature_grad = feature_grad + shifted(seq_sum, "fsdp", (parts,), (step,)).astype(jnp.float32)
    _, pullback = jax.vjp(partial(normalize, norm_gain=norm_gain), source)
    slot_grad = pullback(feature_grad)[0].astype(jnp.bfloat16)
    own_columns = lax.dynamic_slice_in_dim(picker, place * own_rows, own_rows, 1)
    branch_grad = contract_first(own_columns, slot_grad).astype(jnp.bfloat16)
    return (branch_grad, gate_grad, up_grad, down_grad)


def solution(mesh):
    in_specs = (
        P(("rep", "seq"), None),
        P(("rep", "seq"), None),
        P(),
        P(None, ("seq", "fsdp")),
        P(None, ("seq", "fsdp")),
        P(("seq", "fsdp"), None),
        P(("rep", "seq")),
    )
    out_specs = (
        P(("rep", "seq", "fsdp"), None),
        P("rep", ("seq", "fsdp")),
        P("rep", ("seq", "fsdp")),
        P(("seq", "fsdp"), "rep"),
    )
    return jax.shard_map(local, mesh=mesh, in_specs=in_specs, out_specs=out_specs, check_vma=False)
```

```python
from functools import partial

import jax
import jax.numpy as jnp
from jax import lax
from jax.experimental import pallas as pl
from jax.experimental.pallas import tpu as pltpu
from jax.sharding import PartitionSpec as P

REC = 1
MAXACT = 8


EPSILON = 1e-05


def normalize(widened, norm_gain):
    factor = lax.rsqrt(jnp.mean(widened * widened, axis=-1, keepdims=True) + EPSILON)
    return widened * factor * norm_gain


def contract_first(left, right):
    return lax.dot_general(
        left, right, (((0,), (0,)), ((), ())), preferred_element_type=jnp.float32
    )


def contract_last(left, right):
    return lax.dot_general(
        left, right, (((1,), (1,)), ((), ())), preferred_element_type=jnp.float32
    )


def shifted(value, axes, sizes, steps):
    total = 1
    for size in sizes:
        total *= size
    pairs = []
    for index in range(total):
        coords, rest = [], index
        for size in reversed(sizes):
            coords.append(rest % size)
            rest //= size
        coords = coords[::-1]
        target, scale = 0, 1
        for axis in reversed(range(len(sizes))):
            target += ((coords[axis] + steps[axis]) % sizes[axis]) * scale
            scale *= sizes[axis]
        pairs.append((index, target))
    return lax.ppermute(value, axes, pairs)


def swapped(value, axis, size, distance):
    return lax.ppermute(value, axis, [(i, i ^ distance) for i in range(size)])


def power_of_two(size):
    return size & (size - 1) == 0


def gather_blocks(value, axis, size):
    if power_of_two(size):
        blocks, distance = [value], 1
        while distance < size:
            arrived = swapped(jnp.stack(blocks), axis, size, distance)
            blocks = blocks + [arrived[k] for k in range(distance)]
            distance *= 2
        return blocks, lambda k: ("xor", k)
    blocks = [value] + [shifted(value, axis, (size,), (k,)) for k in range(1, size)]
    return blocks, lambda k: ("shift", k)


def scatter_sum(pieces, axis, size):
    if power_of_two(size):
        held = {k: piece.astype(jnp.float32) for k, piece in enumerate(pieces)}
        distance = size // 2
        while distance >= 1:
            leaving = sorted(k for k in held if k & distance)
            arrived = swapped(
                jnp.stack([held[k] for k in leaving]).astype(jnp.bfloat16), axis, size, distance
            )
            for position, k in enumerate(leaving):
                held[k ^ distance] = held[k ^ distance] + arrived[position].astype(jnp.float32)
            held = {k: v for k, v in held.items() if not k & distance}
            distance //= 2
        return held[0]
    total = pieces[0].astype(jnp.float32)
    for k in range(1, size):
        total = total + shifted(pieces[k], axis, (size,), (-k,)).astype(jnp.float32)
    return total


def all_sum(value, axis, size):
    if power_of_two(size):
        total, distance = value, 1
        while distance < size:
            total = total + swapped(total.astype(jnp.bfloat16), axis, size, distance).astype(jnp.float32)
            distance *= 2
        return total
    total = value
    for k in range(1, size):
        total = total + shifted(value.astype(jnp.bfloat16), axis, (size,), (k,)).astype(jnp.float32)
    return total


def exchange_blocks(blocks, axis, size):
    index = lax.axis_index(axis)
    if power_of_two(size):
        stacked = jnp.stack(blocks)
        held = {(0, k): lax.dynamic_index_in_dim(stacked, index ^ k, 0, keepdims=False) for k in range(size)}
        distance = 1
        while distance < size:
            leaving = sorted(key for key in held if key[1] & distance)
            arrived = swapped(jnp.stack([held[key] for key in leaving]), axis, size, distance)
            held = {key: v for key, v in held.items() if not key[1] & distance}
            for position, (origin, target) in enumerate(leaving):
                held[(origin ^ distance, target ^ distance)] = arrived[position]
            distance *= 2
        return [held[(k, 0)] for k in range(size)]
    stacked = jnp.stack(blocks)
    out = [lax.dynamic_index_in_dim(stacked, index, 0, keepdims=False)]
    for k in range(1, size):
        outgoing = lax.dynamic_index_in_dim(stacked, (index + k) % size, 0, keepdims=False)
        out.append(shifted(outgoing, axis, (size,), (k,)))
    return out


def rep_exchange(factors, column_blocks, axis, size):
    index = lax.axis_index(axis)
    stacked = jnp.stack(column_blocks)
    if power_of_two(size):
        gathered = {0: factors}
        held = {(0, k): lax.dynamic_index_in_dim(stacked, index ^ k, 0, keepdims=False) for k in range(size)}
        distance = size // 2
        while distance >= 1:
            origins = sorted(gathered)
            arrived = swapped(jnp.stack([gathered[o] for o in origins]), axis, size, distance)
            for position, origin in enumerate(origins):
                gathered[origin ^ distance] = arrived[position]
            leaving = sorted(key for key in held if key[1] & distance)
            arrived = swapped(jnp.stack([held[key] for key in leaving]), axis, size, distance)
            held = {key: v for key, v in held.items() if not key[1] & distance}
            for position, (origin, target) in enumerate(leaving):
                held[(origin ^ distance, target ^ distance)] = arrived[position]
            distance //= 2
        return [gathered[o] for o in range(size)], [held[(o, 0)] for o in range(size)]
    every_factors = [factors]
    every_columns = [lax.dynamic_index_in_dim(stacked, index, 0, keepdims=False)]
    for k in range(1, size):
        every_factors.append(shifted(factors, axis, (size,), (k,)))
        outgoing = lax.dynamic_index_in_dim(stacked, (index + k) % size, 0, keepdims=False)
        every_columns.append(shifted(outgoing, axis, (size,), (k,)))
    return every_factors, every_columns


def weight_pass_kernel(normed_ref, masked_ref, gate_w_ref, up_w_ref, down_w_ref,
                       gate_rows_ref, up_rows_ref, hidden_ref, features_ref):
    step = pl.program_id(0)
    normed = normed_ref[...]
    gate_w = gate_w_ref[...]
    up_w = up_w_ref[...]
    gate = jnp.dot(normed, gate_w, preferred_element_type=jnp.float32)
    up = jnp.dot(normed, up_w, preferred_element_type=jnp.float32)
    hidden_grad = contract_last(masked_ref[...], down_w_ref[...])
    sigmoid_gate = 1.0 / (1.0 + jnp.exp(-gate))
    swished = gate * sigmoid_gate
    gate_rows = (hidden_grad * up * sigmoid_gate * (1.0 + gate * (1.0 - sigmoid_gate))).astype(
        jnp.bfloat16
    )
    up_rows = (hidden_grad * swished).astype(jnp.bfloat16)
    hidden_ref[...] = (swished * up).astype(jnp.bfloat16)
    gate_rows_ref[...] = gate_rows
    up_rows_ref[...] = up_rows
    partial_features = contract_last(gate_rows, gate_w) + contract_last(up_rows, up_w)

    @pl.when(step == 0)
    def _():
        features_ref[...] = partial_features

    @pl.when(step > 0)
    def _():
        features_ref[...] += partial_features


def weight_pass(window_normed, window_masked, gate_weight, up_weight, down_weight):
    rows, features = window_normed.shape
    units = gate_weight.shape[1]
    chunk = next((size for size in (384, 512, 256, 128) if units % size == 0), units)
    factor_shape = jax.ShapeDtypeStruct((rows, units), jnp.bfloat16)
    return pl.pallas_call(
        weight_pass_kernel,
        grid=(units // chunk,),
        in_specs=[
            pl.BlockSpec((rows, features), lambda j: (0, 0)),
            pl.BlockSpec((rows, features), lambda j: (0, 0)),
            pl.BlockSpec((features, chunk), lambda j: (0, j)),
            pl.BlockSpec((features, chunk), lambda j: (0, j)),
            pl.BlockSpec((chunk, features), lambda j: (j, 0)),
        ],
        out_specs=[
            pl.BlockSpec((rows, chunk), lambda j: (0, j)),
            pl.BlockSpec((rows, chunk), lambda j: (0, j)),
            pl.BlockSpec((rows, chunk), lambda j: (0, j)),
            pl.BlockSpec((rows, features), lambda j: (0, 0)),
        ],
        out_shape=[
            factor_shape,
            factor_shape,
            factor_shape,
            jax.ShapeDtypeStruct((rows, features), jnp.float32),
        ],
        compiler_params=pltpu.CompilerParams(vmem_limit_bytes=56 * 1024 * 1024),
        cost_estimate=pl.CostEstimate(
            flops=10 * rows * features * units,
            transcendentals=rows * units,
            bytes_accessed=6 * features * units + 4 * rows * features * 2,
        ),
    )(window_normed, window_masked, gate_weight, up_weight, down_weight)


def grads_kernel(normed_ref, gate_ref, up_ref, hidden_ref, masked_ref,
                 gate_grad_ref, up_grad_ref, down_grad_ref):
    normed = normed_ref[...]
    gate_grad_ref[...] = contract_first(normed, gate_ref[...])
    up_grad_ref[...] = contract_first(normed, up_ref[...])
    down_grad_ref[...] = contract_first(hidden_ref[...], masked_ref[...])


def weight_grads(normed_cols, every_gate, every_up, every_hidden, masked_cols):
    rows, share = normed_cols.shape
    units = every_gate.shape[1]
    steps = 2 if share % 256 == 0 and units % 256 == 0 else 1
    share_block, unit_block = share // steps, units // steps
    return pl.pallas_call(
        grads_kernel,
        grid=(steps,),
        in_specs=[
            pl.BlockSpec((rows, share_block), lambda i: (0, i)),
            pl.BlockSpec((rows, units), lambda i: (0, 0)),
            pl.BlockSpec((rows, units), lambda i: (0, 0)),
            pl.BlockSpec((rows, unit_block), lambda i: (0, i)),
            pl.BlockSpec((rows, share), lambda i: (0, 0)),
        ],
        out_specs=[
            pl.BlockSpec((share_block, units), lambda i: (i, 0)),
            pl.BlockSpec((share_block, units), lambda i: (i, 0)),
            pl.BlockSpec((unit_block, share), lambda i: (i, 0)),
        ],
        out_shape=[
            jax.ShapeDtypeStruct((share, units), jnp.float32),
            jax.ShapeDtypeStruct((share, units), jnp.float32),
            jax.ShapeDtypeStruct((units, share), jnp.float32),
        ],
        compiler_params=pltpu.CompilerParams(vmem_limit_bytes=48 * 1024 * 1024),
        cost_estimate=pl.CostEstimate(
            flops=6 * rows * share * units,
            transcendentals=0,
            bytes_accessed=12 * share * units + 2 * rows * (2 * share + 3 * units),
        ),
    )(normed_cols, every_gate, every_up, every_hidden, masked_cols)


def local(tokens, cotangent, norm_gain, gate_weight, up_weight, down_weight, depths):
    parts = lax.axis_size("fsdp")
    place = lax.axis_index("fsdp")
    replicas = lax.axis_size("rep")
    replica = lax.axis_index("rep")
    shards = lax.axis_size("seq")
    features = tokens.shape[1]
    feature_share = features // replicas
    rows_here = tokens.shape[0]
    own_rows = rows_here // parts
    active = depths > REC
    ordinal = jnp.cumsum(active.astype(jnp.int32)) - 1
    selector = (ordinal[None, :] == jnp.arange(MAXACT, dtype=jnp.int32)[:, None]) & active[None, :]
    picker = selector.astype(jnp.bfloat16)
    source = jnp.dot(picker, tokens, preferred_element_type=jnp.float32)
    send_masked = jnp.dot(picker, cotangent, preferred_element_type=jnp.float32).astype(jnp.bfloat16)
    send_normed = normalize(source, norm_gain).astype(jnp.bfloat16)
    packed = jnp.concatenate([send_normed, send_masked], axis=0)
    blocks = [packed] + [shifted(packed, "seq", (shards,), (k,)) for k in range(1, shards)]
    window_normed = jnp.concatenate([b[:MAXACT] for b in blocks], axis=0)
    window_masked = jnp.concatenate([b[MAXACT:] for b in blocks], axis=0)
    window = window_normed.shape[0]
    gate_rows, up_rows, hidden, partial_features = weight_pass(
        window_normed, window_masked, gate_weight, up_weight, down_weight
    )
    columns = jnp.concatenate([window_normed, window_masked], axis=0)
    columns = columns.reshape(2 * window, replicas, feature_share)
    every_factors, every_columns = rep_exchange(
        jnp.concatenate([gate_rows, up_rows, hidden], axis=0),
        [columns[:, b] for b in range(replicas)],
        "rep",
        replicas,
    )
    partial_features = partial_features.astype(jnp.bfloat16)
    feature_grad = partial_features[:MAXACT].astype(jnp.float32)
    for k in range(1, shards):
        piece = partial_features[k * MAXACT : (k + 1) * MAXACT]
        feature_grad = feature_grad + shifted(piece, "seq", (shards,), (-k,)).astype(jnp.float32)
    every_gate = jnp.concatenate([f[:window] for f in every_factors], axis=0)
    every_up = jnp.concatenate([f[window : 2 * window] for f in every_factors], axis=0)
    every_hidden = jnp.concatenate([f[2 * window :] for f in every_factors], axis=0)
    normed_cols = jnp.concatenate([c[:window] for c in every_columns], axis=0)
    masked_cols = jnp.concatenate([c[window:] for c in every_columns], axis=0)
    gate_grad, up_grad, down_grad = weight_grads(
        normed_cols, every_gate, every_up, every_hidden, masked_cols
    )
    seq_sum = feature_grad.astype(jnp.bfloat16)
    for step in range(1, parts):
        feature_grad = feature_grad + shifted(seq_sum, "fsdp", (parts,), (step,)).astype(jnp.float32)
    _, pullback = jax.vjp(partial(normalize, norm_gain=norm_gain), source)
    slot_grad = pullback(feature_grad)[0].astype(jnp.bfloat16)
    own_columns = lax.dynamic_slice_in_dim(picker, place * own_rows, own_rows, 1)
    branch_grad = contract_first(own_columns, slot_grad).astype(jnp.bfloat16)
    return (branch_grad, gate_grad, up_grad, down_grad)


def solution(mesh):
    in_specs = (
        P(("rep", "seq"), None),
        P(("rep", "seq"), None),
        P(),
        P(None, ("seq", "fsdp")),
        P(None, ("seq", "fsdp")),
        P(("seq", "fsdp"), None),
        P(("rep", "seq")),
    )
    out_specs = (
        P(("rep", "seq", "fsdp"), None),
        P("rep", ("seq", "fsdp")),
        P("rep", ("seq", "fsdp")),
        P(("seq", "fsdp"), "rep"),
    )
    return jax.shard_map(local, mesh=mesh, in_specs=in_specs, out_specs=out_specs, check_vma=False)
```
